128 devices in a mesh: wide: 32 (over y, x, z_lo), narrow: 4 (over z_hi, core).
Axes of the slice: x: 4, y: 4, z: 4 (z_hi: 2, z_lo: 2; z = z_hi * 2 + z_lo), core: 2. Of those that a mesh axis runs over, the one named last changes fastest.
Arguments:
- hidden: bfloat16 [4096, 2048], P('wide'), may hold values from -6 to 6
- attn_gain: bfloat16 [2048], replicated, may hold values from 0.099609375 to 1.8984375
- q_weight: bfloat16 [2048, 3072], P('wide', 'narrow'), may hold values from -0.125 to 0.125
- kva_weight: bfloat16 [2048, 576], P('wide'), may hold values from -0.125 to 0.125
- kv_gain: bfloat16 [512], replicated, may hold values from 0.099609375 to 1.8984375
- kvb_weight: bfloat16 [512, 4096], P('wide', 'narrow'), may hold values from -0.25 to 0.25
- o_weight: bfloat16 [2048, 2048], P('narrow', 'wide'), may hold values from -12 to 12
- cache: bfloat16 [8, 20480, 576], P(None, 'wide'), as said below
- lengths: int32 [8], replicated, may hold values from 2 to 20480, as said below
Outputs:
- attn_out: bfloat16 [4096, 2048], P('wide')
The draws below stay inside these ranges and needn't reach their ends.
Inputs may be any that keep to these rules, and one draw needn't show every extreme that they name: `lengths`: each request has at most 20480 cached positions; one request of every draw has exactly 20480. `cache`: each cached row holds a stored latent (first 512 entries) and a rotated key (last 64); rows at or past a request's length are never read.
All inputs are finite; a program needn't handle non-finite values.
Results may differ from the reference program's by a relative error of at most 0.02.
Values may be sent and summed in bfloat16 or wider, within the bound.
No kernel may reach another device: no remote copies, remote signals or barrier semaphores. Data moves between devices by JAX's collectives and lax.ppermute only.
A program may use at most 128 MiB of HBM per device.

```python
import jax
import jax.numpy as jnp
from jax import lax

D = 2048
H = 16
NOPE = 128
ROPE = 64
VDIM = 128
LAT = 512
SPAN = 512
TOKENS = 4096
REQ = 8
CACHE = 20480


def draw_lengths(key, part):
    drawn = jax.random.randint(jax.random.fold_in(key, 11), (REQ,), 2, CACHE + 1)
    longest = jax.random.randint(jax.random.fold_in(key, 12), (), 0, REQ)
    return jnp.where(jnp.arange(REQ) == longest, CACHE, drawn).astype(jnp.int32)


def draw_cache(key, part):
    base = jax.random.normal(jax.random.fold_in(key, 21), (REQ, CACHE, LAT + ROPE), jnp.float32)
    return base.astype(jnp.bfloat16)


def level_of(own_key, dims, cuts, low, top_value):
    level, own = 1.0, jax.random.fold_in(own_key, 6)
    for axis_at, blocks in cuts:
        heights = jnp.exp(jax.random.uniform(jax.random.fold_in(own, axis_at), (blocks,), jnp.float32, low / len(cuts), top_value / len(cuts)))
        level = level * jnp.repeat(heights, dims[axis_at] // blocks).reshape([-1 if axis == axis_at else 1 for axis in range(len(dims))])
    return level


def gaussian(own_key, extent, spread, bound, cuts=(), held_as=jnp.bfloat16):
    array = spread * jax.random.normal(own_key, extent, jnp.float32)
    if cuts:
        array = array * level_of(own_key, extent, cuts, -0.22, 0.18)
    return jnp.clip(array, -bound, bound).astype(held_as)


def setup_inputs(seed: int = 0) -> dict:
    seeds = jax.random.split(jax.random.key(seed), 10)
    hidden = gaussian(seeds[0], (TOKENS, D), 1.0, 6.0, ((0, 32),))
    attn_gain = jnp.clip(1.0 + 0.18 * jax.random.normal(seeds[1], (D,), jnp.float32), 0.099609375, 1.8984375).astype(jnp.bfloat16)
    q_weight = gaussian(seeds[2], (D, H * (NOPE + ROPE)), D ** -0.5, 0.125, ((0, 32), (1, 4)))
    kva_weight = gaussian(seeds[3], (D, LAT + ROPE), D ** -0.5, 0.125, ((0, 32),))
    kv_gain = jnp.clip(1.0 + 0.18 * jax.random.normal(seeds[4], (LAT,), jnp.float32), 0.099609375, 1.8984375).astype(jnp.bfloat16)
    kvb_weight = gaussian(seeds[5], (LAT, H * (NOPE + VDIM)), LAT ** -0.5, 0.25, ((0, 32), (1, 4)))
    o_weight = gaussian(seeds[6], (H * VDIM, D), 2.0, 12.0, ((0, 4), (1, 32)))
    cache = draw_cache(jax.random.fold_in(seeds[9], 71), 0)
    lengths = draw_lengths(jax.random.fold_in(seeds[9], 71), 0)
    return {"hidden": hidden, "attn_gain": attn_gain, "q_weight": q_weight, "kva_weight": kva_weight, "kv_gain": kv_gain, "kvb_weight": kvb_weight, "o_weight": o_weight, "cache": cache, "lengths": lengths}


eps = 1e-06
score_scale = 1.0 / 13.856406460551018

def rotate(values, positions):
    half_size = values.shape[-1] // 2
    frequency = 10000.0 ** (-jnp.arange(half_size, dtype=jnp.float32) / half_size)
    angles = positions.astype(jnp.float32)[..., None] * frequency
    lower_half = values[..., :half_size]
    upper_half = values[..., half_size:]
    cosine = jnp.cos(angles)
    sine_part = jnp.sin(angles)
    return jnp.concatenate([lower_half * cosine - upper_half * sine_part, lower_half * sine_part + upper_half * cosine], axis=-1)

def scaled_norm(values, gain):
    return values * lax.rsqrt(lax.optimization_barrier(jnp.mean(values * values, axis=-1, keepdims=True)) + eps) * gain.astype(jnp.float32)

def reference(hidden, attn_gain, q_weight, kva_weight, kv_gain, kvb_weight, o_weight, cache, lengths):
    normed = scaled_norm(hidden.astype(jnp.float32), attn_gain).astype(jnp.bfloat16)
    query_rows = jnp.dot(normed, q_weight, preferred_element_type=jnp.float32).astype(jnp.bfloat16)
    query_rows = query_rows.reshape(TOKENS, H, NOPE + ROPE)
    compressed = jnp.dot(normed, kva_weight, preferred_element_type=jnp.float32)
    token_ids = jnp.arange(TOKENS, dtype=jnp.int32)
    request_of = (token_ids // SPAN).astype(jnp.int32)
    positions = lengths[request_of] + token_ids % SPAN
    new_keys = jnp.concatenate([scaled_norm(compressed[:, :LAT], kv_gain).astype(jnp.bfloat16), rotate(compressed[:, LAT:], positions).astype(jnp.bfloat16)], axis=1)
    kvb_heads = kvb_weight.reshape(LAT, H, NOPE + VDIM)
    q_latent = jnp.einsum('thc,lhc->thl', query_rows[..., :NOPE].astype(jnp.float32), kvb_heads[..., :NOPE].astype(jnp.float32)).astype(jnp.bfloat16)
    q_rope = rotate(query_rows[..., NOPE:].astype(jnp.float32), positions[:, None]).astype(jnp.bfloat16)
    per_head = jnp.transpose(jnp.concatenate([q_latent, q_rope], axis=-1), (1, 0, 2))
    value_maps = jnp.transpose(kvb_heads[..., NOPE:].astype(jnp.float32), (1, 0, 2))
    slot_ids = jnp.arange(SPAN, dtype=jnp.int32)
    causal = slot_ids[None, :] <= slot_ids[:, None]
    contexts = []
    for request in range(REQ):
        key_rows = jnp.concatenate([cache[request], new_keys[request * SPAN:(request + 1) * SPAN]], axis=0)
        key_cols = jnp.transpose(key_rows)
        cache_live = jnp.arange(CACHE, dtype=jnp.int32) < lengths[request]
        live_mask = jnp.concatenate([jnp.broadcast_to(cache_live[None, :], (SPAN, CACHE)), causal], axis=1)

        def one_head(pair):
            head_query, value_map = pair
            scores = jnp.dot(head_query, key_cols, preferred_element_type=jnp.float32) * score_scale
            row_peak = lax.optimization_barrier(jnp.max(jnp.where(live_mask, scores, -1e+30), axis=-1))
            weights = jnp.where(live_mask, jnp.exp(scores - row_peak[:, None]), 0.0)
            row_total = lax.optimization_barrier(jnp.sum(weights, axis=-1))
            mixed = jnp.dot(weights.astype(jnp.bfloat16), key_rows[:, :LAT], preferred_element_type=jnp.float32)
            return jnp.dot(mixed, value_map, precision=lax.Precision.HIGHEST) / row_total[:, None]
        contexts.append(lax.map(one_head, (per_head[:, request * SPAN:(request + 1) * SPAN], value_maps)))
    context = jnp.concatenate(contexts, axis=1)
    context = jnp.transpose(context, (1, 0, 2)).reshape(TOKENS, H * VDIM).astype(jnp.bfloat16)
    return jnp.dot(context, o_weight, preferred_element_type=jnp.float32).astype(jnp.bfloat16)
```

```python
import jax
import jax.numpy as jnp
from jax import lax
from jax.sharding import PartitionSpec as P

NOPE = 128
ROPE = 64
VDIM = 128
LAT = 512
SPAN = 512


eps = 1e-06
score_scale = 1.0 / 13.856406460551018


def rotate(values, positions):
    half_size = values.shape[-1] // 2
    frequency = 10000.0 ** (-jnp.arange(half_size, dtype=jnp.float32) / half_size)
    angles = positions.astype(jnp.float32)[..., None] * frequency
    lower_half = values[..., :half_size]
    upper_half = values[..., half_size:]
    cosine = jnp.cos(angles)
    sine_part = jnp.sin(angles)
    return jnp.concatenate(
        [
            lower_half * cosine - upper_half * sine_part,
            lower_half * sine_part + upper_half * cosine,
        ],
        axis=-1,
    )


def scaled_norm(values, gain):
    return (
        values
        * lax.rsqrt(jnp.mean(values * values, axis=-1, keepdims=True) + eps)
        * gain.astype(jnp.float32)
    )


def gather_axis(x, axis_name):
    count = lax.axis_size(axis_name)
    spread = jnp.broadcast_to(x[None], (count,) + x.shape)
    return lax.all_to_all(spread, axis_name, split_axis=0, concat_axis=0, tiled=True)


def absorb(nope_part, key_maps):
    return jnp.einsum(
        "thc,lhc->thl", nope_part, key_maps, preferred_element_type=jnp.float32
    ).astype(jnp.bfloat16)


def project_values(mixed, value_maps):
    upper_part = mixed.astype(jnp.bfloat16)
    lower_part = (mixed - upper_part.astype(jnp.float32)).astype(jnp.bfloat16)
    first_term = jnp.einsum(
        "qhc,chv->qhv", upper_part, value_maps, preferred_element_type=jnp.float32
    )
    second_term = jnp.einsum(
        "qhc,chv->qhv", lower_part, value_maps, preferred_element_type=jnp.float32
    )
    return first_term + second_term


def attend(block_queries, key_rows, live_mask, value_maps):
    scores = (
        jnp.einsum("qhc,kc->qhk", block_queries, key_rows, preferred_element_type=jnp.float32)
        * score_scale
    )
    live_rows = live_mask[:, None, :]
    row_peak = jnp.max(jnp.where(live_rows, scores, -1e30), axis=-1)
    row_peak = row_peak.astype(jnp.bfloat16).astype(jnp.float32)
    weights = jnp.where(live_rows, jnp.exp(scores - row_peak[..., None]), 0.0)
    row_total = jnp.sum(weights, axis=-1)
    mixed = jnp.einsum(
        "qhk,kc->qhc",
        weights.astype(jnp.bfloat16),
        key_rows[:, :LAT],
        preferred_element_type=jnp.float32,
    )
    return (row_peak, row_total, project_values(mixed, value_maps))


def skipped(block_queries, key_rows, live_mask, value_maps):
    rows_here = block_queries.shape[0]
    heads_here = block_queries.shape[1]
    return (
        jnp.full((rows_here, heads_here), -1e30, jnp.float32),
        jnp.zeros((rows_here, heads_here), jnp.float32),
        jnp.zeros((rows_here, heads_here, value_maps.shape[2]), jnp.float32),
    )


def merge_parts(first, second):
    joint_peak = jnp.maximum(first[0], second[0])
    first_factor = jnp.exp(first[0] - joint_peak)
    second_factor = jnp.exp(second[0] - joint_peak)
    joint_total = first_factor * first[1] + second_factor * second[1]
    joint_value = first_factor[..., None] * first[2] + second_factor[..., None] * second[2]
    return (joint_peak, joint_total, joint_value)


def per_device(
    hidden, attn_gain, q_weight, kva_weight, kv_gain, kvb_weight, o_weight, cache, lengths
):
    wide_count = lax.axis_size("wide")
    wide_place = lax.axis_index("wide")
    tok_rows = hidden.shape[0]
    requests = lengths.shape[0]
    cache_rows = cache.shape[1]
    heads_here = q_weight.shape[1] // (NOPE + ROPE)
    q_cols = q_weight.shape[1]
    kva_cols = kva_weight.shape[1]
    kvb_cols = kvb_weight.shape[1]
    q_size = q_weight.size
    kva_size = kva_weight.size
    packed = jnp.concatenate(
        [q_weight.reshape(-1), kva_weight.reshape(-1), kvb_weight.reshape(-1)]
    )
    got_weights = gather_axis(packed, "wide")
    q_full = got_weights[:, :q_size].reshape(-1, q_cols)
    kva_full = got_weights[:, q_size : q_size + kva_size].reshape(-1, kva_cols)
    kvb_full = got_weights[:, q_size + kva_size :].reshape(-1, kvb_cols)
    o_got = gather_axis(o_weight, "wide")
    o_full = jnp.transpose(o_got, (1, 0, 2)).reshape(o_weight.shape[0], -1)

    normed = scaled_norm(hidden.astype(jnp.float32), attn_gain).astype(jnp.bfloat16)
    query_rows = jnp.dot(normed, q_full, preferred_element_type=jnp.float32).astype(jnp.bfloat16)
    compressed = jnp.dot(normed, kva_full, preferred_element_type=jnp.float32)
    first_token = wide_place * tok_rows
    token_ids = first_token + jnp.arange(tok_rows, dtype=jnp.int32)
    request_of = token_ids // SPAN
    request_ids = jnp.arange(requests, dtype=jnp.int32)
    own_length = jnp.sum(
        jnp.where(request_of[:, None] == request_ids[None, :], lengths[None, :], 0), axis=1
    )
    positions = own_length + token_ids % SPAN
    own_keys = jnp.concatenate(
        [
            scaled_norm(compressed[:, :LAT], kv_gain).astype(jnp.bfloat16),
            rotate(compressed[:, LAT:], positions).astype(jnp.bfloat16),
        ],
        axis=1,
    )

    raw_all = gather_axis(query_rows, "wide")
    total_tokens = raw_all.shape[0] * tok_rows
    raw_all = raw_all.reshape(total_tokens, heads_here, NOPE + ROPE)
    all_ids = jnp.arange(total_tokens, dtype=jnp.int32)
    all_request = all_ids // SPAN
    all_length = jnp.sum(
        jnp.where(all_request[:, None] == request_ids[None, :], lengths[None, :], 0), axis=1
    )
    all_positions = all_length + all_ids % SPAN
    kvb_heads = kvb_full.reshape(LAT, heads_here, NOPE + VDIM)
    key_maps = kvb_heads[..., :NOPE]
    value_maps = kvb_heads[..., NOPE:]
    q_rope = rotate(raw_all[..., NOPE:].astype(jnp.float32), all_positions[:, None]).astype(
        jnp.bfloat16
    )
    queries = jnp.concatenate([absorb(raw_all[..., :NOPE], key_maps), q_rope], axis=-1)

    own_request = first_token // SPAN
    blocks = [cache[request] for request in range(requests)]
    start = wide_place * cache_rows
    cache_slots = jnp.arange(cache_rows, dtype=jnp.int32)
    peaks_list = []
    totals_list = []
    values_list = []
    for request in range(requests):
        length_now = lengths[request]
        cache_live = start + cache_slots < length_now
        live_mask = jnp.broadcast_to(cache_live[None, :], (SPAN, cache_rows))
        block_live = start < length_now
        block_queries = queries[request * SPAN : (request + 1) * SPAN]
        row_peak, row_total, row_value = lax.cond(
            block_live, attend, skipped, block_queries, blocks[request], live_mask, value_maps
        )
        peaks_list.append(row_peak)
        totals_list.append(row_total)
        values_list.append(row_value)
    peak_all = jnp.concatenate(peaks_list, axis=0)
    total_all = jnp.concatenate(totals_list, axis=0)
    value_all = jnp.concatenate(values_list, axis=0)
    start_row = own_request * SPAN
    own_slots = first_token % SPAN + jnp.arange(tok_rows, dtype=jnp.int32)
    causal = own_slots[None, :] <= jnp.arange(SPAN, dtype=jnp.int32)[:, None]
    own_queries = lax.dynamic_slice_in_dim(queries, start_row, SPAN, 0)
    own_part = attend(own_queries, own_keys, causal, value_maps)
    old_part = (
        lax.dynamic_slice_in_dim(peak_all, start_row, SPAN, 0),
        lax.dynamic_slice_in_dim(total_all, start_row, SPAN, 0),
        lax.dynamic_slice_in_dim(value_all, start_row, SPAN, 0),
    )
    joint = merge_parts(old_part, own_part)
    joint_peak = joint[0].astype(jnp.bfloat16).astype(jnp.float32)
    shift = jnp.exp(joint[0] - joint_peak)
    peak_all = lax.dynamic_update_slice_in_dim(peak_all, joint_peak, start_row, 0)
    total_all = lax.dynamic_update_slice_in_dim(total_all, joint[1] * shift, start_row, 0)
    value_all = lax.dynamic_update_slice_in_dim(
        value_all, joint[2] * shift[..., None], start_row, 0
    )
    stats = jnp.concatenate([peak_all, total_all], axis=1).astype(jnp.bfloat16)
    got_stats = lax.all_to_all(
        stats.reshape(wide_count, tok_rows, 2 * heads_here), "wide", 0, 0, tiled=True
    ).astype(jnp.float32)
    got_value = lax.all_to_all(
        value_all.astype(jnp.bfloat16).reshape(wide_count, tok_rows, heads_here, VDIM),
        "wide",
        0,
        0,
        tiled=True,
    ).astype(jnp.float32)
    got_peak = got_stats[..., :heads_here]
    got_total = got_stats[..., heads_here:]
    peak_value = jnp.max(got_peak, axis=0)
    factor = jnp.exp(got_peak - peak_value[None])
    denominator = jnp.sum(factor * got_total, axis=0)
    numerator = jnp.sum(factor[..., None] * got_value, axis=0)
    context = (
        (numerator / denominator[..., None])
        .astype(jnp.bfloat16)
        .reshape(tok_rows, heads_here * VDIM)
    )
    partial_out = jnp.dot(context, o_full, preferred_element_type=jnp.float32)
    narrow_count = lax.axis_size("narrow")
    out_cols = partial_out.shape[1]
    pieces = jnp.transpose(
        partial_out.astype(jnp.bfloat16).reshape(tok_rows, narrow_count, out_cols // narrow_count),
        (1, 0, 2),
    )
    got_pieces = lax.all_to_all(pieces, "narrow", 0, 0, tiled=True)
    mine = jnp.sum(got_pieces.astype(jnp.float32), axis=0).astype(jnp.bfloat16)
    all_pieces = gather_axis(mine, "narrow")
    return jnp.transpose(all_pieces, (1, 0, 2)).reshape(tok_rows, out_cols)


def solution(mesh):
    in_specs = (
        P("wide", None),
        P(),
        P("wide", "narrow"),
        P("wide", None),
        P(),
        P("wide", "narrow"),
        P("narrow", "wide"),
        P(None, "wide", None),
        P(),
    )
    out_specs = P("wide", None)
    return jax.shard_map(
        per_device, mesh=mesh, in_specs=in_specs, out_specs=out_specs, check_vma=False
    )
```

```python
import jax
import jax.numpy as jnp
from jax import lax
from jax.sharding import PartitionSpec as P

NOPE = 128
ROPE = 64
VDIM = 128
LAT = 512
SPAN = 512


eps = 1e-06
score_scale = 1.0 / 13.856406460551018


def rotate(values, positions):
    half_size = values.shape[-1] // 2
    frequency = 10000.0 ** (-jnp.arange(half_size, dtype=jnp.float32) / half_size)
    angles = positions.astype(jnp.float32)[..., None] * frequency
    lower_half = values[..., :half_size]
    upper_half = values[..., half_size:]
    cosine = jnp.cos(angles)
    sine_part = jnp.sin(angles)
    return jnp.concatenate(
        [
            lower_half * cosine - upper_half * sine_part,
            lower_half * sine_part + upper_half * cosine,
        ],
        axis=-1,
    )


def scaled_norm(values, gain):
    return (
        values
        * lax.rsqrt(jnp.mean(values * values, axis=-1, keepdims=True) + eps)
        * gain.astype(jnp.float32)
    )


def gather_axis(x, axis_name):
    count = lax.axis_size(axis_name)
    spread = jnp.broadcast_to(x[None], (count,) + x.shape)
    return lax.all_to_all(spread, axis_name, split_axis=0, concat_axis=0, tiled=True)


def absorb(nope_part, key_maps):
    return jnp.einsum(
        "thc,lhc->thl", nope_part, key_maps, preferred_element_type=jnp.float32
    ).astype(jnp.bfloat16)


def project_values(mixed, value_maps):
    upper_part = mixed.astype(jnp.bfloat16)
    lower_part = (mixed - upper_part.astype(jnp.float32)).astype(jnp.bfloat16)
    first_term = jnp.einsum(
        "qhc,chv->qhv", upper_part, value_maps, preferred_element_type=jnp.float32
    )
    second_term = jnp.einsum(
        "qhc,chv->qhv", lower_part, value_maps, preferred_element_type=jnp.float32
    )
    return first_term + second_term


def attend(block_queries, key_rows, live_mask, value_maps):
    scores = (
        jnp.einsum("qhc,kc->qhk", block_queries, key_rows, preferred_element_type=jnp.float32)
        * score_scale
    )
    live_rows = live_mask[:, None, :]
    row_peak = jnp.max(jnp.where(live_rows, scores, -1e30), axis=-1)
    row_peak = row_peak.astype(jnp.bfloat16).astype(jnp.float32)
    weights = jnp.where(live_rows, jnp.exp(scores - row_peak[..., None]), 0.0)
    row_total = jnp.sum(weights, axis=-1)
    mixed = jnp.einsum(
        "qhk,kc->qhc",
        weights.astype(jnp.bfloat16),
        key_rows[:, :LAT],
        preferred_element_type=jnp.float32,
    )
    return (row_peak, row_total, project_values(mixed, value_maps))


def skipped(block_queries, key_rows, live_mask, value_maps):
    rows_here = block_queries.shape[0]
    heads_here = block_queries.shape[1]
    return (
        jnp.full((rows_here, heads_here), -1e30, jnp.float32),
        jnp.zeros((rows_here, heads_here), jnp.float32),
        jnp.zeros((rows_here, heads_here, value_maps.shape[2]), jnp.float32),
    )


def merge_parts(first, second):
    joint_peak = jnp.maximum(first[0], second[0])
    first_factor = jnp.exp(first[0] - joint_peak)
    second_factor = jnp.exp(second[0] - joint_peak)
    joint_total = first_factor * first[1] + second_factor * second[1]
    joint_value = first_factor[..., None] * first[2] + second_factor[..., None] * second[2]
    return (joint_peak, joint_total, joint_value)


def per_device(
    hidden, attn_gain, q_weight, kva_weight, kv_gain, kvb_weight, o_weight, cache, lengths
):
    wide_count = lax.axis_size("wide")
    wide_place = lax.axis_index("wide")
    tok_rows = hidden.shape[0]
    requests = lengths.shape[0]
    cache_rows = cache.shape[1]
    heads_here = q_weight.shape[1] // (NOPE + ROPE)
    narrow_count = lax.axis_size("narrow")
    narrow_place = lax.axis_index("narrow")
    q_cols = q_weight.shape[1]
    kva_cols = kva_weight.shape[1]
    kva_part = kva_cols // narrow_count
    kva_mine = lax.dynamic_slice_in_dim(kva_weight, narrow_place * kva_part, kva_part, 1)
    packed = jnp.concatenate([q_weight, kva_mine], axis=1)
    got_weights = gather_axis(packed, "wide")
    proj_full = got_weights.reshape(-1, q_cols + kva_part)
    kvb_full = gather_axis(kvb_weight, "wide").reshape(-1, kvb_weight.shape[1])
    o_got = gather_axis(o_weight, "wide")

    normed = scaled_norm(hidden.astype(jnp.float32), attn_gain).astype(jnp.bfloat16)
    projected = jnp.dot(normed, proj_full, preferred_element_type=jnp.float32)
    query_rows = projected[:, :q_cols].astype(jnp.bfloat16)
    compressed_part = projected[:, q_cols:]
    compressed = jnp.transpose(gather_axis(compressed_part, "narrow"), (1, 0, 2)).reshape(
        tok_rows, kva_cols
    )
    first_token = wide_place * tok_rows
    token_ids = first_token + jnp.arange(tok_rows, dtype=jnp.int32)
    positions = lengths[token_ids // SPAN] + token_ids % SPAN
    own_keys = jnp.concatenate(
        [
            scaled_norm(compressed[:, :LAT], kv_gain).astype(jnp.bfloat16),
            rotate(compressed[:, LAT:], positions).astype(jnp.bfloat16),
        ],
        axis=1,
    )

    query_heads = query_rows.reshape(tok_rows, heads_here, NOPE + ROPE)
    outgoing = jnp.concatenate(
        [
            query_heads[..., :NOPE].reshape(tok_rows, heads_here * NOPE),
            query_heads[..., NOPE:].reshape(tok_rows, heads_here * ROPE),
        ],
        axis=1,
    )
    raw_all = gather_axis(outgoing, "wide")
    total_tokens = raw_all.shape[0] * tok_rows
    raw_all = raw_all.reshape(total_tokens, heads_here * (NOPE + ROPE))
    all_ids = jnp.arange(total_tokens, dtype=jnp.int32)
    all_positions = lengths[all_ids // SPAN] + all_ids % SPAN
    kvb_heads = kvb_full.reshape(LAT, heads_here, NOPE + VDIM)
    key_maps = kvb_heads[..., :NOPE]
    value_maps = kvb_heads[..., NOPE:]
    nope_all = raw_all[:, : heads_here * NOPE].reshape(total_tokens, heads_here, NOPE)
    rope_all = raw_all[:, heads_here * NOPE :].reshape(total_tokens, heads_here, ROPE)
    q_rope = rotate(rope_all.astype(jnp.float32), all_positions[:, None]).astype(jnp.bfloat16)
    queries = jnp.concatenate([absorb(nope_all, key_maps), q_rope], axis=-1)

    own_request = first_token // SPAN
    blocks = [cache[request] for request in range(requests)]
    start = wide_place * cache_rows
    cache_slots = jnp.arange(cache_rows, dtype=jnp.int32)
    peaks_list = []
    totals_list = []
    values_list = []
    for request in range(requests):
        length_now = lengths[request]
        cache_live = start + cache_slots < length_now
        live_mask = jnp.broadcast_to(cache_live[None, :], (SPAN, cache_rows))
        block_live = start < length_now
        block_queries = queries[request * SPAN : (request + 1) * SPAN]
        row_peak, row_total, row_value = lax.cond(
            block_live, attend, skipped, block_queries, blocks[request], live_mask, value_maps
        )
        peaks_list.append(row_peak)
        totals_list.append(row_total)
        values_list.append(row_value)
    peak_all = jnp.concatenate(peaks_list, axis=0)
    total_all = jnp.concatenate(totals_list, axis=0)
    value_all = jnp.concatenate(values_list, axis=0)
    start_row = own_request * SPAN
    own_slots = first_token % SPAN + jnp.arange(tok_rows, dtype=jnp.int32)
    causal = own_slots[None, :] <= jnp.arange(SPAN, dtype=jnp.int32)[:, None]
    own_queries = lax.dynamic_slice_in_dim(queries, start_row, SPAN, 0)
    own_part = attend(own_queries, own_keys, causal, value_maps)
    old_part = (
        lax.dynamic_slice_in_dim(peak_all, start_row, SPAN, 0),
        lax.dynamic_slice_in_dim(total_all, start_row, SPAN, 0),
        lax.dynamic_slice_in_dim(value_all, start_row, SPAN, 0),
    )
    joint = merge_parts(old_part, own_part)
    joint_peak = joint[0].astype(jnp.bfloat16).astype(jnp.float32)
    shift = jnp.exp(joint[0] - joint_peak)
    peak_all = lax.dynamic_update_slice_in_dim(peak_all, joint_peak, start_row, 0)
    total_all = lax.dynamic_update_slice_in_dim(total_all, joint[1] * shift, start_row, 0)
    value_all = lax.dynamic_update_slice_in_dim(
        value_all, joint[2] * shift[..., None], start_row, 0
    )
    stats = jnp.concatenate([peak_all, total_all], axis=1).astype(jnp.bfloat16)
    got_stats = lax.all_to_all(
        stats.reshape(wide_count, tok_rows, 2 * heads_here), "wide", 0, 0, tiled=True
    ).astype(jnp.float32)
    got_value = lax.all_to_all(
        value_all.astype(jnp.bfloat16).reshape(wide_count, tok_rows, heads_here, VDIM),
        "wide",
        0,
        0,
        tiled=True,
    ).astype(jnp.float32)
    got_peak = got_stats[..., :heads_here]
    got_total = got_stats[..., heads_here:]
    peak_value = jnp.max(got_peak, axis=0)
    factor = jnp.exp(got_peak - peak_value[None])
    denominator = jnp.sum(factor * got_total, axis=0)
    numerator = jnp.sum(factor[..., None] * got_value, axis=0)
    context = (
        (numerator / denominator[..., None])
        .astype(jnp.bfloat16)
        .reshape(tok_rows, heads_here * VDIM)
    )
    partial_out = jnp.einsum(
        "tk,wkc->twc", context, o_got, preferred_element_type=jnp.float32
    ).reshape(tok_rows, -1)
    out_cols = partial_out.shape[1]
    pieces = jnp.transpose(
        partial_out.astype(jnp.bfloat16).reshape(tok_rows, narrow_count, out_cols // narrow_count),
        (1, 0, 2),
    )
    got_pieces = lax.all_to_all(pieces, "narrow", 0, 0, tiled=True)
    mine = jnp.sum(got_pieces.astype(jnp.float32), axis=0).astype(jnp.bfloat16)
    all_pieces = gather_axis(mine, "narrow")
    return jnp.transpose(all_pieces, (1, 0, 2)).reshape(tok_rows, out_cols)


def solution(mesh):
    in_specs = (
        P("wide", None),
        P(),
        P("wide", "narrow"),
        P("wide", None),
        P(),
        P("wide", "narrow"),
        P("narrow", "wide"),
        P(None, "wide", None),
        P(),
    )
    out_specs = P("wide", None)
    return jax.shard_map(
        per_device, mesh=mesh, in_specs=in_specs, out_specs=out_specs, check_vma=False
    )
```

```python
import jax
import jax.numpy as jnp
from jax import lax
from jax.sharding import PartitionSpec as P
from jax.experimental import pallas as pl
from jax.experimental.pallas import tpu as pltpu

NOPE = 128
ROPE = 64
VDIM = 128
LAT = 512
SPAN = 512


eps = 1e-06
score_scale = 1.0 / 13.856406460551018


def rotate(values, positions):
    half_size = values.shape[-1] // 2
    frequency = 10000.0 ** (-jnp.arange(half_size, dtype=jnp.float32) / half_size)
    angles = positions.astype(jnp.float32)[..., None] * frequency
    lower_half = values[..., :half_size]
    upper_half = values[..., half_size:]
    cosine = jnp.cos(angles)
    sine_part = jnp.sin(angles)
    return jnp.concatenate(
        [
            lower_half * cosine - upper_half * sine_part,
            lower_half * sine_part + upper_half * cosine,
        ],
        axis=-1,
    )


def scaled_norm(values, gain):
    return (
        values
        * lax.rsqrt(jnp.mean(values * values, axis=-1, keepdims=True) + eps)
        * gain.astype(jnp.float32)
    )


def gather_axis(x, axis_name):
    count = lax.axis_size(axis_name)
    spread = jnp.broadcast_to(x[None], (count,) + x.shape)
    return lax.all_to_all(spread, axis_name, split_axis=0, concat_axis=0, tiled=True)


def absorb(nope_part, key_maps):
    return jnp.einsum(
        "thc,lhc->thl", nope_part, key_maps, preferred_element_type=jnp.float32
    ).astype(jnp.bfloat16)


def project_values(mixed, value_maps):
    upper_part = mixed.astype(jnp.bfloat16)
    lower_part = (mixed - upper_part.astype(jnp.float32)).astype(jnp.bfloat16)
    first_term = jnp.einsum(
        "qhc,chv->qhv", upper_part, value_maps, preferred_element_type=jnp.float32
    )
    second_term = jnp.einsum(
        "qhc,chv->qhv", lower_part, value_maps, preferred_element_type=jnp.float32
    )
    return first_term + second_term


def attend(block_queries, key_rows, live_mask, value_maps):
    scores = (
        jnp.einsum("qhc,kc->qhk", block_queries, key_rows, preferred_element_type=jnp.float32)
        * score_scale
    )
    live_rows = live_mask[:, None, :]
    row_peak = jnp.max(jnp.where(live_rows, scores, -1e30), axis=-1)
    weights = jnp.where(live_rows, jnp.exp(scores - row_peak[..., None]), 0.0)
    row_total = jnp.sum(weights, axis=-1)
    mixed = jnp.einsum(
        "qhk,kc->qhc",
        weights.astype(jnp.bfloat16),
        key_rows[:, :LAT],
        preferred_element_type=jnp.float32,
    )
    return (row_peak, row_total, project_values(mixed, value_maps))


def skipped(block_queries, key_rows, live_mask, value_maps):
    rows_here = block_queries.shape[0]
    heads_here = block_queries.shape[1]
    return (
        jnp.full((rows_here, heads_here), -1e30, jnp.float32),
        jnp.zeros((rows_here, heads_here), jnp.float32),
        jnp.zeros((rows_here, heads_here, value_maps.shape[2]), jnp.float32),
    )


def cache_kernel(lens_ref, base_ref, lat_ref, rope_ref, kv_ref, vm_ref, peak_ref, total_ref, value_ref):
    length_now = lens_ref[pl.program_id(0)]
    base = base_ref[0]
    live_block = base < length_now

    @pl.when(live_block)
    def _():
        keys = kv_ref[0]
        key_lat = keys[:, :LAT]
        key_rope = keys[:, LAT:]
        nt = (((1,), (1,)), ((), ()))
        scores = (
            lax.dot_general(lat_ref[0], key_lat, nt, preferred_element_type=jnp.float32)
            + lax.dot_general(rope_ref[0], key_rope, nt, preferred_element_type=jnp.float32)
        ) * score_scale
        slots = base + lax.broadcasted_iota(jnp.int32, scores.shape, 1)
        live = slots < length_now
        peak = jnp.max(jnp.where(live, scores, -1e30), axis=-1, keepdims=True)
        weights = jnp.where(live, jnp.exp(scores - peak), 0.0)
        peak_ref[0] = peak
        total_ref[0] = jnp.sum(weights, axis=-1, keepdims=True)
        mixed = jnp.dot(weights.astype(jnp.bfloat16), key_lat, preferred_element_type=jnp.float32)
        value_map = vm_ref[0]
        upper_part = mixed.astype(jnp.bfloat16)
        lower_part = (mixed - upper_part.astype(jnp.float32)).astype(jnp.bfloat16)
        value_ref[0] = jnp.dot(upper_part, value_map, preferred_element_type=jnp.float32) + jnp.dot(
            lower_part, value_map, preferred_element_type=jnp.float32
        )

    @pl.when(jnp.logical_not(live_block))
    def _():
        peak_ref[...] = jnp.full(peak_ref.shape, -1e30, jnp.float32)
        total_ref[...] = jnp.zeros(total_ref.shape, jnp.float32)
        value_ref[...] = jnp.zeros(value_ref.shape, jnp.float32)


def cache_attention(lengths, base, lat_hm, rope_hm, cache, value_hm):
    heads_here, total_tokens, _ = lat_hm.shape
    requests, cache_rows, width = cache.shape
    span = total_tokens // requests
    vdim = value_hm.shape[2]
    grid_spec = pltpu.PrefetchScalarGridSpec(
        num_scalar_prefetch=2,
        grid=(requests, heads_here),
        in_specs=[
            pl.BlockSpec((1, span, LAT), lambda r, h, lens, b: (h, r, 0)),
            pl.BlockSpec((1, span, ROPE), lambda r, h, lens, b: (h, r, 0)),
            pl.BlockSpec((1, cache_rows, width), lambda r, h, lens, b: (r, 0, 0)),
            pl.BlockSpec((1, LAT, vdim), lambda r, h, lens, b: (h, 0, 0)),
        ],
        out_specs=[
            pl.BlockSpec((1, span, 1), lambda r, h, lens, b: (h, r, 0)),
            pl.BlockSpec((1, span, 1), lambda r, h, lens, b: (h, r, 0)),
            pl.BlockSpec((1, span, vdim), lambda r, h, lens, b: (h, r, 0)),
        ],
    )
    return pl.pallas_call(
        cache_kernel,
        grid_spec=grid_spec,
        out_shape=[
            jax.ShapeDtypeStruct((heads_here, total_tokens, 1), jnp.float32),
            jax.ShapeDtypeStruct((heads_here, total_tokens, 1), jnp.float32),
            jax.ShapeDtypeStruct((heads_here, total_tokens, vdim), jnp.float32),
        ],
        compiler_params=pltpu.CompilerParams(dimension_semantics=("arbitrary", "arbitrary")),
    )(lengths, base, lat_hm, rope_hm, cache, value_hm)


def merge_parts(first, second):
    joint_peak = jnp.maximum(first[0], second[0])
    first_factor = jnp.exp(first[0] - joint_peak)
    second_factor = jnp.exp(second[0] - joint_peak)
    joint_total = first_factor * first[1] + second_factor * second[1]
    joint_value = first_factor[..., None] * first[2] + second_factor[..., None] * second[2]
    return (joint_peak, joint_total, joint_value)


def per_device(
    hidden, attn_gain, q_weight, kva_weight, kv_gain, kvb_weight, o_weight, cache, lengths
):
    wide_count = lax.axis_size("wide")
    wide_place = lax.axis_index("wide")
    tok_rows = hidden.shape[0]
    requests = lengths.shape[0]
    cache_rows = cache.shape[1]
    heads_here = q_weight.shape[1] // (NOPE + ROPE)
    narrow_count = lax.axis_size("narrow")
    narrow_place = lax.axis_index("narrow")
    q_cols = q_weight.shape[1]
    kva_cols = kva_weight.shape[1]
    kva_part = kva_cols // narrow_count
    kva_mine = lax.dynamic_slice_in_dim(kva_weight, narrow_place * kva_part, kva_part, 1)
    packed = jnp.concatenate([q_weight, kva_mine], axis=1)
    got_weights = gather_axis(packed, "wide")
    proj_full = got_weights.reshape(-1, q_cols + kva_part)
    kvb_full = gather_axis(kvb_weight, "wide").reshape(-1, kvb_weight.shape[1])
    o_got = gather_axis(o_weight, "wide")

    normed = scaled_norm(hidden.astype(jnp.float32), attn_gain).astype(jnp.bfloat16)
    projected = jnp.dot(normed, proj_full, preferred_element_type=jnp.float32)
    query_rows = projected[:, :q_cols].astype(jnp.bfloat16)
    compressed_part = projected[:, q_cols:]
    compressed = jnp.transpose(gather_axis(compressed_part, "narrow"), (1, 0, 2)).reshape(
        tok_rows, kva_cols
    )
    first_token = wide_place * tok_rows
    token_ids = first_token + jnp.arange(tok_rows, dtype=jnp.int32)
    positions = lengths[token_ids // SPAN] + token_ids % SPAN
    own_keys = jnp.concatenate(
        [
            scaled_norm(compressed[:, :LAT], kv_gain).astype(jnp.bfloat16),
            rotate(compressed[:, LAT:], positions).astype(jnp.bfloat16),
        ],
        axis=1,
    )

    query_heads = query_rows.reshape(tok_rows, heads_here, NOPE + ROPE)
    outgoing = jnp.concatenate(
        [
            query_heads[..., :NOPE].reshape(tok_rows, heads_here * NOPE),
            query_heads[..., NOPE:].reshape(tok_rows, heads_here * ROPE),
        ],
        axis=1,
    )
    raw_all = gather_axis(outgoing, "wide")
    total_tokens = raw_all.shape[0] * tok_rows
    raw_all = raw_all.reshape(total_tokens, heads_here * (NOPE + ROPE))
    all_ids = jnp.arange(total_tokens, dtype=jnp.int32)
    all_positions = lengths[all_ids // SPAN] + all_ids % SPAN
    kvb_heads = kvb_full.reshape(LAT, heads_here, NOPE + VDIM)
    key_maps = kvb_heads[..., :NOPE]
    value_maps = kvb_heads[..., NOPE:]
    nope_all = raw_all[:, : heads_here * NOPE].reshape(total_tokens, heads_here, NOPE)
    rope_all = raw_all[:, heads_here * NOPE :].reshape(total_tokens, heads_here, ROPE)
    q_rope = rotate(rope_all.astype(jnp.float32), all_positions[:, None]).astype(jnp.bfloat16)
    lat_hm = jnp.einsum(
        "thc,lhc->htl", nope_all, key_maps, preferred_element_type=jnp.float32
    ).astype(jnp.bfloat16)
    rope_hm = jnp.transpose(q_rope, (1, 0, 2))
    value_hm = jnp.transpose(value_maps, (1, 0, 2))

    base = (wide_place * cache_rows).reshape(1).astype(jnp.int32)
    peak_hm, total_hm, value_out = cache_attention(lengths, base, lat_hm, rope_hm, cache, value_hm)
    peak_hm = peak_hm[..., 0]
    total_hm = total_hm[..., 0]

    own_request = first_token // SPAN
    start_row = own_request * SPAN
    own_slots = first_token % SPAN + jnp.arange(tok_rows, dtype=jnp.int32)
    causal = own_slots[None, :] <= jnp.arange(SPAN, dtype=jnp.int32)[:, None]
    own_lat = lax.dynamic_slice_in_dim(lat_hm, start_row, SPAN, 1)
    own_rope = lax.dynamic_slice_in_dim(rope_hm, start_row, SPAN, 1)
    own_scores = (
        jnp.einsum("hqc,kc->hqk", own_lat, own_keys[:, :LAT], preferred_element_type=jnp.float32)
        + jnp.einsum("hqc,kc->hqk", own_rope, own_keys[:, LAT:], preferred_element_type=jnp.float32)
    ) * score_scale
    own_live = causal[None]
    own_peak = jnp.max(jnp.where(own_live, own_scores, -1e30), axis=-1)
    own_weights = jnp.where(own_live, jnp.exp(own_scores - own_peak[..., None]), 0.0)
    own_total = jnp.sum(own_weights, axis=-1)
    own_mixed = jnp.einsum(
        "hqk,kc->hqc", own_weights.astype(jnp.bfloat16), own_keys[:, :LAT],
        preferred_element_type=jnp.float32,
    )
    own_upper = own_mixed.astype(jnp.bfloat16)
    own_lower = (own_mixed - own_upper.astype(jnp.float32)).astype(jnp.bfloat16)
    own_value = jnp.einsum(
        "hqc,hcv->hqv", own_upper, value_hm, preferred_element_type=jnp.float32
    ) + jnp.einsum("hqc,hcv->hqv", own_lower, value_hm, preferred_element_type=jnp.float32)
    old_part = (
        lax.dynamic_slice_in_dim(peak_hm, start_row, SPAN, 1),
        lax.dynamic_slice_in_dim(total_hm, start_row, SPAN, 1),
        lax.dynamic_slice_in_dim(value_out, start_row, SPAN, 1),
    )
    joint = merge_parts(old_part, (own_peak, own_total, own_value))
    peak_hm = lax.dynamic_update_slice_in_dim(peak_hm, joint[0], start_row, 1)
    total_hm = lax.dynamic_update_slice_in_dim(total_hm, joint[1], start_row, 1)
    value_out = lax.dynamic_update_slice_in_dim(value_out, joint[2], start_row, 1)

    stats = jnp.stack([peak_hm, total_hm], axis=0).astype(jnp.bfloat16)
    got_stats = lax.all_to_all(
        stats.reshape(2, heads_here, wide_count, tok_rows), "wide", 2, 2, tiled=True
    ).astype(jnp.float32)
    got_value = lax.all_to_all(
        value_out.astype(jnp.bfloat16).reshape(heads_here, wide_count, tok_rows, VDIM),
        "wide",
        1,
        1,
        tiled=True,
    ).astype(jnp.float32)
    got_peak = got_stats[0]
    got_total = got_stats[1]
    peak_value = jnp.max(got_peak, axis=1)
    factor = jnp.exp(got_peak - peak_value[:, None])
    denominator = jnp.sum(factor * got_total, axis=1)
    numerator = jnp.sum(factor[..., None] * got_value, axis=1)
    context = jnp.transpose(
        (numerator / denominator[..., None]).astype(jnp.bfloat16), (1, 0, 2)
    ).reshape(tok_rows, heads_here * VDIM)
    partial_out = jnp.einsum(
        "tk,wkc->twc", context, o_got, preferred_element_type=jnp.float32
    ).reshape(tok_rows, -1)
    out_cols = partial_out.shape[1]
    pieces = jnp.transpose(
        partial_out.astype(jnp.bfloat16).reshape(tok_rows, narrow_count, out_cols // narrow_count),
        (1, 0, 2),
    )
    got_pieces = lax.all_to_all(pieces, "narrow", 0, 0, tiled=True)
    mine = jnp.sum(got_pieces.astype(jnp.float32), axis=0).astype(jnp.bfloat16)
    all_pieces = gather_axis(mine, "narrow")
    return jnp.transpose(all_pieces, (1, 0, 2)).reshape(tok_rows, out_cols)


def solution(mesh):
    in_specs = (
        P("wide", None),
        P(),
        P("wide", "narrow"),
        P("wide", None),
        P(),
        P("wide", "narrow"),
        P("narrow", "wide"),
        P(None, "wide", None),
        P(),
    )
    out_specs = P("wide", None)
    return jax.shard_map(
        per_device, mesh=mesh, in_specs=in_specs, out_specs=out_specs, check_vma=False
    )
```

```python
import jax
import jax.numpy as jnp
from jax import lax
from jax.sharding import PartitionSpec as P
from jax.experimental import pallas as pl
from jax.experimental.pallas import tpu as pltpu

NOPE = 128
ROPE = 64
VDIM = 128
LAT = 512
SPAN = 512


eps = 1e-06
score_scale = 1.0 / 13.856406460551018


def rotate(values, positions):
    half_size = values.shape[-1] // 2
    frequency = 10000.0 ** (-jnp.arange(half_size, dtype=jnp.float32) / half_size)
    angles = positions.astype(jnp.float32)[..., None] * frequency
    lower_half = values[..., :half_size]
    upper_half = values[..., half_size:]
    cosine = jnp.cos(angles)
    sine_part = jnp.sin(angles)
    return jnp.concatenate(
        [
            lower_half * cosine - upper_half * sine_part,
            lower_half * sine_part + upper_half * cosine,
        ],
        axis=-1,
    )


def scaled_norm(values, gain):
    return (
        values
        * lax.rsqrt(jnp.mean(values * values, axis=-1, keepdims=True) + eps)
        * gain.astype(jnp.float32)
    )


def gather_axis(x, axis_name):
    count = lax.axis_size(axis_name)
    spread = jnp.broadcast_to(x[None], (count,) + x.shape)
    return lax.all_to_all(spread, axis_name, split_axis=0, concat_axis=0, tiled=True)


def absorb(nope_part, key_maps):
    return jnp.einsum(
        "thc,lhc->thl", nope_part, key_maps, preferred_element_type=jnp.float32
    ).astype(jnp.bfloat16)


def project_values(mixed, value_maps):
    upper_part = mixed.astype(jnp.bfloat16)
    lower_part = (mixed - upper_part.astype(jnp.float32)).astype(jnp.bfloat16)
    first_term = jnp.einsum(
        "qhc,chv->qhv", upper_part, value_maps, preferred_element_type=jnp.float32
    )
    second_term = jnp.einsum(
        "qhc,chv->qhv", lower_part, value_maps, preferred_element_type=jnp.float32
    )
    return first_term + second_term


def attend(block_queries, key_rows, live_mask, value_maps):
    scores = (
        jnp.einsum("qhc,kc->qhk", block_queries, key_rows, preferred_element_type=jnp.float32)
        * score_scale
    )
    live_rows = live_mask[:, None, :]
    row_peak = jnp.max(jnp.where(live_rows, scores, -1e30), axis=-1)
    weights = jnp.where(live_rows, jnp.exp(scores - row_peak[..., None]), 0.0)
    row_total = jnp.sum(weights, axis=-1)
    mixed = jnp.einsum(
        "qhk,kc->qhc",
        weights.astype(jnp.bfloat16),
        key_rows[:, :LAT],
        preferred_element_type=jnp.float32,
    )
    return (row_peak, row_total, project_values(mixed, value_maps))


def skipped(block_queries, key_rows, live_mask, value_maps):
    rows_here = block_queries.shape[0]
    heads_here = block_queries.shape[1]
    return (
        jnp.full((rows_here, heads_here), -1e30, jnp.float32),
        jnp.zeros((rows_here, heads_here), jnp.float32),
        jnp.zeros((rows_here, heads_here, value_maps.shape[2]), jnp.float32),
    )


def cache_kernel(
    lens_ref, base_ref, nope_ref, rope_ref, kv_ref, km_ref, vm_ref, peak_ref, total_ref, value_ref
):
    length_now = lens_ref[pl.program_id(0)]
    base = base_ref[0]
    cache_rows = kv_ref.shape[1]
    nt = (((1,), (1,)), ((), ()))

    def compute(masked):
        keys = kv_ref[0]
        key_lat = keys[:, :LAT]
        key_rope = keys[:, LAT:]
        q_lat = lax.dot_general(
            nope_ref[...], km_ref[...], nt, preferred_element_type=jnp.float32
        ).astype(jnp.bfloat16)
        scores = (
            lax.dot_general(q_lat, key_lat, nt, preferred_element_type=jnp.float32)
            + lax.dot_general(rope_ref[0], key_rope, nt, preferred_element_type=jnp.float32)
        ) * score_scale
        if masked:
            slots = base + lax.broadcasted_iota(jnp.int32, scores.shape, 1)
            live = slots < length_now
            peak = jnp.max(jnp.where(live, scores, -1e30), axis=-1, keepdims=True)
            weights = jnp.where(live, jnp.exp(scores - peak), 0.0)
        else:
            peak = jnp.max(scores, axis=-1, keepdims=True)
            weights = jnp.exp(scores - peak)
        peak_ref[0] = peak
        total_ref[0] = jnp.sum(weights, axis=-1, keepdims=True)
        mixed = jnp.dot(weights.astype(jnp.bfloat16), key_lat, preferred_element_type=jnp.float32)
        value_map = vm_ref[...]
        upper_part = mixed.astype(jnp.bfloat16)
        lower_part = (mixed - upper_part.astype(jnp.float32)).astype(jnp.bfloat16)
        value_ref[0] = jnp.dot(upper_part, value_map, preferred_element_type=jnp.float32) + jnp.dot(
            lower_part, value_map, preferred_element_type=jnp.float32
        )

    whole_live = base + cache_rows <= length_now
    part_live = jnp.logical_and(base < length_now, jnp.logical_not(whole_live))

    @pl.when(whole_live)
    def _():
        compute(False)

    @pl.when(part_live)
    def _():
        compute(True)

    @pl.when(base >= length_now)
    def _():
        peak_ref[...] = jnp.full(peak_ref.shape, -1e30, jnp.float32)
        total_ref[...] = jnp.zeros(total_ref.shape, jnp.float32)
        value_ref[...] = jnp.zeros(value_ref.shape, jnp.float32)


def cache_attention(lengths, base, nope_rows, rope_hm, cache, kvb_full):
    heads_here, total_tokens, _ = rope_hm.shape
    requests, cache_rows, width = cache.shape
    span = total_tokens // requests
    grid_spec = pltpu.PrefetchScalarGridSpec(
        num_scalar_prefetch=2,
        grid=(requests, heads_here),
        in_specs=[
            pl.BlockSpec((span, NOPE), lambda r, h, lens, b: (r, h)),
            pl.BlockSpec((1, span, ROPE), lambda r, h, lens, b: (h, r, 0)),
            pl.BlockSpec((1, cache_rows, width), lambda r, h, lens, b: (r, 0, 0)),
            pl.BlockSpec((LAT, NOPE), lambda r, h, lens, b: (0, 2 * h)),
            pl.BlockSpec((LAT, VDIM), lambda r, h, lens, b: (0, 2 * h + 1)),
        ],
        out_specs=[
            pl.BlockSpec((1, span, 1), lambda r, h, lens, b: (h, r, 0)),
            pl.BlockSpec((1, span, 1), lambda r, h, lens, b: (h, r, 0)),
            pl.BlockSpec((1, span, VDIM), lambda r, h, lens, b: (h, r, 0)),
        ],
    )
    return pl.pallas_call(
        cache_kernel,
        grid_spec=grid_spec,
        out_shape=[
            jax.ShapeDtypeStruct((heads_here, total_tokens, 1), jnp.float32),
            jax.ShapeDtypeStruct((heads_here, total_tokens, 1), jnp.float32),
            jax.ShapeDtypeStruct((heads_here, total_tokens, VDIM), jnp.float32),
        ],
        compiler_params=pltpu.CompilerParams(dimension_semantics=("arbitrary", "arbitrary")),
    )(lengths, base, nope_rows, rope_hm, cache, kvb_full, kvb_full)

def merge_parts(first, second):
    joint_peak = jnp.maximum(first[0], second[0])
    first_factor = jnp.exp(first[0] - joint_peak)
    second_factor = jnp.exp(second[0] - joint_peak)
    joint_total = first_factor * first[1] + second_factor * second[1]
    joint_value = first_factor[..., None] * first[2] + second_factor[..., None] * second[2]
    return (joint_peak, joint_total, joint_value)


def per_device(
    hidden, attn_gain, q_weight, kva_weight, kv_gain, kvb_weight, o_weight, cache, lengths
):
    wide_count = lax.axis_size("wide")
    wide_place = lax.axis_index("wide")
    tok_rows = hidden.shape[0]
    requests = lengths.shape[0]
    cache_rows = cache.shape[1]
    heads_here = q_weight.shape[1] // (NOPE + ROPE)
    narrow_count = lax.axis_size("narrow")
    narrow_place = lax.axis_index("narrow")
    q_cols = q_weight.shape[1]
    kva_cols = kva_weight.shape[1]
    kva_part = kva_cols // narrow_count
    kva_mine = lax.dynamic_slice_in_dim(kva_weight, narrow_place * kva_part, kva_part, 1)
    packed = jnp.concatenate([q_weight, kva_mine], axis=1)
    got_weights = gather_axis(packed, "wide")
    proj_full = got_weights.reshape(-1, q_cols + kva_part)
    kvb_full = gather_axis(kvb_weight, "wide").reshape(-1, kvb_weight.shape[1])
    o_got = gather_axis(o_weight, "wide")

    normed = scaled_norm(hidden.astype(jnp.float32), attn_gain).astype(jnp.bfloat16)
    projected = jnp.dot(normed, proj_full, preferred_element_type=jnp.float32)
    query_rows = projected[:, :q_cols].astype(jnp.bfloat16)
    compressed_part = projected[:, q_cols:]
    compressed = jnp.transpose(gather_axis(compressed_part, "narrow"), (1, 0, 2)).reshape(
        tok_rows, kva_cols
    )
    first_token = wide_place * tok_rows
    token_ids = first_token + jnp.arange(tok_rows, dtype=jnp.int32)
    positions = lengths[token_ids // SPAN] + token_ids % SPAN
    own_keys = jnp.concatenate(
        [
            scaled_norm(compressed[:, :LAT], kv_gain).astype(jnp.bfloat16),
            rotate(compressed[:, LAT:], positions).astype(jnp.bfloat16),
        ],
        axis=1,
    )

    query_heads = query_rows.reshape(tok_rows, heads_here, NOPE + ROPE)
    outgoing = jnp.concatenate(
        [
            query_heads[..., :NOPE].reshape(tok_rows, heads_here * NOPE),
            query_heads[..., NOPE:].reshape(tok_rows, heads_here * ROPE),
        ],
        axis=1,
    )
    raw_all = gather_axis(outgoing, "wide")
    total_tokens = raw_all.shape[0] * tok_rows
    raw_all = raw_all.reshape(total_tokens, heads_here * (NOPE + ROPE))
    all_ids = jnp.arange(total_tokens, dtype=jnp.int32)
    all_positions = lengths[all_ids // SPAN] + all_ids % SPAN
    kvb_heads = kvb_full.reshape(LAT, heads_here, NOPE + VDIM)
    key_maps = kvb_heads[..., :NOPE]
    value_maps = kvb_heads[..., NOPE:]
    nope_all = raw_all[:, : heads_here * NOPE].reshape(total_tokens, heads_here, NOPE)
    rope_all = raw_all[:, heads_here * NOPE :].reshape(total_tokens, heads_here, ROPE)
    q_rope = rotate(rope_all.astype(jnp.float32), all_positions[:, None]).astype(jnp.bfloat16)
    rope_hm = jnp.transpose(q_rope, (1, 0, 2))

    base = (wide_place * cache_rows).reshape(1).astype(jnp.int32)
    peak_hm, total_hm, value_out = cache_attention(
        lengths, base, raw_all, rope_hm, cache, kvb_full
    )
    peak_hm = peak_hm[..., 0]
    total_hm = total_hm[..., 0]

    own_request = first_token // SPAN
    start_row = own_request * SPAN
    own_slots = first_token % SPAN + jnp.arange(tok_rows, dtype=jnp.int32)
    causal = own_slots[None, :] <= jnp.arange(SPAN, dtype=jnp.int32)[:, None]
    own_lat = jnp.einsum(
        "thc,lhc->htl",
        lax.dynamic_slice_in_dim(nope_all, start_row, SPAN, 0),
        key_maps,
        preferred_element_type=jnp.float32,
    ).astype(jnp.bfloat16)
    own_rope = lax.dynamic_slice_in_dim(rope_hm, start_row, SPAN, 1)
    own_scores = (
        jnp.einsum("hqc,kc->hqk", own_lat, own_keys[:, :LAT], preferred_element_type=jnp.float32)
        + jnp.einsum("hqc,kc->hqk", own_rope, own_keys[:, LAT:], preferred_element_type=jnp.float32)
    ) * score_scale
    own_live = causal[None]
    own_peak = jnp.max(jnp.where(own_live, own_scores, -1e30), axis=-1)
    own_weights = jnp.where(own_live, jnp.exp(own_scores - own_peak[..., None]), 0.0)
    own_total = jnp.sum(own_weights, axis=-1)
    own_mixed = jnp.einsum(
        "hqk,kc->hqc", own_weights.astype(jnp.bfloat16), own_keys[:, :LAT],
        preferred_element_type=jnp.float32,
    )
    own_upper = own_mixed.astype(jnp.bfloat16)
    own_lower = (own_mixed - own_upper.astype(jnp.float32)).astype(jnp.bfloat16)
    own_value = jnp.einsum(
        "hqc,chv->hqv", own_upper, value_maps, preferred_element_type=jnp.float32
    ) + jnp.einsum("hqc,chv->hqv", own_lower, value_maps, preferred_element_type=jnp.float32)
    old_part = (
        lax.dynamic_slice_in_dim(peak_hm, start_row, SPAN, 1),
        lax.dynamic_slice_in_dim(total_hm, start_row, SPAN, 1),
        lax.dynamic_slice_in_dim(value_out, start_row, SPAN, 1),
    )
    joint = merge_parts(old_part, (own_peak, own_total, own_value))
    peak_hm = lax.dynamic_update_slice_in_dim(peak_hm, joint[0], start_row, 1)
    total_hm = lax.dynamic_update_slice_in_dim(total_hm, joint[1], start_row, 1)
    value_out = lax.dynamic_update_slice_in_dim(value_out, joint[2], start_row, 1)

    stats = jnp.stack([peak_hm, total_hm], axis=0).astype(jnp.bfloat16)
    got_stats = lax.all_to_all(
        stats.reshape(2, heads_here, wide_count, tok_rows), "wide", 2, 2, tiled=True
    ).astype(jnp.float32)
    got_value = lax.all_to_all(
        value_out.astype(jnp.bfloat16).reshape(heads_here, wide_count, tok_rows, VDIM),
        "wide",
        1,
        1,
        tiled=True,
    ).astype(jnp.float32)
    got_peak = got_stats[0]
    got_total = got_stats[1]
    peak_value = jnp.max(got_peak, axis=1)
    factor = jnp.exp(got_peak - peak_value[:, None])
    denominator = jnp.sum(factor * got_total, axis=1)
    numerator = jnp.sum(factor[..., None] * got_value, axis=1)
    context = jnp.transpose(
        (numerator / denominator[..., None]).astype(jnp.bfloat16), (1, 0, 2)
    ).reshape(tok_rows, heads_here * VDIM)
    partial_out = jnp.einsum(
        "tk,wkc->twc", context, o_got, preferred_element_type=jnp.float32
    ).reshape(tok_rows, -1)
    out_cols = partial_out.shape[1]
    pieces = jnp.transpose(
        partial_out.astype(jnp.bfloat16).reshape(tok_rows, narrow_count, out_cols // narrow_count),
        (1, 0, 2),
    )
    got_pieces = lax.all_to_all(pieces, "narrow", 0, 0, tiled=True)
    mine = jnp.sum(got_pieces.astype(jnp.float32), axis=0).astype(jnp.bfloat16)
    all_pieces = gather_axis(mine, "narrow")
    return jnp.transpose(all_pieces, (1, 0, 2)).reshape(tok_rows, out_cols)


def solution(mesh):
    in_specs = (
        P("wide", None),
        P(),
        P("wide", "narrow"),
        P("wide", None),
        P(),
        P("wide", "narrow"),
        P("narrow", "wide"),
        P(None, "wide", None),
        P(),
    )
    out_specs = P("wide", None)
    return jax.shard_map(
        per_device, mesh=mesh, in_specs=in_specs, out_specs=out_specs, check_vma=False
    )
```

```python
import jax
import jax.numpy as jnp
from jax import lax
from jax.sharding import PartitionSpec as P
from jax.experimental import pallas as pl
from jax.experimental.pallas import tpu as pltpu

NOPE = 128
ROPE = 64
VDIM = 128
LAT = 512
SPAN = 512


eps = 1e-06
score_scale = 1.0 / 13.856406460551018


def rotate(values, positions):
    half_size = values.shape[-1] // 2
    frequency = 10000.0 ** (-jnp.arange(half_size, dtype=jnp.float32) / half_size)
    angles = positions.astype(jnp.float32)[..., None] * frequency
    lower_half = values[..., :half_size]
    upper_half = values[..., half_size:]
    cosine = jnp.cos(angles)
    sine_part = jnp.sin(angles)
    return jnp.concatenate(
        [
            lower_half * cosine - upper_half * sine_part,
            lower_half * sine_part + upper_half * cosine,
        ],
        axis=-1,
    )


def scaled_norm(values, gain):
    return (
        values
        * lax.rsqrt(jnp.mean(values * values, axis=-1, keepdims=True) + eps)
        * gain.astype(jnp.float32)
    )


def gather_axis(x, axis_name):
    count = lax.axis_size(axis_name)
    spread = jnp.broadcast_to(x[None], (count,) + x.shape)
    return lax.all_to_all(spread, axis_name, split_axis=0, concat_axis=0, tiled=True)


def absorb(nope_part, key_maps):
    return jnp.einsum(
        "thc,lhc->thl", nope_part, key_maps, preferred_element_type=jnp.float32
    ).astype(jnp.bfloat16)


def project_values(mixed, value_maps):
    upper_part = mixed.astype(jnp.bfloat16)
    lower_part = (mixed - upper_part.astype(jnp.float32)).astype(jnp.bfloat16)
    first_term = jnp.einsum(
        "qhc,chv->qhv", upper_part, value_maps, preferred_element_type=jnp.float32
    )
    second_term = jnp.einsum(
        "qhc,chv->qhv", lower_part, value_maps, preferred_element_type=jnp.float32
    )
    return first_term + second_term


def attend(block_queries, key_rows, live_mask, value_maps):
    scores = (
        jnp.einsum("qhc,kc->qhk", block_queries, key_rows, preferred_element_type=jnp.float32)
        * score_scale
    )
    live_rows = live_mask[:, None, :]
    row_peak = jnp.max(jnp.where(live_rows, scores, -1e30), axis=-1)
    weights = jnp.where(live_rows, jnp.exp(scores - row_peak[..., None]), 0.0)
    row_total = jnp.sum(weights, axis=-1)
    mixed = jnp.einsum(
        "qhk,kc->qhc",
        weights.astype(jnp.bfloat16),
        key_rows[:, :LAT],
        preferred_element_type=jnp.float32,
    )
    return (row_peak, row_total, project_values(mixed, value_maps))


def skipped(block_queries, key_rows, live_mask, value_maps):
    rows_here = block_queries.shape[0]
    heads_here = block_queries.shape[1]
    return (
        jnp.full((rows_here, heads_here), -1e30, jnp.float32),
        jnp.zeros((rows_here, heads_here), jnp.float32),
        jnp.zeros((rows_here, heads_here, value_maps.shape[2]), jnp.float32),
    )


def cache_kernel(lens_ref, base_ref, lat_ref, rope_ref, kv_ref, vm_ref, peak_ref, total_ref, value_ref):
    length_now = lens_ref[pl.program_id(0)]
    base = base_ref[0]
    live_block = base < length_now

    @pl.when(live_block)
    def _():
        keys = kv_ref[0]
        key_lat = keys[:, :LAT]
        key_rope = keys[:, LAT:]
        nt = (((1,), (1,)), ((), ()))
        scores = (
            lax.dot_general(lat_ref[0], key_lat, nt, preferred_element_type=jnp.float32)
            + lax.dot_general(rope_ref[0], key_rope, nt, preferred_element_type=jnp.float32)
        ) * score_scale
        slots = base + lax.broadcasted_iota(jnp.int32, scores.shape, 1)
        live = slots < length_now
        peak = jnp.max(jnp.where(live, scores, -1e30), axis=-1, keepdims=True)
        weights = jnp.where(live, jnp.exp(scores - peak), 0.0)
        peak_ref[0] = peak
        total_ref[0] = jnp.sum(weights, axis=-1, keepdims=True)
        mixed = jnp.dot(weights.astype(jnp.bfloat16), key_lat, preferred_element_type=jnp.float32)
        value_map = vm_ref[0]
        upper_part = mixed.astype(jnp.bfloat16)
        lower_part = (mixed - upper_part.astype(jnp.float32)).astype(jnp.bfloat16)
        value_ref[0] = jnp.dot(upper_part, value_map, preferred_element_type=jnp.float32) + jnp.dot(
            lower_part, value_map, preferred_element_type=jnp.float32
        )

    @pl.when(jnp.logical_not(live_block))
    def _():
        peak_ref[...] = jnp.full(peak_ref.shape, -1e30, jnp.float32)
        total_ref[...] = jnp.zeros(total_ref.shape, jnp.float32)
        value_ref[...] = jnp.zeros(value_ref.shape, jnp.float32)


def cache_attention(lengths, base, lat_hm, rope_hm, cache, value_hm):
    heads_here, total_tokens, _ = lat_hm.shape
    requests, cache_rows, width = cache.shape
    span = total_tokens // requests
    vdim = value_hm.shape[2]
    grid_spec = pltpu.PrefetchScalarGridSpec(
        num_scalar_prefetch=2,
        grid=(requests, heads_here),
        in_specs=[
            pl.BlockSpec((1, span, LAT), lambda r, h, lens, b: (h, r, 0)),
            pl.BlockSpec((1, span, ROPE), lambda r, h, lens, b: (h, r, 0)),
            pl.BlockSpec((1, cache_rows, width), lambda r, h, lens, b: (r, 0, 0)),
            pl.BlockSpec((1, LAT, vdim), lambda r, h, lens, b: (h, 0, 0)),
        ],
        out_specs=[
            pl.BlockSpec((1, span, 1), lambda r, h, lens, b: (h, r, 0)),
            pl.BlockSpec((1, span, 1), lambda r, h, lens, b: (h, r, 0)),
            pl.BlockSpec((1, span, vdim), lambda r, h, lens, b: (h, r, 0)),
        ],
    )
    return pl.pallas_call(
        cache_kernel,
        grid_spec=grid_spec,
        out_shape=[
            jax.ShapeDtypeStruct((heads_here, total_tokens, 1), jnp.float32),
            jax.ShapeDtypeStruct((heads_here, total_tokens, 1), jnp.float32),
            jax.ShapeDtypeStruct((heads_here, total_tokens, vdim), jnp.float32),
        ],
        compiler_params=pltpu.CompilerParams(dimension_semantics=("arbitrary", "arbitrary")),
    )(lengths, base, lat_hm, rope_hm, cache, value_hm)


def merge_parts(first, second):
    joint_peak = jnp.maximum(first[0], second[0])
    first_factor = jnp.exp(first[0] - joint_peak)
    second_factor = jnp.exp(second[0] - joint_peak)
    joint_total = first_factor * first[1] + second_factor * second[1]
    joint_value = first_factor[..., None] * first[2] + second_factor[..., None] * second[2]
    return (joint_peak, joint_total, joint_value)


def per_device(
    hidden, attn_gain, q_weight, kva_weight, kv_gain, kvb_weight, o_weight, cache, lengths
):
    wide_count = lax.axis_size("wide")
    wide_place = lax.axis_index("wide")
    tok_rows = hidden.shape[0]
    requests = lengths.shape[0]
    cache_rows = cache.shape[1]
    heads_here = q_weight.shape[1] // (NOPE + ROPE)
    narrow_count = lax.axis_size("narrow")
    narrow_place = lax.axis_index("narrow")
    q_cols = q_weight.shape[1]
    kva_cols = kva_weight.shape[1]
    kva_part = kva_cols // narrow_count
    kva_mine = lax.dynamic_slice_in_dim(kva_weight, narrow_place * kva_part, kva_part, 1)
    packed = jnp.concatenate([q_weight, kva_mine], axis=1)
    got_weights = gather_axis(packed, "wide")
    proj_full = got_weights.reshape(-1, q_cols + kva_part)
    kvb_rows, kvb_cols = kvb_weight.shape
    o_rows, o_cols = o_weight.shape
    late = jnp.concatenate([kvb_weight, o_weight.reshape(-1, kvb_cols)], axis=0)
    late_got = lax.all_gather(late, "wide", axis=0, tiled=False)
    kvb_full = late_got[:, :kvb_rows].reshape(-1, kvb_cols)
    o_got = late_got[:, kvb_rows:].reshape(wide_count, o_rows, o_cols)

    normed = scaled_norm(hidden.astype(jnp.float32), attn_gain).astype(jnp.bfloat16)
    projected = jnp.dot(normed, proj_full, preferred_element_type=jnp.float32)
    query_rows = projected[:, :q_cols].astype(jnp.bfloat16)
    compressed_part = projected[:, q_cols:]
    compressed = jnp.transpose(gather_axis(compressed_part, "narrow"), (1, 0, 2)).reshape(
        tok_rows, kva_cols
    )
    first_token = wide_place * tok_rows
    token_ids = first_token + jnp.arange(tok_rows, dtype=jnp.int32)
    positions = lengths[token_ids // SPAN] + token_ids % SPAN
    own_keys = jnp.concatenate(
        [
            scaled_norm(compressed[:, :LAT], kv_gain).astype(jnp.bfloat16),
            rotate(compressed[:, LAT:], positions).astype(jnp.bfloat16),
        ],
        axis=1,
    )

    query_heads = query_rows.reshape(tok_rows, heads_here, NOPE + ROPE)
    outgoing = jnp.concatenate(
        [
            query_heads[..., :NOPE].reshape(tok_rows, heads_here * NOPE),
            query_heads[..., NOPE:].reshape(tok_rows, heads_here * ROPE),
        ],
        axis=1,
    )
    raw_all = gather_axis(outgoing, "wide")
    total_tokens = raw_all.shape[0] * tok_rows
    raw_all = raw_all.reshape(total_tokens, heads_here * (NOPE + ROPE))
    all_ids = jnp.arange(total_tokens, dtype=jnp.int32)
    all_positions = lengths[all_ids // SPAN] + all_ids % SPAN
    kvb_heads = kvb_full.reshape(LAT, heads_here, NOPE + VDIM)
    key_maps = kvb_heads[..., :NOPE]
    value_maps = kvb_heads[..., NOPE:]
    nope_all = raw_all[:, : heads_here * NOPE].reshape(total_tokens, heads_here, NOPE)
    rope_all = raw_all[:, heads_here * NOPE :].reshape(total_tokens, heads_here, ROPE)
    q_rope = rotate(rope_all.astype(jnp.float32), all_positions[:, None]).astype(jnp.bfloat16)
    lat_hm = jnp.einsum(
        "thc,lhc->htl", nope_all, key_maps, preferred_element_type=jnp.float32
    ).astype(jnp.bfloat16)
    rope_hm = jnp.transpose(q_rope, (1, 0, 2))
    value_hm = jnp.transpose(value_maps, (1, 0, 2))

    base = (wide_place * cache_rows).reshape(1).astype(jnp.int32)
    peak_hm, total_hm, value_out = cache_attention(lengths, base, lat_hm, rope_hm, cache, value_hm)
    peak_hm = peak_hm[..., 0]
    total_hm = total_hm[..., 0]

    own_request = first_token // SPAN
    start_row = own_request * SPAN
    own_slots = first_token % SPAN + jnp.arange(tok_rows, dtype=jnp.int32)
    causal = own_slots[None, :] <= jnp.arange(SPAN, dtype=jnp.int32)[:, None]
    own_lat = lax.dynamic_slice_in_dim(lat_hm, start_row, SPAN, 1)
    own_rope = lax.dynamic_slice_in_dim(rope_hm, start_row, SPAN, 1)
    own_scores = (
        jnp.einsum("hqc,kc->hqk", own_lat, own_keys[:, :LAT], preferred_element_type=jnp.float32)
        + jnp.einsum("hqc,kc->hqk", own_rope, own_keys[:, LAT:], preferred_element_type=jnp.float32)
    ) * score_scale
    own_live = causal[None]
    own_peak = jnp.max(jnp.where(own_live, own_scores, -1e30), axis=-1)
    own_weights = jnp.where(own_live, jnp.exp(own_scores - own_peak[..., None]), 0.0)
    own_total = jnp.sum(own_weights, axis=-1)
    own_mixed = jnp.einsum(
        "hqk,kc->hqc", own_weights.astype(jnp.bfloat16), own_keys[:, :LAT],
        preferred_element_type=jnp.float32,
    )
    own_upper = own_mixed.astype(jnp.bfloat16)
    own_lower = (own_mixed - own_upper.astype(jnp.float32)).astype(jnp.bfloat16)
    own_value = jnp.einsum(
        "hqc,hcv->hqv", own_upper, value_hm, preferred_element_type=jnp.float32
    ) + jnp.einsum("hqc,hcv->hqv", own_lower, value_hm, preferred_element_type=jnp.float32)
    old_part = (
        lax.dynamic_slice_in_dim(peak_hm, start_row, SPAN, 1),
        lax.dynamic_slice_in_dim(total_hm, start_row, SPAN, 1),
        lax.dynamic_slice_in_dim(value_out, start_row, SPAN, 1),
    )
    joint = merge_parts(old_part, (own_peak, own_total, own_value))
    peak_hm = lax.dynamic_update_slice_in_dim(peak_hm, joint[0], start_row, 1)
    total_hm = lax.dynamic_update_slice_in_dim(total_hm, joint[1], start_row, 1)
    value_out = lax.dynamic_update_slice_in_dim(value_out, joint[2], start_row, 1)

    stats = jnp.stack([peak_hm, total_hm], axis=0).astype(jnp.bfloat16)
    got_stats = lax.all_to_all(
        stats.reshape(2, heads_here, wide_count, tok_rows), "wide", 2, 2, tiled=True
    ).astype(jnp.float32)
    got_value = lax.all_to_all(
        value_out.astype(jnp.bfloat16).reshape(heads_here, wide_count, tok_rows, VDIM),
        "wide",
        1,
        1,
        tiled=True,
    ).astype(jnp.float32)
    got_peak = got_stats[0]
    got_total = got_stats[1]
    peak_value = jnp.max(got_peak, axis=1)
    factor = jnp.exp(got_peak - peak_value[:, None])
    denominator = jnp.sum(factor * got_total, axis=1)
    numerator = jnp.sum(factor[..., None] * got_value, axis=1)
    context = jnp.transpose(
        (numerator / denominator[..., None]).astype(jnp.bfloat16), (1, 0, 2)
    ).reshape(tok_rows, heads_here * VDIM)
    partial_out = jnp.einsum(
        "tk,wkc->twc", context, o_got, preferred_element_type=jnp.float32
    ).reshape(tok_rows, -1)
    out_cols = partial_out.shape[1]
    pieces = jnp.transpose(
        partial_out.astype(jnp.bfloat16).reshape(tok_rows, narrow_count, out_cols // narrow_count),
        (1, 0, 2),
    )
    got_pieces = lax.all_to_all(pieces, "narrow", 0, 0, tiled=True)
    mine = jnp.sum(got_pieces.astype(jnp.float32), axis=0).astype(jnp.bfloat16)
    all_pieces = gather_axis(mine, "narrow")
    return jnp.transpose(all_pieces, (1, 0, 2)).reshape(tok_rows, out_cols)


def solution(mesh):
    in_specs = (
        P("wide", None),
        P(),
        P("wide", "narrow"),
        P("wide", None),
        P(),
        P("wide", "narrow"),
        P("narrow", "wide"),
        P(None, "wide", None),
        P(),
    )
    out_specs = P("wide", None)
    return jax.shard_map(
        per_device, mesh=mesh, in_specs=in_specs, out_specs=out_specs, check_vma=False
    )
```

```python
import jax
import jax.numpy as jnp
from jax import lax
from jax.sharding import PartitionSpec as P
from jax.experimental import pallas as pl
from jax.experimental.pallas import tpu as pltpu

NOPE = 128
ROPE = 64
VDIM = 128
LAT = 512
SPAN = 512


eps = 1e-06
score_scale = 1.0 / 13.856406460551018


def rotate(values, positions):
    half_size = values.shape[-1] // 2
    frequency = 10000.0 ** (-jnp.arange(half_size, dtype=jnp.float32) / half_size)
    angles = positions.astype(jnp.float32)[..., None] * frequency
    lower_half = values[..., :half_size]
    upper_half = values[..., half_size:]
    cosine = jnp.cos(angles)
    sine_part = jnp.sin(angles)
    return jnp.concatenate(
        [
            lower_half * cosine - upper_half * sine_part,
            lower_half * sine_part + upper_half * cosine,
        ],
        axis=-1,
    )


def scaled_norm(values, gain):
    return (
        values
        * lax.rsqrt(jnp.mean(values * values, axis=-1, keepdims=True) + eps)
        * gain.astype(jnp.float32)
    )


def gather_axis(x, axis_name):
    count = lax.axis_size(axis_name)
    spread = jnp.broadcast_to(x[None], (count,) + x.shape)
    return lax.all_to_all(spread, axis_name, split_axis=0, concat_axis=0, tiled=True)


def absorb(nope_part, key_maps):
    return jnp.einsum(
        "thc,lhc->thl", nope_part, key_maps, preferred_element_type=jnp.float32
    ).astype(jnp.bfloat16)


def project_values(mixed, value_maps):
    upper_part = mixed.astype(jnp.bfloat16)
    lower_part = (mixed - upper_part.astype(jnp.float32)).astype(jnp.bfloat16)
    first_term = jnp.einsum(
        "qhc,chv->qhv", upper_part, value_maps, preferred_element_type=jnp.float32
    )
    second_term = jnp.einsum(
        "qhc,chv->qhv", lower_part, value_maps, preferred_element_type=jnp.float32
    )
    return first_term + second_term


def attend(block_queries, key_rows, live_mask, value_maps):
    scores = (
        jnp.einsum("qhc,kc->qhk", block_queries, key_rows, preferred_element_type=jnp.float32)
        * score_scale
    )
    live_rows = live_mask[:, None, :]
    row_peak = jnp.max(jnp.where(live_rows, scores, -1e30), axis=-1)
    weights = jnp.where(live_rows, jnp.exp(scores - row_peak[..., None]), 0.0)
    row_total = jnp.sum(weights, axis=-1)
    mixed = jnp.einsum(
        "qhk,kc->qhc",
        weights.astype(jnp.bfloat16),
        key_rows[:, :LAT],
        preferred_element_type=jnp.float32,
    )
    return (row_peak, row_total, project_values(mixed, value_maps))


def skipped(block_queries, key_rows, live_mask, value_maps):
    rows_here = block_queries.shape[0]
    heads_here = block_queries.shape[1]
    return (
        jnp.full((rows_here, heads_here), -1e30, jnp.float32),
        jnp.zeros((rows_here, heads_here), jnp.float32),
        jnp.zeros((rows_here, heads_here, value_maps.shape[2]), jnp.float32),
    )


def cache_kernel(lens_ref, base_ref, lat_ref, rope_ref, kv_ref, vm_ref, peak_ref, total_ref, value_ref):
    length_now = lens_ref[pl.program_id(0)]
    base = base_ref[0]
    live_block = base < length_now

    @pl.when(live_block)
    def _():
        keys = kv_ref[0]
        key_lat = keys[:, :LAT]
        key_rope = keys[:, LAT:]
        nt = (((1,), (1,)), ((), ()))
        scores = (
            lax.dot_general(lat_ref[0], key_lat, nt, preferred_element_type=jnp.float32)
            + lax.dot_general(rope_ref[0], key_rope, nt, preferred_element_type=jnp.float32)
        ) * score_scale
        slots = base + lax.broadcasted_iota(jnp.int32, scores.shape, 1)
        live = slots < length_now
        peak = jnp.max(jnp.where(live, scores, -1e30), axis=-1, keepdims=True)
        weights = jnp.where(live, jnp.exp(scores - peak), 0.0)
        peak_ref[0] = peak
        total_ref[0] = jnp.sum(weights, axis=-1, keepdims=True)
        mixed = jnp.dot(weights.astype(jnp.bfloat16), key_lat, preferred_element_type=jnp.float32)
        value_map = vm_ref[0]
        upper_part = mixed.astype(jnp.bfloat16)
        lower_part = (mixed - upper_part.astype(jnp.float32)).astype(jnp.bfloat16)
        value_ref[0] = jnp.dot(upper_part, value_map, preferred_element_type=jnp.float32) + jnp.dot(
            lower_part, value_map, preferred_element_type=jnp.float32
        )

    @pl.when(jnp.logical_not(live_block))
    def _():
        peak_ref[...] = jnp.full(peak_ref.shape, -1e30, jnp.float32)
        total_ref[...] = jnp.zeros(total_ref.shape, jnp.float32)
        value_ref[...] = jnp.zeros(value_ref.shape, jnp.float32)


def cache_attention(lengths, base, lat_hm, rope_hm, cache, value_hm):
    heads_here, total_tokens, _ = lat_hm.shape
    requests, cache_rows, width = cache.shape
    span = total_tokens // requests
    vdim = value_hm.shape[2]
    grid_spec = pltpu.PrefetchScalarGridSpec(
        num_scalar_prefetch=2,
        grid=(requests, heads_here),
        in_specs=[
            pl.BlockSpec((1, span, LAT), lambda r, h, lens, b: (h, r, 0)),
            pl.BlockSpec((1, span, ROPE), lambda r, h, lens, b: (h, r, 0)),
            pl.BlockSpec((1, cache_rows, width), lambda r, h, lens, b: (r, 0, 0)),
            pl.BlockSpec((1, LAT, vdim), lambda r, h, lens, b: (h, 0, 0)),
        ],
        out_specs=[
            pl.BlockSpec((1, span, 1), lambda r, h, lens, b: (h, r, 0)),
            pl.BlockSpec((1, span, 1), lambda r, h, lens, b: (h, r, 0)),
            pl.BlockSpec((1, span, vdim), lambda r, h, lens, b: (h, r, 0)),
        ],
    )
    return pl.pallas_call(
        cache_kernel,
        grid_spec=grid_spec,
        out_shape=[
            jax.ShapeDtypeStruct((heads_here, total_tokens, 1), jnp.float32),
            jax.ShapeDtypeStruct((heads_here, total_tokens, 1), jnp.float32),
            jax.ShapeDtypeStruct((heads_here, total_tokens, vdim), jnp.float32),
        ],
        compiler_params=pltpu.CompilerParams(dimension_semantics=("arbitrary", "arbitrary")),
    )(lengths, base, lat_hm, rope_hm, cache, value_hm)


def merge_parts(first, second):
    joint_peak = jnp.maximum(first[0], second[0])
    first_factor = jnp.exp(first[0] - joint_peak)
    second_factor = jnp.exp(second[0] - joint_peak)
    joint_total = first_factor * first[1] + second_factor * second[1]
    joint_value = first_factor[..., None] * first[2] + second_factor[..., None] * second[2]
    return (joint_peak, joint_total, joint_value)


def per_device(
    hidden, attn_gain, q_weight, kva_weight, kv_gain, kvb_weight, o_weight, cache, lengths
):
    wide_count = lax.axis_size("wide")
    wide_place = lax.axis_index("wide")
    tok_rows = hidden.shape[0]
    requests = lengths.shape[0]
    cache_rows = cache.shape[1]
    heads_here = q_weight.shape[1] // (NOPE + ROPE)
    narrow_count = lax.axis_size("narrow")
    narrow_place = lax.axis_index("narrow")
    q_cols = q_weight.shape[1]
    kva_cols = kva_weight.shape[1]
    kva_part = kva_cols // narrow_count
    kva_mine = lax.dynamic_slice_in_dim(kva_weight, narrow_place * kva_part, kva_part, 1)
    packed = jnp.concatenate([q_weight, kva_mine], axis=1)
    got_weights = gather_axis(packed, "wide")
    proj_full = got_weights.reshape(-1, q_cols + kva_part)
    kvb_full = gather_axis(kvb_weight, "wide").reshape(-1, kvb_weight.shape[1])
    o_got = lax.all_gather(o_weight, "wide", axis=0, tiled=False)

    normed = scaled_norm(hidden.astype(jnp.float32), attn_gain).astype(jnp.bfloat16)
    projected = jnp.dot(normed, proj_full, preferred_element_type=jnp.float32)
    query_rows = projected[:, :q_cols].astype(jnp.bfloat16)
    compressed_part = projected[:, q_cols:]
    compressed = jnp.transpose(gather_axis(compressed_part, "narrow"), (1, 0, 2)).reshape(
        tok_rows, kva_cols
    )
    first_token = wide_place * tok_rows
    token_ids = first_token + jnp.arange(tok_rows, dtype=jnp.int32)
    positions = lengths[token_ids // SPAN] + token_ids % SPAN
    own_keys = jnp.concatenate(
        [
            scaled_norm(compressed[:, :LAT], kv_gain).astype(jnp.bfloat16),
            rotate(compressed[:, LAT:], positions).astype(jnp.bfloat16),
        ],
        axis=1,
    )

    query_heads = query_rows.reshape(tok_rows, heads_here, NOPE + ROPE)
    outgoing = jnp.concatenate(
        [
            query_heads[..., :NOPE].reshape(tok_rows, heads_here * NOPE),
            query_heads[..., NOPE:].reshape(tok_rows, heads_here * ROPE),
        ],
        axis=1,
    )
    raw_all = gather_axis(outgoing, "wide")
    total_tokens = raw_all.shape[0] * tok_rows
    raw_all = raw_all.reshape(total_tokens, heads_here * (NOPE + ROPE))
    all_ids = jnp.arange(total_tokens, dtype=jnp.int32)
    all_positions = lengths[all_ids // SPAN] + all_ids % SPAN
    kvb_heads = kvb_full.reshape(LAT, heads_here, NOPE + VDIM)
    key_maps = kvb_heads[..., :NOPE]
    value_maps = kvb_heads[..., NOPE:]
    nope_all = raw_all[:, : heads_here * NOPE].reshape(total_tokens, heads_here, NOPE)
    rope_all = raw_all[:, heads_here * NOPE :].reshape(total_tokens, heads_here, ROPE)
    q_rope = rotate(rope_all.astype(jnp.float32), all_positions[:, None]).astype(jnp.bfloat16)
    lat_hm = jnp.einsum(
        "thc,lhc->htl", nope_all, key_maps, preferred_element_type=jnp.float32
    ).astype(jnp.bfloat16)
    rope_hm = jnp.transpose(q_rope, (1, 0, 2))
    value_hm = jnp.transpose(value_maps, (1, 0, 2))

    base = (wide_place * cache_rows).reshape(1).astype(jnp.int32)
    peak_hm, total_hm, value_out = cache_attention(lengths, base, lat_hm, rope_hm, cache, value_hm)
    peak_hm = peak_hm[..., 0]
    total_hm = total_hm[..., 0]

    own_request = first_token // SPAN
    start_row = own_request * SPAN
    own_slots = first_token % SPAN + jnp.arange(tok_rows, dtype=jnp.int32)
    causal = own_slots[None, :] <= jnp.arange(SPAN, dtype=jnp.int32)[:, None]
    own_lat = lax.dynamic_slice_in_dim(lat_hm, start_row, SPAN, 1)
    own_rope = lax.dynamic_slice_in_dim(rope_hm, start_row, SPAN, 1)
    own_scores = (
        jnp.einsum("hqc,kc->hqk", own_lat, own_keys[:, :LAT], preferred_element_type=jnp.float32)
        + jnp.einsum("hqc,kc->hqk", own_rope, own_keys[:, LAT:], preferred_element_type=jnp.float32)
    ) * score_scale
    own_live = causal[None]
    own_peak = jnp.max(jnp.where(own_live, own_scores, -1e30), axis=-1)
    own_weights = jnp.where(own_live, jnp.exp(own_scores - own_peak[..., None]), 0.0)
    own_total = jnp.sum(own_weights, axis=-1)
    own_mixed = jnp.einsum(
        "hqk,kc->hqc", own_weights.astype(jnp.bfloat16), own_keys[:, :LAT],
        preferred_element_type=jnp.float32,
    )
    own_upper = own_mixed.astype(jnp.bfloat16)
    own_lower = (own_mixed - own_upper.astype(jnp.float32)).astype(jnp.bfloat16)
    own_value = jnp.einsum(
        "hqc,hcv->hqv", own_upper, value_hm, preferred_element_type=jnp.float32
    ) + jnp.einsum("hqc,hcv->hqv", own_lower, value_hm, preferred_element_type=jnp.float32)
    old_part = (
        lax.dynamic_slice_in_dim(peak_hm, start_row, SPAN, 1),
        lax.dynamic_slice_in_dim(total_hm, start_row, SPAN, 1),
        lax.dynamic_slice_in_dim(value_out, start_row, SPAN, 1),
    )
    joint = merge_parts(old_part, (own_peak, own_total, own_value))
    peak_hm = lax.dynamic_update_slice_in_dim(peak_hm, joint[0], start_row, 1)
    total_hm = lax.dynamic_update_slice_in_dim(total_hm, joint[1], start_row, 1)
    value_out = lax.dynamic_update_slice_in_dim(value_out, joint[2], start_row, 1)

    stats = jnp.stack([peak_hm, total_hm], axis=0).astype(jnp.bfloat16)
    got_stats = lax.all_to_all(
        stats.reshape(2, heads_here, wide_count, tok_rows), "wide", 2, 2, tiled=True
    ).astype(jnp.float32)
    got_value = lax.all_to_all(
        value_out.astype(jnp.bfloat16).reshape(heads_here, wide_count, tok_rows, VDIM),
        "wide",
        1,
        1,
        tiled=True,
    ).astype(jnp.float32)
    got_peak = got_stats[0]
    got_total = got_stats[1]
    peak_value = jnp.max(got_peak, axis=1)
    factor = jnp.exp(got_peak - peak_value[:, None])
    denominator = jnp.sum(factor * got_total, axis=1)
    numerator = jnp.sum(factor[..., None] * got_value, axis=1)
    context = jnp.transpose(
        (numerator / denominator[..., None]).astype(jnp.bfloat16), (1, 0, 2)
    ).reshape(tok_rows, heads_here * VDIM)
    partial_out = jnp.einsum(
        "tk,wkc->twc", context, o_got, preferred_element_type=jnp.float32
    ).reshape(tok_rows, -1)
    out_cols = partial_out.shape[1]
    pieces = jnp.transpose(
        partial_out.astype(jnp.bfloat16).reshape(tok_rows, narrow_count, out_cols // narrow_count),
        (1, 0, 2),
    )
    got_pieces = lax.all_to_all(pieces, "narrow", 0, 0, tiled=True)
    mine = jnp.sum(got_pieces.astype(jnp.float32), axis=0).astype(jnp.bfloat16)
    all_pieces = gather_axis(mine, "narrow")
    return jnp.transpose(all_pieces, (1, 0, 2)).reshape(tok_rows, out_cols)


def solution(mesh):
    in_specs = (
        P("wide", None),
        P(),
        P("wide", "narrow"),
        P("wide", None),
        P(),
        P("wide", "narrow"),
        P("narrow", "wide"),
        P(None, "wide", None),
        P(),
    )
    out_specs = P("wide", None)
    return jax.shard_map(
        per_device, mesh=mesh, in_specs=in_specs, out_specs=out_specs, check_vma=False
    )
```

```python
import jax
import jax.numpy as jnp
from jax import lax
from jax.sharding import PartitionSpec as P
from jax.experimental import pallas as pl
from jax.experimental.pallas import tpu as pltpu

NOPE = 128
ROPE = 64
VDIM = 128
LAT = 512
SPAN = 512


eps = 1e-06
score_scale = 1.0 / 13.856406460551018


def rotate(values, positions):
    half_size = values.shape[-1] // 2
    frequency = 10000.0 ** (-jnp.arange(half_size, dtype=jnp.float32) / half_size)
    angles = positions.astype(jnp.float32)[..., None] * frequency
    lower_half = values[..., :half_size]
    upper_half = values[..., half_size:]
    cosine = jnp.cos(angles)
    sine_part = jnp.sin(angles)
    return jnp.concatenate(
        [
            lower_half * cosine - upper_half * sine_part,
            lower_half * sine_part + upper_half * cosine,
        ],
        axis=-1,
    )


def scaled_norm(values, gain):
    return (
        values
        * lax.rsqrt(jnp.mean(values * values, axis=-1, keepdims=True) + eps)
        * gain.astype(jnp.float32)
    )


def gather_axis(x, axis_name):
    count = lax.axis_size(axis_name)
    spread = jnp.broadcast_to(x[None], (count,) + x.shape)
    return lax.all_to_all(spread, axis_name, split_axis=0, concat_axis=0, tiled=True)


def absorb(nope_part, key_maps):
    return jnp.einsum(
        "thc,lhc->thl", nope_part, key_maps, preferred_element_type=jnp.float32
    ).astype(jnp.bfloat16)


def project_values(mixed, value_maps):
    upper_part = mixed.astype(jnp.bfloat16)
    lower_part = (mixed - upper_part.astype(jnp.float32)).astype(jnp.bfloat16)
    first_term = jnp.einsum(
        "qhc,chv->qhv", upper_part, value_maps, preferred_element_type=jnp.float32
    )
    second_term = jnp.einsum(
        "qhc,chv->qhv", lower_part, value_maps, preferred_element_type=jnp.float32
    )
    return first_term + second_term


def attend(block_queries, key_rows, live_mask, value_maps):
    scores = (
        jnp.einsum("qhc,kc->qhk", block_queries, key_rows, preferred_element_type=jnp.float32)
        * score_scale
    )
    live_rows = live_mask[:, None, :]
    row_peak = jnp.max(jnp.where(live_rows, scores, -1e30), axis=-1)
    weights = jnp.where(live_rows, jnp.exp(scores - row_peak[..., None]), 0.0)
    row_total = jnp.sum(weights, axis=-1)
    mixed = jnp.einsum(
        "qhk,kc->qhc",
        weights.astype(jnp.bfloat16),
        key_rows[:, :LAT],
        preferred_element_type=jnp.float32,
    )
    return (row_peak, row_total, project_values(mixed, value_maps))


def skipped(block_queries, key_rows, live_mask, value_maps):
    rows_here = block_queries.shape[0]
    heads_here = block_queries.shape[1]
    return (
        jnp.full((rows_here, heads_here), -1e30, jnp.float32),
        jnp.zeros((rows_here, heads_here), jnp.float32),
        jnp.zeros((rows_here, heads_here, value_maps.shape[2]), jnp.float32),
    )


def cache_kernel(lens_ref, base_ref, lat_ref, rope_ref, kv_ref, vm_ref, stats_ref, value_ref):
    length_now = lens_ref[pl.program_id(0)]
    base = base_ref[0]
    live_block = base < length_now

    @pl.when(live_block)
    def _():
        keys = kv_ref[0]
        key_lat = keys[:, :LAT]
        key_rope = keys[:, LAT:]
        nt = (((1,), (1,)), ((), ()))
        scores = (
            lax.dot_general(lat_ref[0], key_lat, nt, preferred_element_type=jnp.float32)
            + lax.dot_general(rope_ref[0], key_rope, nt, preferred_element_type=jnp.float32)
        ) * score_scale
        slots = base + lax.broadcasted_iota(jnp.int32, scores.shape, 1)
        live = slots < length_now
        peak = jnp.max(jnp.where(live, scores, -1e30), axis=-1, keepdims=True)
        weights = jnp.where(live, jnp.exp(scores - peak), 0.0)
        total = jnp.sum(weights, axis=-1, keepdims=True)
        lane = lax.broadcasted_iota(jnp.int32, stats_ref.shape[1:], 1)
        stats_ref[0] = jnp.where(lane == 0, peak, total)
        mixed = jnp.dot(weights.astype(jnp.bfloat16), key_lat, preferred_element_type=jnp.float32)
        value_map = vm_ref[0]
        upper_part = mixed.astype(jnp.bfloat16)
        lower_part = (mixed - upper_part.astype(jnp.float32)).astype(jnp.bfloat16)
        value_ref[0] = jnp.dot(upper_part, value_map, preferred_element_type=jnp.float32) + jnp.dot(
            lower_part, value_map, preferred_element_type=jnp.float32
        )

    @pl.when(jnp.logical_not(live_block))
    def _():
        lane = lax.broadcasted_iota(jnp.int32, stats_ref.shape, 2)
        stats_ref[...] = jnp.where(lane == 0, -1e30, 0.0).astype(jnp.float32)
        value_ref[...] = jnp.zeros(value_ref.shape, jnp.float32)


def cache_attention(lengths, base, lat_hm, rope_hm, cache, value_hm):
    heads_here, total_tokens, _ = lat_hm.shape
    requests, cache_rows, width = cache.shape
    span = total_tokens // requests
    vdim = value_hm.shape[2]
    grid_spec = pltpu.PrefetchScalarGridSpec(
        num_scalar_prefetch=2,
        grid=(requests, heads_here),
        in_specs=[
            pl.BlockSpec((1, span, LAT), lambda r, h, lens, b: (h, r, 0)),
            pl.BlockSpec((1, span, ROPE), lambda r, h, lens, b: (h, r, 0)),
            pl.BlockSpec((1, cache_rows, width), lambda r, h, lens, b: (r, 0, 0)),
            pl.BlockSpec((1, LAT, vdim), lambda r, h, lens, b: (h, 0, 0)),
        ],
        out_specs=[
            pl.BlockSpec((1, span, 128), lambda r, h, lens, b: (h, r, 0)),
            pl.BlockSpec((1, span, vdim), lambda r, h, lens, b: (h, r, 0)),
        ],
    )
    return pl.pallas_call(
        cache_kernel,
        grid_spec=grid_spec,
        out_shape=[
            jax.ShapeDtypeStruct((heads_here, total_tokens, 128), jnp.float32),
            jax.ShapeDtypeStruct((heads_here, total_tokens, vdim), jnp.float32),
        ],
        compiler_params=pltpu.CompilerParams(dimension_semantics=("arbitrary", "arbitrary")),
    )(lengths, base, lat_hm, rope_hm, cache, value_hm)


def merge_parts(first, second):
    joint_peak = jnp.maximum(first[0], second[0])
    first_factor = jnp.exp(first[0] - joint_peak)
    second_factor = jnp.exp(second[0] - joint_peak)
    joint_total = first_factor * first[1] + second_factor * second[1]
    joint_value = first_factor[..., None] * first[2] + second_factor[..., None] * second[2]
    return (joint_peak, joint_total, joint_value)


def per_device(
    hidden, attn_gain, q_weight, kva_weight, kv_gain, kvb_weight, o_weight, cache, lengths
):
    wide_count = lax.axis_size("wide")
    wide_place = lax.axis_index("wide")
    tok_rows = hidden.shape[0]
    requests = lengths.shape[0]
    cache_rows = cache.shape[1]
    heads_here = q_weight.shape[1] // (NOPE + ROPE)
    narrow_count = lax.axis_size("narrow")
    narrow_place = lax.axis_index("narrow")
    q_cols = q_weight.shape[1]
    kva_cols = kva_weight.shape[1]
    kva_part = kva_cols // narrow_count
    kva_mine = lax.dynamic_slice_in_dim(kva_weight, narrow_place * kva_part, kva_part, 1)
    packed = jnp.concatenate([q_weight, kva_mine], axis=1)
    got_weights = gather_axis(packed, "wide")
    proj_full = got_weights.reshape(-1, q_cols + kva_part)
    kvb_full = gather_axis(kvb_weight, "wide").reshape(-1, kvb_weight.shape[1])
    o_got = lax.all_gather(o_weight, "wide", axis=0, tiled=False)

    normed = scaled_norm(hidden.astype(jnp.float32), attn_gain).astype(jnp.bfloat16)
    projected = jnp.dot(normed, proj_full, preferred_element_type=jnp.float32)
    query_rows = projected[:, :q_cols].astype(jnp.bfloat16)
    compressed_part = projected[:, q_cols:]
    compressed = jnp.transpose(gather_axis(compressed_part, "narrow"), (1, 0, 2)).reshape(
        tok_rows, kva_cols
    )
    first_token = wide_place * tok_rows
    token_ids = first_token + jnp.arange(tok_rows, dtype=jnp.int32)
    positions = lengths[token_ids // SPAN] + token_ids % SPAN
    own_keys = jnp.concatenate(
        [
            scaled_norm(compressed[:, :LAT], kv_gain).astype(jnp.bfloat16),
            rotate(compressed[:, LAT:], positions).astype(jnp.bfloat16),
        ],
        axis=1,
    )

    query_heads = query_rows.reshape(tok_rows, heads_here, NOPE + ROPE)
    own_rope_q = rotate(query_heads[..., NOPE:].astype(jnp.float32), positions[:, None]).astype(
        jnp.bfloat16
    )
    outgoing = jnp.concatenate(
        [
            query_heads[..., :NOPE].reshape(tok_rows, heads_here * NOPE),
            own_rope_q.reshape(tok_rows, heads_here * ROPE),
        ],
        axis=1,
    )
    raw_all = gather_axis(outgoing, "wide")
    total_tokens = raw_all.shape[0] * tok_rows
    raw_all = raw_all.reshape(total_tokens, heads_here * (NOPE + ROPE))
    kvb_heads = kvb_full.reshape(LAT, heads_here, NOPE + VDIM)
    key_maps = kvb_heads[..., :NOPE]
    value_maps = kvb_heads[..., NOPE:]
    nope_all = raw_all[:, : heads_here * NOPE].reshape(total_tokens, heads_here, NOPE)
    rope_all = raw_all[:, heads_here * NOPE :].reshape(total_tokens, heads_here, ROPE)
    lat_hm = jnp.einsum(
        "thc,lhc->htl", nope_all, key_maps, preferred_element_type=jnp.float32
    ).astype(jnp.bfloat16)
    rope_hm = jnp.transpose(rope_all, (1, 0, 2))
    value_hm = jnp.transpose(value_maps, (1, 0, 2))

    base = (wide_place * cache_rows).reshape(1).astype(jnp.int32)
    stats_hm, value_out = cache_attention(lengths, base, lat_hm, rope_hm, cache, value_hm)
    peak_hm = stats_hm[..., 0]
    total_hm = stats_hm[..., 1]

    own_request = first_token // SPAN
    start_row = own_request * SPAN
    own_slots = first_token % SPAN + jnp.arange(tok_rows, dtype=jnp.int32)
    causal = own_slots[None, :] <= jnp.arange(SPAN, dtype=jnp.int32)[:, None]
    own_lat = lax.dynamic_slice_in_dim(lat_hm, start_row, SPAN, 1)
    own_rope = lax.dynamic_slice_in_dim(rope_hm, start_row, SPAN, 1)
    own_scores = (
        jnp.einsum("hqc,kc->hqk", own_lat, own_keys[:, :LAT], preferred_element_type=jnp.float32)
        + jnp.einsum("hqc,kc->hqk", own_rope, own_keys[:, LAT:], preferred_element_type=jnp.float32)
    ) * score_scale
    own_live = causal[None]
    own_peak = jnp.max(jnp.where(own_live, own_scores, -1e30), axis=-1)
    own_weights = jnp.where(own_live, jnp.exp(own_scores - own_peak[..., None]), 0.0)
    own_total = jnp.sum(own_weights, axis=-1)
    own_mixed = jnp.einsum(
        "hqk,kc->hqc", own_weights.astype(jnp.bfloat16), own_keys[:, :LAT],
        preferred_element_type=jnp.float32,
    )
    own_upper = own_mixed.astype(jnp.bfloat16)
    own_lower = (own_mixed - own_upper.astype(jnp.float32)).astype(jnp.bfloat16)
    own_value = jnp.einsum(
        "hqc,hcv->hqv", own_upper, value_hm, preferred_element_type=jnp.float32
    ) + jnp.einsum("hqc,hcv->hqv", own_lower, value_hm, preferred_element_type=jnp.float32)
    old_part = (
        lax.dynamic_slice_in_dim(peak_hm, start_row, SPAN, 1),
        lax.dynamic_slice_in_dim(total_hm, start_row, SPAN, 1),
        lax.dynamic_slice_in_dim(value_out, start_row, SPAN, 1),
    )
    joint = merge_parts(old_part, (own_peak, own_total, own_value))
    peak_hm = lax.dynamic_update_slice_in_dim(peak_hm, joint[0], start_row, 1)
    total_hm = lax.dynamic_update_slice_in_dim(total_hm, joint[1], start_row, 1)
    value_out = lax.dynamic_update_slice_in_dim(value_out, joint[2], start_row, 1)

    stats = jnp.stack([peak_hm, total_hm], axis=0).astype(jnp.bfloat16)
    got_stats = lax.all_to_all(
        stats.reshape(2, heads_here, wide_count, tok_rows), "wide", 2, 2, tiled=True
    ).astype(jnp.float32)
    got_value = lax.all_to_all(
        value_out.astype(jnp.bfloat16).reshape(heads_here, wide_count, tok_rows, VDIM),
        "wide",
        1,
        1,
        tiled=True,
    ).astype(jnp.float32)
    got_peak = got_stats[0]
    got_total = got_stats[1]
    peak_value = jnp.max(got_peak, axis=1)
    factor = jnp.exp(got_peak - peak_value[:, None])
    denominator = jnp.sum(factor * got_total, axis=1)
    numerator = jnp.sum(factor[..., None] * got_value, axis=1)
    context = jnp.transpose(
        (numerator / denominator[..., None]).astype(jnp.bfloat16), (1, 0, 2)
    ).reshape(tok_rows, heads_here * VDIM)
    partial_out = jnp.einsum(
        "tk,wkc->twc", context, o_got, preferred_element_type=jnp.float32
    ).reshape(tok_rows, -1)
    out_cols = partial_out.shape[1]
    pieces = jnp.transpose(
        partial_out.astype(jnp.bfloat16).reshape(tok_rows, narrow_count, out_cols // narrow_count),
        (1, 0, 2),
    )
    got_pieces = lax.all_to_all(pieces, "narrow", 0, 0, tiled=True)
    mine = jnp.sum(got_pieces.astype(jnp.float32), axis=0).astype(jnp.bfloat16)
    all_pieces = gather_axis(mine, "narrow")
    return jnp.transpose(all_pieces, (1, 0, 2)).reshape(tok_rows, out_cols)


def solution(mesh):
    in_specs = (
        P("wide", None),
        P(),
        P("wide", "narrow"),
        P("wide", None),
        P(),
        P("wide", "narrow"),
        P("narrow", "wide"),
        P(None, "wide", None),
        P(),
    )
    out_specs = P("wide", None)
    return jax.shard_map(
        per_device, mesh=mesh, in_specs=in_specs, out_specs=out_specs, check_vma=False
    )
```

```python
import jax
import jax.numpy as jnp
from jax import lax
from jax.sharding import PartitionSpec as P
from jax.experimental import pallas as pl
from jax.experimental.pallas import tpu as pltpu

NOPE = 128
ROPE = 64
VDIM = 128
LAT = 512
SPAN = 512


eps = 1e-06
score_scale = 1.0 / 13.856406460551018


def rotate(values, positions):
    half_size = values.shape[-1] // 2
    frequency = 10000.0 ** (-jnp.arange(half_size, dtype=jnp.float32) / half_size)
    angles = positions.astype(jnp.float32)[..., None] * frequency
    lower_half = values[..., :half_size]
    upper_half = values[..., half_size:]
    cosine = jnp.cos(angles)
    sine_part = jnp.sin(angles)
    return jnp.concatenate(
        [
            lower_half * cosine - upper_half * sine_part,
            lower_half * sine_part + upper_half * cosine,
        ],
        axis=-1,
    )


def scaled_norm(values, gain):
    return (
        values
        * lax.rsqrt(jnp.mean(values * values, axis=-1, keepdims=True) + eps)
        * gain.astype(jnp.float32)
    )


def gather_axis(x, axis_name):
    count = lax.axis_size(axis_name)
    spread = jnp.broadcast_to(x[None], (count,) + x.shape)
    return lax.all_to_all(spread, axis_name, split_axis=0, concat_axis=0, tiled=True)


def absorb(nope_part, key_maps):
    return jnp.einsum(
        "thc,lhc->thl", nope_part, key_maps, preferred_element_type=jnp.float32
    ).astype(jnp.bfloat16)


def project_values(mixed, value_maps):
    upper_part = mixed.astype(jnp.bfloat16)
    lower_part = (mixed - upper_part.astype(jnp.float32)).astype(jnp.bfloat16)
    first_term = jnp.einsum(
        "qhc,chv->qhv", upper_part, value_maps, preferred_element_type=jnp.float32
    )
    second_term = jnp.einsum(
        "qhc,chv->qhv", lower_part, value_maps, preferred_element_type=jnp.float32
    )
    return first_term + second_term


def attend(block_queries, key_rows, live_mask, value_maps):
    scores = (
        jnp.einsum("qhc,kc->qhk", block_queries, key_rows, preferred_element_type=jnp.float32)
        * score_scale
    )
    live_rows = live_mask[:, None, :]
    row_peak = jnp.max(jnp.where(live_rows, scores, -1e30), axis=-1)
    weights = jnp.where(live_rows, jnp.exp(scores - row_peak[..., None]), 0.0)
    row_total = jnp.sum(weights, axis=-1)
    mixed = jnp.einsum(
        "qhk,kc->qhc",
        weights.astype(jnp.bfloat16),
        key_rows[:, :LAT],
        preferred_element_type=jnp.float32,
    )
    return (row_peak, row_total, project_values(mixed, value_maps))


def skipped(block_queries, key_rows, live_mask, value_maps):
    rows_here = block_queries.shape[0]
    heads_here = block_queries.shape[1]
    return (
        jnp.full((rows_here, heads_here), -1e30, jnp.float32),
        jnp.zeros((rows_here, heads_here), jnp.float32),
        jnp.zeros((rows_here, heads_here, value_maps.shape[2]), jnp.float32),
    )


def cache_kernel(lens_ref, base_ref, lat_ref, rope_ref, kv_ref, vm_ref, stats_ref, value_ref):
    length_now = lens_ref[pl.program_id(0)]
    base = base_ref[0]
    live_block = base < length_now

    @pl.when(live_block)
    def _():
        keys = kv_ref[0]
        key_lat = keys[:, :LAT]
        key_rope = keys[:, LAT:]
        nt = (((1,), (1,)), ((), ()))
        scores = (
            lax.dot_general(lat_ref[0], key_lat, nt, preferred_element_type=jnp.float32)
            + lax.dot_general(rope_ref[0], key_rope, nt, preferred_element_type=jnp.float32)
        ) * score_scale
        slots = base + lax.broadcasted_iota(jnp.int32, scores.shape, 1)
        live = slots < length_now
        peak = jnp.max(jnp.where(live, scores, -1e30), axis=-1, keepdims=True)
        weights = jnp.where(live, jnp.exp(scores - peak), 0.0)
        total = jnp.sum(weights, axis=-1, keepdims=True)
        lane = lax.broadcasted_iota(jnp.int32, (peak.shape[0], 128), 1)
        packed = jnp.where(lane == 0, peak, jnp.where(lane == 1, total, 0.0))
        stats_ref[0, 0] = jnp.transpose(packed)[: stats_ref.shape[2]]
        mixed = jnp.dot(weights.astype(jnp.bfloat16), key_lat, preferred_element_type=jnp.float32)
        value_map = vm_ref[0]
        upper_part = mixed.astype(jnp.bfloat16)
        lower_part = (mixed - upper_part.astype(jnp.float32)).astype(jnp.bfloat16)
        value_ref[0] = jnp.dot(upper_part, value_map, preferred_element_type=jnp.float32) + jnp.dot(
            lower_part, value_map, preferred_element_type=jnp.float32
        )

    @pl.when(jnp.logical_not(live_block))
    def _():
        row = lax.broadcasted_iota(jnp.int32, stats_ref.shape, 2)
        stats_ref[...] = jnp.where(row == 0, -1e30, 0.0).astype(jnp.float32)
        value_ref[...] = jnp.zeros(value_ref.shape, jnp.float32)


def cache_attention(lengths, base, lat_hm, rope_hm, cache, value_hm):
    heads_here, total_tokens, _ = lat_hm.shape
    requests, cache_rows, width = cache.shape
    span = total_tokens // requests
    vdim = value_hm.shape[2]
    grid_spec = pltpu.PrefetchScalarGridSpec(
        num_scalar_prefetch=2,
        grid=(requests, heads_here),
        in_specs=[
            pl.BlockSpec((1, span, LAT), lambda r, h, lens, b: (h, r, 0)),
            pl.BlockSpec((1, span, ROPE), lambda r, h, lens, b: (h, r, 0)),
            pl.BlockSpec((1, cache_rows, width), lambda r, h, lens, b: (r, 0, 0)),
            pl.BlockSpec((1, LAT, vdim), lambda r, h, lens, b: (h, 0, 0)),
        ],
        out_specs=[
            pl.BlockSpec((1, 1, 8, span), lambda r, h, lens, b: (h, r, 0, 0)),
            pl.BlockSpec((1, span, vdim), lambda r, h, lens, b: (h, r, 0)),
        ],
    )
    return pl.pallas_call(
        cache_kernel,
        grid_spec=grid_spec,
        out_shape=[
            jax.ShapeDtypeStruct((heads_here, requests, 8, span), jnp.float32),
            jax.ShapeDtypeStruct((heads_here, total_tokens, vdim), jnp.float32),
        ],
        compiler_params=pltpu.CompilerParams(dimension_semantics=("arbitrary", "arbitrary")),
    )(lengths, base, lat_hm, rope_hm, cache, value_hm)


def merge_parts(first, second):
    joint_peak = jnp.maximum(first[0], second[0])
    first_factor = jnp.exp(first[0] - joint_peak)
    second_factor = jnp.exp(second[0] - joint_peak)
    joint_total = first_factor * first[1] + second_factor * second[1]
    joint_value = first_factor[..., None] * first[2] + second_factor[..., None] * second[2]
    return (joint_peak, joint_total, joint_value)


def per_device(
    hidden, attn_gain, q_weight, kva_weight, kv_gain, kvb_weight, o_weight, cache, lengths
):
    wide_count = lax.axis_size("wide")
    wide_place = lax.axis_index("wide")
    tok_rows = hidden.shape[0]
    requests = lengths.shape[0]
    cache_rows = cache.shape[1]
    heads_here = q_weight.shape[1] // (NOPE + ROPE)
    narrow_count = lax.axis_size("narrow")
    narrow_place = lax.axis_index("narrow")
    q_cols = q_weight.shape[1]
    kva_cols = kva_weight.shape[1]
    kva_part = kva_cols // narrow_count
    kva_mine = lax.dynamic_slice_in_dim(kva_weight, narrow_place * kva_part, kva_part, 1)
    packed = jnp.concatenate([q_weight, kva_mine], axis=1)
    got_weights = gather_axis(packed, "wide")
    proj_full = got_weights.reshape(-1, q_cols + kva_part)
    kvb_full = gather_axis(kvb_weight, "wide").reshape(-1, kvb_weight.shape[1])
    o_got = lax.all_gather(o_weight, "wide", axis=0, tiled=False)

    normed = scaled_norm(hidden.astype(jnp.float32), attn_gain).astype(jnp.bfloat16)
    projected = jnp.dot(normed, proj_full, preferred_element_type=jnp.float32)
    query_rows = projected[:, :q_cols].astype(jnp.bfloat16)
    compressed_part = projected[:, q_cols:]
    compressed = jnp.transpose(gather_axis(compressed_part, "narrow"), (1, 0, 2)).reshape(
        tok_rows, kva_cols
    )
    first_token = wide_place * tok_rows
    token_ids = first_token + jnp.arange(tok_rows, dtype=jnp.int32)
    positions = lengths[token_ids // SPAN] + token_ids % SPAN
    own_keys = jnp.concatenate(
        [
            scaled_norm(compressed[:, :LAT], kv_gain).astype(jnp.bfloat16),
            rotate(compressed[:, LAT:], positions).astype(jnp.bfloat16),
        ],
        axis=1,
    )

    query_heads = query_rows.reshape(tok_rows, heads_here, NOPE + ROPE)
    own_rope_q = rotate(query_heads[..., NOPE:].astype(jnp.float32), positions[:, None]).astype(
        jnp.bfloat16
    )
    outgoing = jnp.concatenate(
        [
            query_heads[..., :NOPE].reshape(tok_rows, heads_here * NOPE),
            own_rope_q.reshape(tok_rows, heads_here * ROPE),
        ],
        axis=1,
    )
    raw_all = gather_axis(outgoing, "wide")
    total_tokens = raw_all.shape[0] * tok_rows
    raw_all = raw_all.reshape(total_tokens, heads_here * (NOPE + ROPE))
    kvb_heads = kvb_full.reshape(LAT, heads_here, NOPE + VDIM)
    key_maps = kvb_heads[..., :NOPE]
    value_maps = kvb_heads[..., NOPE:]
    nope_all = raw_all[:, : heads_here * NOPE].reshape(total_tokens, heads_here, NOPE)
    rope_all = raw_all[:, heads_here * NOPE :].reshape(total_tokens, heads_here, ROPE)
    lat_hm = jnp.einsum(
        "thc,lhc->htl", nope_all, key_maps, preferred_element_type=jnp.float32
    ).astype(jnp.bfloat16)
    rope_hm = jnp.transpose(rope_all, (1, 0, 2))
    value_hm = jnp.transpose(value_maps, (1, 0, 2))

    base = (wide_place * cache_rows).reshape(1).astype(jnp.int32)
    stats_hm, value_out = cache_attention(lengths, base, lat_hm, rope_hm, cache, value_hm)
    peak_hm = stats_hm[:, :, 0].reshape(heads_here, total_tokens)
    total_hm = stats_hm[:, :, 1].reshape(heads_here, total_tokens)

    own_request = first_token // SPAN
    start_row = own_request * SPAN
    own_slots = first_token % SPAN + jnp.arange(tok_rows, dtype=jnp.int32)
    causal = own_slots[None, :] <= jnp.arange(SPAN, dtype=jnp.int32)[:, None]
    own_lat = lax.dynamic_slice_in_dim(lat_hm, start_row, SPAN, 1)
    own_rope = lax.dynamic_slice_in_dim(rope_hm, start_row, SPAN, 1)
    own_scores = (
        jnp.einsum("hqc,kc->hqk", own_lat, own_keys[:, :LAT], preferred_element_type=jnp.float32)
        + jnp.einsum("hqc,kc->hqk", own_rope, own_keys[:, LAT:], preferred_element_type=jnp.float32)
    ) * score_scale
    own_live = causal[None]
    own_peak = jnp.max(jnp.where(own_live, own_scores, -1e30), axis=-1)
    own_weights = jnp.where(own_live, jnp.exp(own_scores - own_peak[..., None]), 0.0)
    own_total = jnp.sum(own_weights, axis=-1)
    own_mixed = jnp.einsum(
        "hqk,kc->hqc", own_weights.astype(jnp.bfloat16), own_keys[:, :LAT],
        preferred_element_type=jnp.float32,
    )
    own_upper = own_mixed.astype(jnp.bfloat16)
    own_lower = (own_mixed - own_upper.astype(jnp.float32)).astype(jnp.bfloat16)
    own_value = jnp.einsum(
        "hqc,hcv->hqv", own_upper, value_hm, preferred_element_type=jnp.float32
    ) + jnp.einsum("hqc,hcv->hqv", own_lower, value_hm, preferred_element_type=jnp.float32)
    old_part = (
        lax.dynamic_slice_in_dim(peak_hm, start_row, SPAN, 1),
        lax.dynamic_slice_in_dim(total_hm, start_row, SPAN, 1),
        lax.dynamic_slice_in_dim(value_out, start_row, SPAN, 1),
    )
    joint = merge_parts(old_part, (own_peak, own_total, own_value))
    peak_hm = lax.dynamic_update_slice_in_dim(peak_hm, joint[0], start_row, 1)
    total_hm = lax.dynamic_update_slice_in_dim(total_hm, joint[1], start_row, 1)
    value_out = lax.dynamic_update_slice_in_dim(value_out, joint[2], start_row, 1)

    stats = jnp.stack([peak_hm, total_hm], axis=0).astype(jnp.bfloat16)
    got_stats = lax.all_to_all(
        stats.reshape(2, heads_here, wide_count, tok_rows), "wide", 2, 2, tiled=True
    ).astype(jnp.float32)
    got_value = lax.all_to_all(
        value_out.astype(jnp.bfloat16).reshape(heads_here, wide_count, tok_rows, VDIM),
        "wide",
        1,
        1,
        tiled=True,
    ).astype(jnp.float32)
    got_peak = got_stats[0]
    got_total = got_stats[1]
    peak_value = jnp.max(got_peak, axis=1)
    factor = jnp.exp(got_peak - peak_value[:, None])
    denominator = jnp.sum(factor * got_total, axis=1)
    numerator = jnp.sum(factor[..., None] * got_value, axis=1)
    context = jnp.transpose(
        (numerator / denominator[..., None]).astype(jnp.bfloat16), (1, 0, 2)
    ).reshape(tok_rows, heads_here * VDIM)
    partial_out = jnp.einsum(
        "tk,wkc->twc", context, o_got, preferred_element_type=jnp.float32
    ).reshape(tok_rows, -1)
    out_cols = partial_out.shape[1]
    pieces = jnp.transpose(
        partial_out.astype(jnp.bfloat16).reshape(tok_rows, narrow_count, out_cols // narrow_count),
        (1, 0, 2),
    )
    got_pieces = lax.all_to_all(pieces, "narrow", 0, 0, tiled=True)
    mine = jnp.sum(got_pieces.astype(jnp.float32), axis=0).astype(jnp.bfloat16)
    all_pieces = gather_axis(mine, "narrow")
    return jnp.transpose(all_pieces, (1, 0, 2)).reshape(tok_rows, out_cols)


def solution(mesh):
    in_specs = (
        P("wide", None),
        P(),
        P("wide", "narrow"),
        P("wide", None),
        P(),
        P("wide", "narrow"),
        P("narrow", "wide"),
        P(None, "wide", None),
        P(),
    )
    out_specs = P("wide", None)
    return jax.shard_map(
        per_device, mesh=mesh, in_specs=in_specs, out_specs=out_specs, check_vma=False
    )
```

```python
import jax
import jax.numpy as jnp
from jax import lax
from jax.sharding import PartitionSpec as P
from jax.experimental import pallas as pl
from jax.experimental.pallas import tpu as pltpu

NOPE = 128
ROPE = 64
VDIM = 128
LAT = 512
SPAN = 512


eps = 1e-06
score_scale = 1.0 / 13.856406460551018


def rotate(values, positions):
    half_size = values.shape[-1] // 2
    frequency = 10000.0 ** (-jnp.arange(half_size, dtype=jnp.float32) / half_size)
    angles = positions.astype(jnp.float32)[..., None] * frequency
    lower_half = values[..., :half_size]
    upper_half = values[..., half_size:]
    cosine = jnp.cos(angles)
    sine_part = jnp.sin(angles)
    return jnp.concatenate(
        [
            lower_half * cosine - upper_half * sine_part,
            lower_half * sine_part + upper_half * cosine,
        ],
        axis=-1,
    )


def scaled_norm(values, gain):
    return (
        values
        * lax.rsqrt(jnp.mean(values * values, axis=-1, keepdims=True) + eps)
        * gain.astype(jnp.float32)
    )


def gather_axis(x, axis_name):
    count = lax.axis_size(axis_name)
    spread = jnp.broadcast_to(x[None], (count,) + x.shape)
    return lax.all_to_all(spread, axis_name, split_axis=0, concat_axis=0, tiled=True)


def absorb(nope_part, key_maps):
    return jnp.einsum(
        "thc,lhc->thl", nope_part, key_maps, preferred_element_type=jnp.float32
    ).astype(jnp.bfloat16)


def project_values(mixed, value_maps):
    upper_part = mixed.astype(jnp.bfloat16)
    lower_part = (mixed - upper_part.astype(jnp.float32)).astype(jnp.bfloat16)
    first_term = jnp.einsum(
        "qhc,chv->qhv", upper_part, value_maps, preferred_element_type=jnp.float32
    )
    second_term = jnp.einsum(
        "qhc,chv->qhv", lower_part, value_maps, preferred_element_type=jnp.float32
    )
    return first_term + second_term


def attend(block_queries, key_rows, live_mask, value_maps):
    scores = (
        jnp.einsum("qhc,kc->qhk", block_queries, key_rows, preferred_element_type=jnp.float32)
        * score_scale
    )
    live_rows = live_mask[:, None, :]
    row_peak = jnp.max(jnp.where(live_rows, scores, -1e30), axis=-1)
    weights = jnp.where(live_rows, jnp.exp(scores - row_peak[..., None]), 0.0)
    row_total = jnp.sum(weights, axis=-1)
    mixed = jnp.einsum(
        "qhk,kc->qhc",
        weights.astype(jnp.bfloat16),
        key_rows[:, :LAT],
        preferred_element_type=jnp.float32,
    )
    return (row_peak, row_total, project_values(mixed, value_maps))


def skipped(block_queries, key_rows, live_mask, value_maps):
    rows_here = block_queries.shape[0]
    heads_here = block_queries.shape[1]
    return (
        jnp.full((rows_here, heads_here), -1e30, jnp.float32),
        jnp.zeros((rows_here, heads_here), jnp.float32),
        jnp.zeros((rows_here, heads_here, value_maps.shape[2]), jnp.float32),
    )


def cache_kernel(
    lens_ref, base_ref, nope_ref, rope_ref, kv_ref, km_ref, vm_ref, stats_ref, value_ref
):
    length_now = lens_ref[pl.program_id(0)]
    base = base_ref[0]
    live_block = base < length_now

    @pl.when(live_block)
    def _():
        keys = kv_ref[0]
        key_lat = keys[:, :LAT]
        key_rope = keys[:, LAT:]
        nt = (((1,), (1,)), ((), ()))
        q_lat = lax.dot_general(
            nope_ref[...], km_ref[...], nt, preferred_element_type=jnp.float32
        ).astype(jnp.bfloat16)
        scores = (
            lax.dot_general(q_lat, key_lat, nt, preferred_element_type=jnp.float32)
            + lax.dot_general(rope_ref[0], key_rope, nt, preferred_element_type=jnp.float32)
        ) * score_scale
        slots = base + lax.broadcasted_iota(jnp.int32, scores.shape, 1)
        live = slots < length_now
        peak = jnp.max(jnp.where(live, scores, -1e30), axis=-1, keepdims=True)
        weights = jnp.where(live, jnp.exp(scores - peak), 0.0)
        total = jnp.sum(weights, axis=-1, keepdims=True)
        lane = lax.broadcasted_iota(jnp.int32, (peak.shape[0], 128), 1)
        packed = jnp.where(lane == 0, peak, jnp.where(lane == 1, total, 0.0))
        stats_ref[0, 0] = jnp.transpose(packed)[: stats_ref.shape[2]]
        mixed = jnp.dot(weights.astype(jnp.bfloat16), key_lat, preferred_element_type=jnp.float32)
        value_map = vm_ref[...]
        upper_part = mixed.astype(jnp.bfloat16)
        lower_part = (mixed - upper_part.astype(jnp.float32)).astype(jnp.bfloat16)
        value_ref[0] = jnp.dot(upper_part, value_map, preferred_element_type=jnp.float32) + jnp.dot(
            lower_part, value_map, preferred_element_type=jnp.float32
        )

    @pl.when(jnp.logical_not(live_block))
    def _():
        row = lax.broadcasted_iota(jnp.int32, stats_ref.shape, 2)
        stats_ref[...] = jnp.where(row == 0, -1e30, 0.0).astype(jnp.float32)
        value_ref[...] = jnp.zeros(value_ref.shape, jnp.float32)


def cache_attention(lengths, base, nope_rows, rope_hm, cache, kvb_full):
    heads_here, total_tokens, _ = rope_hm.shape
    requests, cache_rows, width = cache.shape
    span = total_tokens // requests
    vdim = VDIM
    grid_spec = pltpu.PrefetchScalarGridSpec(
        num_scalar_prefetch=2,
        grid=(requests, heads_here),
        in_specs=[
            pl.BlockSpec((span, NOPE), lambda r, h, lens, b: (r, h)),
            pl.BlockSpec((1, span, ROPE), lambda r, h, lens, b: (h, r, 0)),
            pl.BlockSpec((1, cache_rows, width), lambda r, h, lens, b: (r, 0, 0)),
            pl.BlockSpec((LAT, NOPE), lambda r, h, lens, b: (0, 2 * h)),
            pl.BlockSpec((LAT, VDIM), lambda r, h, lens, b: (0, 2 * h + 1)),
        ],
        out_specs=[
            pl.BlockSpec((1, 1, 8, span), lambda r, h, lens, b: (h, r, 0, 0)),
            pl.BlockSpec((1, span, vdim), lambda r, h, lens, b: (h, r, 0)),
        ],
    )
    return pl.pallas_call(
        cache_kernel,
        grid_spec=grid_spec,
        out_shape=[
            jax.ShapeDtypeStruct((heads_here, requests, 8, span), jnp.float32),
            jax.ShapeDtypeStruct((heads_here, total_tokens, vdim), jnp.float32),
        ],
        compiler_params=pltpu.CompilerParams(dimension_semantics=("arbitrary", "arbitrary")),
    )(lengths, base, nope_rows, rope_hm, cache, kvb_full, kvb_full)


def merge_parts(first, second):
    joint_peak = jnp.maximum(first[0], second[0])
    first_factor = jnp.exp(first[0] - joint_peak)
    second_factor = jnp.exp(second[0] - joint_peak)
    joint_total = first_factor * first[1] + second_factor * second[1]
    joint_value = first_factor[..., None] * first[2] + second_factor[..., None] * second[2]
    return (joint_peak, joint_total, joint_value)


def per_device(
    hidden, attn_gain, q_weight, kva_weight, kv_gain, kvb_weight, o_weight, cache, lengths
):
    wide_count = lax.axis_size("wide")
    wide_place = lax.axis_index("wide")
    tok_rows = hidden.shape[0]
    requests = lengths.shape[0]
    cache_rows = cache.shape[1]
    heads_here = q_weight.shape[1] // (NOPE + ROPE)
    narrow_count = lax.axis_size("narrow")
    narrow_place = lax.axis_index("narrow")
    q_cols = q_weight.shape[1]
    kva_cols = kva_weight.shape[1]
    kva_part = kva_cols // narrow_count
    kva_mine = lax.dynamic_slice_in_dim(kva_weight, narrow_place * kva_part, kva_part, 1)
    packed = jnp.concatenate([q_weight, kva_mine], axis=1)
    got_weights = gather_axis(packed, "wide")
    proj_full = got_weights.reshape(-1, q_cols + kva_part)
    kvb_full = gather_axis(kvb_weight, "wide").reshape(-1, kvb_weight.shape[1])
    o_got = lax.all_gather(o_weight, "wide", axis=0, tiled=False)

    normed = scaled_norm(hidden.astype(jnp.float32), attn_gain).astype(jnp.bfloat16)
    projected = jnp.dot(normed, proj_full, preferred_element_type=jnp.float32)
    query_rows = projected[:, :q_cols].astype(jnp.bfloat16)
    compressed_part = projected[:, q_cols:]
    compressed = jnp.transpose(gather_axis(compressed_part, "narrow"), (1, 0, 2)).reshape(
        tok_rows, kva_cols
    )
    first_token = wide_place * tok_rows
    token_ids = first_token + jnp.arange(tok_rows, dtype=jnp.int32)
    positions = lengths[token_ids // SPAN] + token_ids % SPAN
    own_keys = jnp.concatenate(
        [
            scaled_norm(compressed[:, :LAT], kv_gain).astype(jnp.bfloat16),
            rotate(compressed[:, LAT:], positions).astype(jnp.bfloat16),
        ],
        axis=1,
    )

    query_heads = query_rows.reshape(tok_rows, heads_here, NOPE + ROPE)
    own_rope_q = rotate(query_heads[..., NOPE:].astype(jnp.float32), positions[:, None]).astype(
        jnp.bfloat16
    )
    outgoing = jnp.concatenate(
        [
            query_heads[..., :NOPE].reshape(tok_rows, heads_here * NOPE),
            own_rope_q.reshape(tok_rows, heads_here * ROPE),
        ],
        axis=1,
    )
    raw_all = gather_axis(outgoing, "wide")
    total_tokens = raw_all.shape[0] * tok_rows
    raw_all = raw_all.reshape(total_tokens, heads_here * (NOPE + ROPE))
    kvb_heads = kvb_full.reshape(LAT, heads_here, NOPE + VDIM)
    key_maps = kvb_heads[..., :NOPE]
    value_maps = kvb_heads[..., NOPE:]
    nope_all = raw_all[:, : heads_here * NOPE].reshape(total_tokens, heads_here, NOPE)
    rope_all = raw_all[:, heads_here * NOPE :].reshape(total_tokens, heads_here, ROPE)
    rope_hm = jnp.transpose(rope_all, (1, 0, 2))
    value_hm = jnp.transpose(value_maps, (1, 0, 2))

    base = (wide_place * cache_rows).reshape(1).astype(jnp.int32)
    stats_hm, value_out = cache_attention(lengths, base, raw_all, rope_hm, cache, kvb_full)
    peak_hm = stats_hm[:, :, 0].reshape(heads_here, total_tokens)
    total_hm = stats_hm[:, :, 1].reshape(heads_here, total_tokens)

    own_request = first_token // SPAN
    start_row = own_request * SPAN
    own_slots = first_token % SPAN + jnp.arange(tok_rows, dtype=jnp.int32)
    causal = own_slots[None, :] <= jnp.arange(SPAN, dtype=jnp.int32)[:, None]
    own_lat = jnp.einsum(
        "thc,lhc->htl",
        lax.dynamic_slice_in_dim(nope_all, start_row, SPAN, 0),
        key_maps,
        preferred_element_type=jnp.float32,
    ).astype(jnp.bfloat16)
    own_rope = lax.dynamic_slice_in_dim(rope_hm, start_row, SPAN, 1)
    own_scores = (
        jnp.einsum("hqc,kc->hqk", own_lat, own_keys[:, :LAT], preferred_element_type=jnp.float32)
        + jnp.einsum("hqc,kc->hqk", own_rope, own_keys[:, LAT:], preferred_element_type=jnp.float32)
    ) * score_scale
    own_live = causal[None]
    own_peak = jnp.max(jnp.where(own_live, own_scores, -1e30), axis=-1)
    own_weights = jnp.where(own_live, jnp.exp(own_scores - own_peak[..., None]), 0.0)
    own_total = jnp.sum(own_weights, axis=-1)
    own_mixed = jnp.einsum(
        "hqk,kc->hqc", own_weights.astype(jnp.bfloat16), own_keys[:, :LAT],
        preferred_element_type=jnp.float32,
    )
    own_upper = own_mixed.astype(jnp.bfloat16)
    own_lower = (own_mixed - own_upper.astype(jnp.float32)).astype(jnp.bfloat16)
    own_value = jnp.einsum(
        "hqc,hcv->hqv", own_upper, value_hm, preferred_element_type=jnp.float32
    ) + jnp.einsum("hqc,hcv->hqv", own_lower, value_hm, preferred_element_type=jnp.float32)
    old_part = (
        lax.dynamic_slice_in_dim(peak_hm, start_row, SPAN, 1),
        lax.dynamic_slice_in_dim(total_hm, start_row, SPAN, 1),
        lax.dynamic_slice_in_dim(value_out, start_row, SPAN, 1),
    )
    joint = merge_parts(old_part, (own_peak, own_total, own_value))
    peak_hm = lax.dynamic_update_slice_in_dim(peak_hm, joint[0], start_row, 1)
    total_hm = lax.dynamic_update_slice_in_dim(total_hm, joint[1], start_row, 1)
    value_out = lax.dynamic_update_slice_in_dim(value_out, joint[2], start_row, 1)

    stats = jnp.stack([peak_hm, total_hm], axis=0).astype(jnp.bfloat16)
    got_stats = lax.all_to_all(
        stats.reshape(2, heads_here, wide_count, tok_rows), "wide", 2, 2, tiled=True
    ).astype(jnp.float32)
    got_value = lax.all_to_all(
        value_out.astype(jnp.bfloat16).reshape(heads_here, wide_count, tok_rows, VDIM),
        "wide",
        1,
        1,
        tiled=True,
    ).astype(jnp.float32)
    got_peak = got_stats[0]
    got_total = got_stats[1]
    peak_value = jnp.max(got_peak, axis=1)
    factor = jnp.exp(got_peak - peak_value[:, None])
    denominator = jnp.sum(factor * got_total, axis=1)
    numerator = jnp.sum(factor[..., None] * got_value, axis=1)
    context = jnp.transpose(
        (numerator / denominator[..., None]).astype(jnp.bfloat16), (1, 0, 2)
    ).reshape(tok_rows, heads_here * VDIM)
    partial_out = jnp.einsum(
        "tk,wkc->twc", context, o_got, preferred_element_type=jnp.float32
    ).reshape(tok_rows, -1)
    out_cols = partial_out.shape[1]
    pieces = jnp.transpose(
        partial_out.astype(jnp.bfloat16).reshape(tok_rows, narrow_count, out_cols // narrow_count),
        (1, 0, 2),
    )
    got_pieces = lax.all_to_all(pieces, "narrow", 0, 0, tiled=True)
    mine = jnp.sum(got_pieces.astype(jnp.float32), axis=0).astype(jnp.bfloat16)
    all_pieces = gather_axis(mine, "narrow")
    return jnp.transpose(all_pieces, (1, 0, 2)).reshape(tok_rows, out_cols)


def solution(mesh):
    in_specs = (
        P("wide", None),
        P(),
        P("wide", "narrow"),
        P("wide", None),
        P(),
        P("wide", "narrow"),
        P("narrow", "wide"),
        P(None, "wide", None),
        P(),
    )
    out_specs = P("wide", None)
    return jax.shard_map(
        per_device, mesh=mesh, in_specs=in_specs, out_specs=out_specs, check_vma=False
    )
```

```python
import jax
import jax.numpy as jnp
from jax import lax
from jax.sharding import PartitionSpec as P
from jax.experimental import pallas as pl
from jax.experimental.pallas import tpu as pltpu

NOPE = 128
ROPE = 64
VDIM = 128
LAT = 512
SPAN = 512


eps = 1e-06
score_scale = 1.0 / 13.856406460551018


def rotate(values, positions):
    half_size = values.shape[-1] // 2
    frequency = 10000.0 ** (-jnp.arange(half_size, dtype=jnp.float32) / half_size)
    angles = positions.astype(jnp.float32)[..., None] * frequency
    lower_half = values[..., :half_size]
    upper_half = values[..., half_size:]
    cosine = jnp.cos(angles)
    sine_part = jnp.sin(angles)
    return jnp.concatenate(
        [
            lower_half * cosine - upper_half * sine_part,
            lower_half * sine_part + upper_half * cosine,
        ],
        axis=-1,
    )


def scaled_norm(values, gain):
    return (
        values
        * lax.rsqrt(jnp.mean(values * values, axis=-1, keepdims=True) + eps)
        * gain.astype(jnp.float32)
    )


def gather_axis(x, axis_name):
    count = lax.axis_size(axis_name)
    spread = jnp.broadcast_to(x[None], (count,) + x.shape)
    return lax.all_to_all(spread, axis_name, split_axis=0, concat_axis=0, tiled=True)


def absorb(nope_part, key_maps):
    return jnp.einsum(
        "thc,lhc->thl", nope_part, key_maps, preferred_element_type=jnp.float32
    ).astype(jnp.bfloat16)


def project_values(mixed, value_maps):
    upper_part = mixed.astype(jnp.bfloat16)
    lower_part = (mixed - upper_part.astype(jnp.float32)).astype(jnp.bfloat16)
    first_term = jnp.einsum(
        "qhc,chv->qhv", upper_part, value_maps, preferred_element_type=jnp.float32
    )
    second_term = jnp.einsum(
        "qhc,chv->qhv", lower_part, value_maps, preferred_element_type=jnp.float32
    )
    return first_term + second_term


def attend(block_queries, key_rows, live_mask, value_maps):
    scores = (
        jnp.einsum("qhc,kc->qhk", block_queries, key_rows, preferred_element_type=jnp.float32)
        * score_scale
    )
    live_rows = live_mask[:, None, :]
    row_peak = jnp.max(jnp.where(live_rows, scores, -1e30), axis=-1)
    weights = jnp.where(live_rows, jnp.exp(scores - row_peak[..., None]), 0.0)
    row_total = jnp.sum(weights, axis=-1)
    mixed = jnp.einsum(
        "qhk,kc->qhc",
        weights.astype(jnp.bfloat16),
        key_rows[:, :LAT],
        preferred_element_type=jnp.float32,
    )
    return (row_peak, row_total, project_values(mixed, value_maps))


def skipped(block_queries, key_rows, live_mask, value_maps):
    rows_here = block_queries.shape[0]
    heads_here = block_queries.shape[1]
    return (
        jnp.full((rows_here, heads_here), -1e30, jnp.float32),
        jnp.zeros((rows_here, heads_here), jnp.float32),
        jnp.zeros((rows_here, heads_here, value_maps.shape[2]), jnp.float32),
    )


def cache_kernel(lens_ref, base_ref, lat_ref, rope_ref, kv_ref, vm_ref, stats_ref, value_ref):
    length_now = lens_ref[pl.program_id(0)]
    base = base_ref[0]
    live_block = base < length_now

    @pl.when(live_block)
    def _():
        keys = kv_ref[0]
        key_lat = keys[:, :LAT]
        key_rope = keys[:, LAT:]
        nt = (((1,), (1,)), ((), ()))
        scores = (
            lax.dot_general(lat_ref[0], key_lat, nt, preferred_element_type=jnp.float32)
            + lax.dot_general(rope_ref[0], key_rope, nt, preferred_element_type=jnp.float32)
        ) * score_scale
        slots = base + lax.broadcasted_iota(jnp.int32, scores.shape, 1)
        live = slots < length_now
        peak = jnp.max(jnp.where(live, scores, -1e30), axis=-1, keepdims=True)
        weights = jnp.where(live, jnp.exp(scores - peak), 0.0)
        total = jnp.sum(weights, axis=-1, keepdims=True)
        lane = lax.broadcasted_iota(jnp.int32, (peak.shape[0], 128), 1)
        packed = jnp.where(lane == 0, peak, jnp.where(lane == 1, total, 0.0))
        stats_ref[0, 0] = jnp.transpose(packed)[: stats_ref.shape[2]]
        mixed = jnp.dot(weights.astype(jnp.bfloat16), key_lat, preferred_element_type=jnp.float32)
        value_map = vm_ref[0]
        upper_part = mixed.astype(jnp.bfloat16)
        lower_part = (mixed - upper_part.astype(jnp.float32)).astype(jnp.bfloat16)
        value_ref[0] = jnp.dot(upper_part, value_map, preferred_element_type=jnp.float32) + jnp.dot(
            lower_part, value_map, preferred_element_type=jnp.float32
        )

    @pl.when(jnp.logical_not(live_block))
    def _():
        row = lax.broadcasted_iota(jnp.int32, stats_ref.shape, 2)
        stats_ref[...] = jnp.where(row == 0, -1e30, 0.0).astype(jnp.float32)
        value_ref[...] = jnp.zeros(value_ref.shape, jnp.float32)


def cache_attention(lengths, base, lat_hm, rope_hm, cache, value_hm):
    heads_here, total_tokens, _ = lat_hm.shape
    requests, cache_rows, width = cache.shape
    span = total_tokens // requests
    vdim = value_hm.shape[2]
    grid_spec = pltpu.PrefetchScalarGridSpec(
        num_scalar_prefetch=2,
        grid=(requests, heads_here),
        in_specs=[
            pl.BlockSpec((1, span, LAT), lambda r, h, lens, b: (h, r, 0)),
            pl.BlockSpec((1, span, ROPE), lambda r, h, lens, b: (h, r, 0)),
            pl.BlockSpec((1, cache_rows, width), lambda r, h, lens, b: (r, 0, 0)),
            pl.BlockSpec((1, LAT, vdim), lambda r, h, lens, b: (h, 0, 0)),
        ],
        out_specs=[
            pl.BlockSpec((1, 1, 8, span), lambda r, h, lens, b: (h, r, 0, 0)),
            pl.BlockSpec((1, span, vdim), lambda r, h, lens, b: (h, r, 0)),
        ],
    )
    return pl.pallas_call(
        cache_kernel,
        grid_spec=grid_spec,
        out_shape=[
            jax.ShapeDtypeStruct((heads_here, requests, 8, span), jnp.float32),
            jax.ShapeDtypeStruct((heads_here, total_tokens, vdim), jnp.float32),
        ],
        compiler_params=pltpu.CompilerParams(dimension_semantics=("arbitrary", "arbitrary")),
    )(lengths, base, lat_hm, rope_hm, cache, value_hm)


def merge_parts(first, second):
    joint_peak = jnp.maximum(first[0], second[0])
    first_factor = jnp.exp(first[0] - joint_peak)
    second_factor = jnp.exp(second[0] - joint_peak)
    joint_total = first_factor * first[1] + second_factor * second[1]
    joint_value = first_factor[..., None] * first[2] + second_factor[..., None] * second[2]
    return (joint_peak, joint_total, joint_value)


def per_device(
    hidden, attn_gain, q_weight, kva_weight, kv_gain, kvb_weight, o_weight, cache, lengths
):
    wide_count = lax.axis_size("wide")
    wide_place = lax.axis_index("wide")
    tok_rows = hidden.shape[0]
    requests = lengths.shape[0]
    cache_rows = cache.shape[1]
    heads_here = q_weight.shape[1] // (NOPE + ROPE)
    narrow_count = lax.axis_size("narrow")
    narrow_place = lax.axis_index("narrow")
    q_cols = q_weight.shape[1]
    kva_cols = kva_weight.shape[1]
    kva_part = kva_cols // narrow_count
    kva_mine = lax.dynamic_slice_in_dim(kva_weight, narrow_place * kva_part, kva_part, 1)
    packed = jnp.concatenate([q_weight, kva_mine], axis=1)
    got_weights = gather_axis(packed, "wide")
    proj_full = got_weights.reshape(-1, q_cols + kva_part)
    kvb_full = gather_axis(kvb_weight, "wide").reshape(-1, kvb_weight.shape[1])
    o_got = lax.all_gather(o_weight, "wide", axis=0, tiled=False)

    normed = scaled_norm(hidden.astype(jnp.float32), attn_gain).astype(jnp.bfloat16)
    projected = jnp.dot(normed, proj_full, preferred_element_type=jnp.float32)
    query_rows = projected[:, :q_cols].astype(jnp.bfloat16)
    compressed_part = projected[:, q_cols:]
    first_token = wide_place * tok_rows
    token_ids = first_token + jnp.arange(tok_rows, dtype=jnp.int32)
    positions = lengths[token_ids // SPAN] + token_ids % SPAN

    query_heads = query_rows.reshape(tok_rows, heads_here, NOPE + ROPE)
    own_rope_q = rotate(query_heads[..., NOPE:].astype(jnp.float32), positions[:, None]).astype(
        jnp.bfloat16
    )
    outgoing = jnp.concatenate(
        [
            query_heads[..., :NOPE].reshape(tok_rows, heads_here * NOPE),
            own_rope_q.reshape(tok_rows, heads_here * ROPE),
        ],
        axis=1,
    )
    raw_all = gather_axis(outgoing, "wide")
    compressed_part, raw_all = lax.optimization_barrier((compressed_part, raw_all))
    compressed = jnp.transpose(gather_axis(compressed_part, "narrow"), (1, 0, 2)).reshape(
        tok_rows, kva_cols
    )
    own_keys = jnp.concatenate(
        [
            scaled_norm(compressed[:, :LAT], kv_gain).astype(jnp.bfloat16),
            rotate(compressed[:, LAT:], positions).astype(jnp.bfloat16),
        ],
        axis=1,
    )
    total_tokens = raw_all.shape[0] * tok_rows
    raw_all = raw_all.reshape(total_tokens, heads_here * (NOPE + ROPE))
    kvb_heads = kvb_full.reshape(LAT, heads_here, NOPE + VDIM)
    key_maps = kvb_heads[..., :NOPE]
    value_maps = kvb_heads[..., NOPE:]
    nope_all = raw_all[:, : heads_here * NOPE].reshape(total_tokens, heads_here, NOPE)
    rope_all = raw_all[:, heads_here * NOPE :].reshape(total_tokens, heads_here, ROPE)
    lat_hm = jnp.einsum(
        "thc,lhc->htl", nope_all, key_maps, preferred_element_type=jnp.float32
    ).astype(jnp.bfloat16)
    rope_hm = jnp.transpose(rope_all, (1, 0, 2))
    value_hm = jnp.transpose(value_maps, (1, 0, 2))

    base = (wide_place * cache_rows).reshape(1).astype(jnp.int32)
    stats_hm, value_out = cache_attention(lengths, base, lat_hm, rope_hm, cache, value_hm)
    peak_hm = stats_hm[:, :, 0].reshape(heads_here, total_tokens)
    total_hm = stats_hm[:, :, 1].reshape(heads_here, total_tokens)

    own_request = first_token // SPAN
    start_row = own_request * SPAN
    own_slots = first_token % SPAN + jnp.arange(tok_rows, dtype=jnp.int32)
    causal = own_slots[None, :] <= jnp.arange(SPAN, dtype=jnp.int32)[:, None]
    own_lat = lax.dynamic_slice_in_dim(lat_hm, start_row, SPAN, 1)
    own_rope = lax.dynamic_slice_in_dim(rope_hm, start_row, SPAN, 1)
    own_scores = (
        jnp.einsum("hqc,kc->hqk", own_lat, own_keys[:, :LAT], preferred_element_type=jnp.float32)
        + jnp.einsum("hqc,kc->hqk", own_rope, own_keys[:, LAT:], preferred_element_type=jnp.float32)
    ) * score_scale
    own_live = causal[None]
    own_peak = jnp.max(jnp.where(own_live, own_scores, -1e30), axis=-1)
    own_weights = jnp.where(own_live, jnp.exp(own_scores - own_peak[..., None]), 0.0)
    own_total = jnp.sum(own_weights, axis=-1)
    own_mixed = jnp.einsum(
        "hqk,kc->hqc", own_weights.astype(jnp.bfloat16), own_keys[:, :LAT],
        preferred_element_type=jnp.float32,
    )
    own_upper = own_mixed.astype(jnp.bfloat16)
    own_lower = (own_mixed - own_upper.astype(jnp.float32)).astype(jnp.bfloat16)
    own_value = jnp.einsum(
        "hqc,hcv->hqv", own_upper, value_hm, preferred_element_type=jnp.float32
    ) + jnp.einsum("hqc,hcv->hqv", own_lower, value_hm, preferred_element_type=jnp.float32)
    old_part = (
        lax.dynamic_slice_in_dim(peak_hm, start_row, SPAN, 1),
        lax.dynamic_slice_in_dim(total_hm, start_row, SPAN, 1),
        lax.dynamic_slice_in_dim(value_out, start_row, SPAN, 1),
    )
    joint = merge_parts(old_part, (own_peak, own_total, own_value))
    peak_hm = lax.dynamic_update_slice_in_dim(peak_hm, joint[0], start_row, 1)
    total_hm = lax.dynamic_update_slice_in_dim(total_hm, joint[1], start_row, 1)
    value_out = lax.dynamic_update_slice_in_dim(value_out, joint[2], start_row, 1)

    stats = jnp.stack([peak_hm, total_hm], axis=0).astype(jnp.bfloat16)
    got_stats = lax.all_to_all(
        stats.reshape(2, heads_here, wide_count, tok_rows), "wide", 2, 2, tiled=True
    ).astype(jnp.float32)
    got_value = lax.all_to_all(
        value_out.astype(jnp.bfloat16).reshape(heads_here, wide_count, tok_rows, VDIM),
        "wide",
        1,
        1,
        tiled=True,
    ).astype(jnp.float32)
    got_peak = got_stats[0]
    got_total = got_stats[1]
    peak_value = jnp.max(got_peak, axis=1)
    factor = jnp.exp(got_peak - peak_value[:, None])
    denominator = jnp.sum(factor * got_total, axis=1)
    numerator = jnp.sum(factor[..., None] * got_value, axis=1)
    context = jnp.transpose(
        (numerator / denominator[..., None]).astype(jnp.bfloat16), (1, 0, 2)
    ).reshape(tok_rows, heads_here * VDIM)
    partial_out = jnp.einsum(
        "tk,wkc->twc", context, o_got, preferred_element_type=jnp.float32
    ).reshape(tok_rows, -1)
    got_parts = gather_axis(partial_out.astype(jnp.bfloat16), "narrow")
    return jnp.sum(got_parts.astype(jnp.float32), axis=0).astype(jnp.bfloat16)


def solution(mesh):
    in_specs = (
        P("wide", None),
        P(),
        P("wide", "narrow"),
        P("wide", None),
        P(),
        P("wide", "narrow"),
        P("narrow", "wide"),
        P(None, "wide", None),
        P(),
    )
    out_specs = P("wide", None)
    return jax.shard_map(
        per_device, mesh=mesh, in_specs=in_specs, out_specs=out_specs, check_vma=False
    )
```

```python
import jax
import jax.numpy as jnp
from jax import lax
from jax.sharding import PartitionSpec as P
from jax.experimental import pallas as pl
from jax.experimental.pallas import tpu as pltpu

NOPE = 128
ROPE = 64
VDIM = 128
LAT = 512
SPAN = 512


eps = 1e-06
score_scale = 1.0 / 13.856406460551018


def rotate(values, positions):
    half_size = values.shape[-1] // 2
    frequency = 10000.0 ** (-jnp.arange(half_size, dtype=jnp.float32) / half_size)
    angles = positions.astype(jnp.float32)[..., None] * frequency
    lower_half = values[..., :half_size]
    upper_half = values[..., half_size:]
    cosine = jnp.cos(angles)
    sine_part = jnp.sin(angles)
    return jnp.concatenate(
        [
            lower_half * cosine - upper_half * sine_part,
            lower_half * sine_part + upper_half * cosine,
        ],
        axis=-1,
    )


def scaled_norm(values, gain):
    return (
        values
        * lax.rsqrt(jnp.mean(values * values, axis=-1, keepdims=True) + eps)
        * gain.astype(jnp.float32)
    )


def gather_axis(x, axis_name):
    count = lax.axis_size(axis_name)
    spread = jnp.broadcast_to(x[None], (count,) + x.shape)
    return lax.all_to_all(spread, axis_name, split_axis=0, concat_axis=0, tiled=True)


def absorb(nope_part, key_maps):
    return jnp.einsum(
        "thc,lhc->thl", nope_part, key_maps, preferred_element_type=jnp.float32
    ).astype(jnp.bfloat16)


def project_values(mixed, value_maps):
    upper_part = mixed.astype(jnp.bfloat16)
    lower_part = (mixed - upper_part.astype(jnp.float32)).astype(jnp.bfloat16)
    first_term = jnp.einsum(
        "qhc,chv->qhv", upper_part, value_maps, preferred_element_type=jnp.float32
    )
    second_term = jnp.einsum(
        "qhc,chv->qhv", lower_part, value_maps, preferred_element_type=jnp.float32
    )
    return first_term + second_term


def attend(block_queries, key_rows, live_mask, value_maps):
    scores = (
        jnp.einsum("qhc,kc->qhk", block_queries, key_rows, preferred_element_type=jnp.float32)
        * score_scale
    )
    live_rows = live_mask[:, None, :]
    row_peak = jnp.max(jnp.where(live_rows, scores, -1e30), axis=-1)
    weights = jnp.where(live_rows, jnp.exp(scores - row_peak[..., None]), 0.0)
    row_total = jnp.sum(weights, axis=-1)
    mixed = jnp.einsum(
        "qhk,kc->qhc",
        weights.astype(jnp.bfloat16),
        key_rows[:, :LAT],
        preferred_element_type=jnp.float32,
    )
    return (row_peak, row_total, project_values(mixed, value_maps))


def skipped(block_queries, key_rows, live_mask, value_maps):
    rows_here = block_queries.shape[0]
    heads_here = block_queries.shape[1]
    return (
        jnp.full((rows_here, heads_here), -1e30, jnp.float32),
        jnp.zeros((rows_here, heads_here), jnp.float32),
        jnp.zeros((rows_here, heads_here, value_maps.shape[2]), jnp.float32),
    )


def cache_kernel(lens_ref, base_ref, lat_ref, rope_ref, kv_ref, vm_ref, stats_ref, value_ref):
    length_now = lens_ref[pl.program_id(0)]
    base = base_ref[0]
    live_block = base < length_now

    @pl.when(live_block)
    def _():
        keys = kv_ref[0]
        key_lat = keys[:, :LAT]
        key_rope = keys[:, LAT:]
        nt = (((1,), (1,)), ((), ()))
        scores = (
            lax.dot_general(lat_ref[0], key_lat, nt, preferred_element_type=jnp.float32)
            + lax.dot_general(rope_ref[0], key_rope, nt, preferred_element_type=jnp.float32)
        ) * score_scale
        slots = base + lax.broadcasted_iota(jnp.int32, scores.shape, 1)
        live = slots < length_now
        peak = jnp.max(jnp.where(live, scores, -1e30), axis=-1, keepdims=True)
        weights = jnp.where(live, jnp.exp(scores - peak), 0.0)
        total = jnp.sum(weights, axis=-1, keepdims=True)
        lane = lax.broadcasted_iota(jnp.int32, (peak.shape[0], 128), 1)
        packed = jnp.where(lane == 0, peak, jnp.where(lane == 1, total, 0.0))
        stats_ref[0, 0] = jnp.transpose(packed)[: stats_ref.shape[2]]
        mixed = jnp.dot(weights.astype(jnp.bfloat16), key_lat, preferred_element_type=jnp.float32)
        value_map = vm_ref[0]
        upper_part = mixed.astype(jnp.bfloat16)
        lower_part = (mixed - upper_part.astype(jnp.float32)).astype(jnp.bfloat16)
        value_ref[0] = jnp.dot(upper_part, value_map, preferred_element_type=jnp.float32) + jnp.dot(
            lower_part, value_map, preferred_element_type=jnp.float32
        )

    @pl.when(jnp.logical_not(live_block))
    def _():
        row = lax.broadcasted_iota(jnp.int32, stats_ref.shape, 2)
        stats_ref[...] = jnp.where(row == 0, -1e30, 0.0).astype(jnp.float32)
        value_ref[...] = jnp.zeros(value_ref.shape, jnp.float32)


def cache_attention(lengths, base, lat_hm, rope_hm, cache, value_hm):
    heads_here, total_tokens, _ = lat_hm.shape
    requests, cache_rows, width = cache.shape
    span = total_tokens // requests
    vdim = value_hm.shape[2]
    grid_spec = pltpu.PrefetchScalarGridSpec(
        num_scalar_prefetch=2,
        grid=(requests, heads_here),
        in_specs=[
            pl.BlockSpec((1, span, LAT), lambda r, h, lens, b: (h, r, 0)),
            pl.BlockSpec((1, span, ROPE), lambda r, h, lens, b: (h, r, 0)),
            pl.BlockSpec((1, cache_rows, width), lambda r, h, lens, b: (r, 0, 0)),
            pl.BlockSpec((1, LAT, vdim), lambda r, h, lens, b: (h, 0, 0)),
        ],
        out_specs=[
            pl.BlockSpec((1, 1, 8, span), lambda r, h, lens, b: (h, r, 0, 0)),
            pl.BlockSpec((1, span, vdim), lambda r, h, lens, b: (h, r, 0)),
        ],
    )
    return pl.pallas_call(
        cache_kernel,
        grid_spec=grid_spec,
        out_shape=[
            jax.ShapeDtypeStruct((heads_here, requests, 8, span), jnp.float32),
            jax.ShapeDtypeStruct((heads_here, total_tokens, vdim), jnp.float32),
        ],
        compiler_params=pltpu.CompilerParams(dimension_semantics=("arbitrary", "arbitrary")),
    )(lengths, base, lat_hm, rope_hm, cache, value_hm)


def merge_parts(first, second):
    joint_peak = jnp.maximum(first[0], second[0])
    first_factor = jnp.exp(first[0] - joint_peak)
    second_factor = jnp.exp(second[0] - joint_peak)
    joint_total = first_factor * first[1] + second_factor * second[1]
    joint_value = first_factor[..., None] * first[2] + second_factor[..., None] * second[2]
    return (joint_peak, joint_total, joint_value)


def per_device(
    hidden, attn_gain, q_weight, kva_weight, kv_gain, kvb_weight, o_weight, cache, lengths
):
    wide_count = lax.axis_size("wide")
    wide_place = lax.axis_index("wide")
    tok_rows = hidden.shape[0]
    requests = lengths.shape[0]
    cache_rows = cache.shape[1]
    heads_here = q_weight.shape[1] // (NOPE + ROPE)
    narrow_count = lax.axis_size("narrow")
    narrow_place = lax.axis_index("narrow")
    q_cols = q_weight.shape[1]
    kva_cols = kva_weight.shape[1]
    kva_part = kva_cols // narrow_count
    kva_mine = lax.dynamic_slice_in_dim(kva_weight, narrow_place * kva_part, kva_part, 1)
    packed = jnp.concatenate([q_weight, kva_mine], axis=1)
    got_weights = gather_axis(packed, "wide")
    proj_full = got_weights.reshape(-1, q_cols + kva_part)
    kvb_full = gather_axis(kvb_weight, "wide").reshape(-1, kvb_weight.shape[1])
    o_got = lax.all_gather(o_weight, "wide", axis=0, tiled=False)

    normed = scaled_norm(hidden.astype(jnp.float32), attn_gain).astype(jnp.bfloat16)
    projected = jnp.dot(normed, proj_full, preferred_element_type=jnp.float32)
    query_rows = projected[:, :q_cols].astype(jnp.bfloat16)
    compressed_part = projected[:, q_cols:]
    first_token = wide_place * tok_rows
    token_ids = first_token + jnp.arange(tok_rows, dtype=jnp.int32)
    positions = lengths[token_ids // SPAN] + token_ids % SPAN

    query_heads = query_rows.reshape(tok_rows, heads_here, NOPE + ROPE)
    own_rope_q = rotate(query_heads[..., NOPE:].astype(jnp.float32), positions[:, None]).astype(
        jnp.bfloat16
    )
    outgoing = jnp.concatenate(
        [
            query_heads[..., :NOPE].reshape(tok_rows, heads_here * NOPE),
            own_rope_q.reshape(tok_rows, heads_here * ROPE),
        ],
        axis=1,
    )
    raw_all = gather_axis(outgoing, "wide")
    compressed_part, raw_all = lax.optimization_barrier((compressed_part, raw_all))
    compressed = jnp.transpose(gather_axis(compressed_part, "narrow"), (1, 0, 2)).reshape(
        tok_rows, kva_cols
    )
    own_keys = jnp.concatenate(
        [
            scaled_norm(compressed[:, :LAT], kv_gain).astype(jnp.bfloat16),
            rotate(compressed[:, LAT:], positions).astype(jnp.bfloat16),
        ],
        axis=1,
    )
    total_tokens = raw_all.shape[0] * tok_rows
    raw_all = raw_all.reshape(total_tokens, heads_here * (NOPE + ROPE))
    kvb_heads = kvb_full.reshape(LAT, heads_here, NOPE + VDIM)
    key_maps = kvb_heads[..., :NOPE]
    value_maps = kvb_heads[..., NOPE:]
    nope_all = raw_all[:, : heads_here * NOPE].reshape(total_tokens, heads_here, NOPE)
    rope_all = raw_all[:, heads_here * NOPE :].reshape(total_tokens, heads_here, ROPE)
    lat_hm = jnp.einsum(
        "thc,lhc->htl", nope_all, key_maps, preferred_element_type=jnp.float32
    ).astype(jnp.bfloat16)
    rope_hm = jnp.transpose(rope_all, (1, 0, 2))
    value_hm = jnp.transpose(value_maps, (1, 0, 2))

    base = (wide_place * cache_rows).reshape(1).astype(jnp.int32)
    stats_hm, value_out = cache_attention(lengths, base, lat_hm, rope_hm, cache, value_hm)
    peak_hm = stats_hm[:, :, 0].reshape(heads_here, total_tokens)
    total_hm = stats_hm[:, :, 1].reshape(heads_here, total_tokens)

    own_request = first_token // SPAN
    start_row = own_request * SPAN
    own_slots = first_token % SPAN + jnp.arange(tok_rows, dtype=jnp.int32)
    causal = own_slots[None, :] <= jnp.arange(SPAN, dtype=jnp.int32)[:, None]
    own_lat = lax.dynamic_slice_in_dim(lat_hm, start_row, SPAN, 1)
    own_rope = lax.dynamic_slice_in_dim(rope_hm, start_row, SPAN, 1)
    own_scores = (
        jnp.einsum("hqc,kc->hqk", own_lat, own_keys[:, :LAT], preferred_element_type=jnp.float32)
        + jnp.einsum("hqc,kc->hqk", own_rope, own_keys[:, LAT:], preferred_element_type=jnp.float32)
    ) * score_scale
    own_live = causal[None]
    own_peak = jnp.max(jnp.where(own_live, own_scores, -1e30), axis=-1)
    own_weights = jnp.where(own_live, jnp.exp(own_scores - own_peak[..., None]), 0.0)
    own_total = jnp.sum(own_weights, axis=-1)
    own_mixed = jnp.einsum(
        "hqk,kc->hqc", own_weights.astype(jnp.bfloat16), own_keys[:, :LAT],
        preferred_element_type=jnp.float32,
    )
    own_upper = own_mixed.astype(jnp.bfloat16)
    own_lower = (own_mixed - own_upper.astype(jnp.float32)).astype(jnp.bfloat16)
    own_value = jnp.einsum(
        "hqc,hcv->hqv", own_upper, value_hm, preferred_element_type=jnp.float32
    ) + jnp.einsum("hqc,hcv->hqv", own_lower, value_hm, preferred_element_type=jnp.float32)
    old_part = (
        lax.dynamic_slice_in_dim(peak_hm, start_row, SPAN, 1),
        lax.dynamic_slice_in_dim(total_hm, start_row, SPAN, 1),
        lax.dynamic_slice_in_dim(value_out, start_row, SPAN, 1),
    )
    joint = merge_parts(old_part, (own_peak, own_total, own_value))
    peak_hm = lax.dynamic_update_slice_in_dim(peak_hm, joint[0], start_row, 1)
    total_hm = lax.dynamic_update_slice_in_dim(total_hm, joint[1], start_row, 1)
    value_out = lax.dynamic_update_slice_in_dim(value_out, joint[2], start_row, 1)

    stats = jnp.stack(
        [peak_hm.reshape(heads_here, wide_count, tok_rows), total_hm.reshape(heads_here, wide_count, tok_rows)],
        axis=2,
    )
    sending = jnp.concatenate(
        [value_out.reshape(heads_here, wide_count, tok_rows, VDIM), stats], axis=2
    ).astype(jnp.bfloat16)
    got_all = lax.all_to_all(sending, "wide", 1, 1, tiled=True).astype(jnp.float32)
    got_value = got_all[:, :, :tok_rows, :]
    got_peak = got_all[:, :, tok_rows, :]
    got_total = got_all[:, :, tok_rows + 1, :]
    peak_value = jnp.max(got_peak, axis=1)
    factor = jnp.exp(got_peak - peak_value[:, None])
    denominator = jnp.sum(factor * got_total, axis=1)
    numerator = jnp.sum(factor[..., None] * got_value, axis=1)
    context = jnp.transpose(
        (numerator / denominator[..., None]).astype(jnp.bfloat16), (1, 0, 2)
    ).reshape(tok_rows, heads_here * VDIM)
    partial_out = jnp.einsum(
        "tk,wkc->twc", context, o_got, preferred_element_type=jnp.float32
    ).reshape(tok_rows, -1)
    out_cols = partial_out.shape[1]
    pieces = jnp.transpose(
        partial_out.astype(jnp.bfloat16).reshape(tok_rows, narrow_count, out_cols // narrow_count),
        (1, 0, 2),
    )
    got_pieces = lax.all_to_all(pieces, "narrow", 0, 0, tiled=True)
    mine = jnp.sum(got_pieces.astype(jnp.float32), axis=0).astype(jnp.bfloat16)
    all_pieces = gather_axis(mine, "narrow")
    return jnp.transpose(all_pieces, (1, 0, 2)).reshape(tok_rows, out_cols)


def solution(mesh):
    in_specs = (
        P("wide", None),
        P(),
        P("wide", "narrow"),
        P("wide", None),
        P(),
        P("wide", "narrow"),
        P("narrow", "wide"),
        P(None, "wide", None),
        P(),
    )
    out_specs = P("wide", None)
    return jax.shard_map(
        per_device, mesh=mesh, in_specs=in_specs, out_specs=out_specs, check_vma=False
    )
```

```python
import jax
import jax.numpy as jnp
from jax import lax
from jax.sharding import PartitionSpec as P
from jax.experimental import pallas as pl
from jax.experimental.pallas import tpu as pltpu

NOPE = 128
ROPE = 64
VDIM = 128
LAT = 512
SPAN = 512


eps = 1e-06
score_scale = 1.0 / 13.856406460551018


def rotate(values, positions):
    half_size = values.shape[-1] // 2
    frequency = 10000.0 ** (-jnp.arange(half_size, dtype=jnp.float32) / half_size)
    angles = positions.astype(jnp.float32)[..., None] * frequency
    lower_half = values[..., :half_size]
    upper_half = values[..., half_size:]
    cosine = jnp.cos(angles)
    sine_part = jnp.sin(angles)
    return jnp.concatenate(
        [
            lower_half * cosine - upper_half * sine_part,
            lower_half * sine_part + upper_half * cosine,
        ],
        axis=-1,
    )


def scaled_norm(values, gain):
    return (
        values
        * lax.rsqrt(jnp.mean(values * values, axis=-1, keepdims=True) + eps)
        * gain.astype(jnp.float32)
    )


def gather_axis(x, axis_name):
    count = lax.axis_size(axis_name)
    spread = jnp.broadcast_to(x[None], (count,) + x.shape)
    return lax.all_to_all(spread, axis_name, split_axis=0, concat_axis=0, tiled=True)


def absorb(nope_part, key_maps):
    return jnp.einsum(
        "thc,lhc->thl", nope_part, key_maps, preferred_element_type=jnp.float32
    ).astype(jnp.bfloat16)


def project_values(mixed, value_maps):
    upper_part = mixed.astype(jnp.bfloat16)
    lower_part = (mixed - upper_part.astype(jnp.float32)).astype(jnp.bfloat16)
    first_term = jnp.einsum(
        "qhc,chv->qhv", upper_part, value_maps, preferred_element_type=jnp.float32
    )
    second_term = jnp.einsum(
        "qhc,chv->qhv", lower_part, value_maps, preferred_element_type=jnp.float32
    )
    return first_term + second_term


def attend(block_queries, key_rows, live_mask, value_maps):
    scores = (
        jnp.einsum("qhc,kc->qhk", block_queries, key_rows, preferred_element_type=jnp.float32)
        * score_scale
    )
    live_rows = live_mask[:, None, :]
    row_peak = jnp.max(jnp.where(live_rows, scores, -1e30), axis=-1)
    weights = jnp.where(live_rows, jnp.exp(scores - row_peak[..., None]), 0.0)
    row_total = jnp.sum(weights, axis=-1)
    mixed = jnp.einsum(
        "qhk,kc->qhc",
        weights.astype(jnp.bfloat16),
        key_rows[:, :LAT],
        preferred_element_type=jnp.float32,
    )
    return (row_peak, row_total, project_values(mixed, value_maps))


def skipped(block_queries, key_rows, live_mask, value_maps):
    rows_here = block_queries.shape[0]
    heads_here = block_queries.shape[1]
    return (
        jnp.full((rows_here, heads_here), -1e30, jnp.float32),
        jnp.zeros((rows_here, heads_here), jnp.float32),
        jnp.zeros((rows_here, heads_here, value_maps.shape[2]), jnp.float32),
    )


def cache_kernel(lens_ref, base_ref, lat_ref, rope_ref, kv_ref, vm_ref, stats_ref, value_ref):
    length_now = lens_ref[pl.program_id(0)]
    base = base_ref[0]
    live_block = base < length_now

    @pl.when(live_block)
    def _():
        keys = kv_ref[0]
        key_lat = keys[:, :LAT]
        key_rope = keys[:, LAT:]
        nt = (((1,), (1,)), ((), ()))
        scores = (
            lax.dot_general(lat_ref[0], key_lat, nt, preferred_element_type=jnp.float32)
            + lax.dot_general(rope_ref[0], key_rope, nt, preferred_element_type=jnp.float32)
        ) * score_scale
        slots = base + lax.broadcasted_iota(jnp.int32, scores.shape, 1)
        live = slots < length_now
        peak = jnp.max(jnp.where(live, scores, -1e30), axis=-1, keepdims=True)
        weights = jnp.where(live, jnp.exp(scores - peak), 0.0)
        total = jnp.sum(weights, axis=-1, keepdims=True)
        lane = lax.broadcasted_iota(jnp.int32, (peak.shape[0], 128), 1)
        packed = jnp.where(lane == 0, peak, jnp.where(lane == 1, total, 0.0))
        stats_ref[0, 0] = jnp.transpose(packed)[: stats_ref.shape[2]]
        mixed = jnp.dot(weights.astype(jnp.bfloat16), key_lat, preferred_element_type=jnp.float32)
        value_map = vm_ref[0]
        upper_part = mixed.astype(jnp.bfloat16)
        lower_part = (mixed - upper_part.astype(jnp.float32)).astype(jnp.bfloat16)
        value_ref[0] = jnp.dot(upper_part, value_map, preferred_element_type=jnp.float32) + jnp.dot(
            lower_part, value_map, preferred_element_type=jnp.float32
        )

    @pl.when(jnp.logical_not(live_block))
    def _():
        row = lax.broadcasted_iota(jnp.int32, stats_ref.shape, 2)
        stats_ref[...] = jnp.where(row == 0, -1e30, 0.0).astype(jnp.float32)
        value_ref[...] = jnp.zeros(value_ref.shape, jnp.float32)


def cache_attention(lengths, base, lat_hm, rope_hm, cache, value_hm):
    heads_here, total_tokens, _ = lat_hm.shape
    requests, cache_rows, width = cache.shape
    span = total_tokens // requests
    vdim = value_hm.shape[2]
    grid_spec = pltpu.PrefetchScalarGridSpec(
        num_scalar_prefetch=2,
        grid=(requests, heads_here),
        in_specs=[
            pl.BlockSpec((1, span, LAT), lambda r, h, lens, b: (h, r, 0)),
            pl.BlockSpec((1, span, ROPE), lambda r, h, lens, b: (h, r, 0)),
            pl.BlockSpec((1, cache_rows, width), lambda r, h, lens, b: (r, 0, 0)),
            pl.BlockSpec((1, LAT, vdim), lambda r, h, lens, b: (h, 0, 0)),
        ],
        out_specs=[
            pl.BlockSpec((1, 1, 8, span), lambda r, h, lens, b: (h, r, 0, 0)),
            pl.BlockSpec((1, span, vdim), lambda r, h, lens, b: (h, r, 0)),
        ],
    )
    return pl.pallas_call(
        cache_kernel,
        grid_spec=grid_spec,
        out_shape=[
            jax.ShapeDtypeStruct((heads_here, requests, 8, span), jnp.float32),
            jax.ShapeDtypeStruct((heads_here, total_tokens, vdim), jnp.float32),
        ],
        compiler_params=pltpu.CompilerParams(dimension_semantics=("arbitrary", "arbitrary")),
    )(lengths, base, lat_hm, rope_hm, cache, value_hm)


def merge_parts(first, second):
    joint_peak = jnp.maximum(first[0], second[0])
    first_factor = jnp.exp(first[0] - joint_peak)
    second_factor = jnp.exp(second[0] - joint_peak)
    joint_total = first_factor * first[1] + second_factor * second[1]
    joint_value = first_factor[..., None] * first[2] + second_factor[..., None] * second[2]
    return (joint_peak, joint_total, joint_value)


def per_device(
    hidden, attn_gain, q_weight, kva_weight, kv_gain, kvb_weight, o_weight, cache, lengths
):
    wide_count = lax.axis_size("wide")
    wide_place = lax.axis_index("wide")
    tok_rows = hidden.shape[0]
    requests = lengths.shape[0]
    cache_rows = cache.shape[1]
    heads_here = q_weight.shape[1] // (NOPE + ROPE)
    narrow_count = lax.axis_size("narrow")
    narrow_place = lax.axis_index("narrow")
    q_cols = q_weight.shape[1]
    kva_cols = kva_weight.shape[1]
    kva_part = kva_cols // narrow_count
    kva_mine = lax.dynamic_slice_in_dim(kva_weight, narrow_place * kva_part, kva_part, 1)
    packed = jnp.concatenate([q_weight, kva_mine], axis=1)
    got_weights = gather_axis(packed, "wide")
    proj_full = got_weights.reshape(-1, q_cols + kva_part)
    kvb_full = gather_axis(kvb_weight, "wide").reshape(-1, kvb_weight.shape[1])
    o_got = lax.all_gather(o_weight, "wide", axis=0, tiled=False)

    normed = scaled_norm(hidden.astype(jnp.float32), attn_gain).astype(jnp.bfloat16)
    projected = jnp.dot(normed, proj_full, preferred_element_type=jnp.float32)
    query_rows = projected[:, :q_cols].astype(jnp.bfloat16)
    compressed_part = projected[:, q_cols:]
    first_token = wide_place * tok_rows
    token_ids = first_token + jnp.arange(tok_rows, dtype=jnp.int32)
    positions = lengths[token_ids // SPAN] + token_ids % SPAN

    query_heads = query_rows.reshape(tok_rows, heads_here, NOPE + ROPE)
    own_rope_q = rotate(query_heads[..., NOPE:].astype(jnp.float32), positions[:, None]).astype(
        jnp.bfloat16
    )
    outgoing = jnp.concatenate(
        [
            query_heads[..., :NOPE].reshape(tok_rows, heads_here * NOPE),
            own_rope_q.reshape(tok_rows, heads_here * ROPE),
        ],
        axis=1,
    )
    raw_all = gather_axis(outgoing, "wide")
    compressed_part, raw_all = lax.optimization_barrier((compressed_part, raw_all))
    compressed = jnp.transpose(gather_axis(compressed_part, "narrow"), (1, 0, 2)).reshape(
        tok_rows, kva_cols
    )
    own_keys = jnp.concatenate(
        [
            scaled_norm(compressed[:, :LAT], kv_gain).astype(jnp.bfloat16),
            rotate(compressed[:, LAT:], positions).astype(jnp.bfloat16),
        ],
        axis=1,
    )
    total_tokens = raw_all.shape[0] * tok_rows
    raw_all = raw_all.reshape(total_tokens, heads_here * (NOPE + ROPE))
    kvb_heads = kvb_full.reshape(LAT, heads_here, NOPE + VDIM)
    key_maps = kvb_heads[..., :NOPE]
    value_maps = kvb_heads[..., NOPE:]
    nope_all = raw_all[:, : heads_here * NOPE].reshape(total_tokens, heads_here, NOPE)
    rope_all = raw_all[:, heads_here * NOPE :].reshape(total_tokens, heads_here, ROPE)
    lat_hm = jnp.einsum(
        "thc,lhc->htl", nope_all, key_maps, preferred_element_type=jnp.float32
    ).astype(jnp.bfloat16)
    rope_hm = jnp.transpose(rope_all, (1, 0, 2))
    value_hm = jnp.transpose(value_maps, (1, 0, 2))

    base = (wide_place * cache_rows).reshape(1).astype(jnp.int32)
    stats_hm, value_out = cache_attention(lengths, base, lat_hm, rope_hm, cache, value_hm)
    peak_hm = stats_hm[:, :, 0].reshape(heads_here, total_tokens)
    total_hm = stats_hm[:, :, 1].reshape(heads_here, total_tokens)

    own_request = first_token // SPAN
    start_row = own_request * SPAN
    own_slots = first_token % SPAN + jnp.arange(tok_rows, dtype=jnp.int32)
    causal = own_slots[None, :] <= jnp.arange(SPAN, dtype=jnp.int32)[:, None]
    own_lat = lax.dynamic_slice_in_dim(lat_hm, start_row, SPAN, 1)
    own_rope = lax.dynamic_slice_in_dim(rope_hm, start_row, SPAN, 1)
    own_scores = (
        jnp.einsum("hqc,kc->hqk", own_lat, own_keys[:, :LAT], preferred_element_type=jnp.float32)
        + jnp.einsum("hqc,kc->hqk", own_rope, own_keys[:, LAT:], preferred_element_type=jnp.float32)
    ) * score_scale
    own_live = causal[None]
    own_peak = jnp.max(jnp.where(own_live, own_scores, -1e30), axis=-1)
    own_weights = jnp.where(own_live, jnp.exp(own_scores - own_peak[..., None]), 0.0)
    own_total = jnp.sum(own_weights, axis=-1)
    own_mixed = jnp.einsum(
        "hqk,kc->hqc", own_weights.astype(jnp.bfloat16), own_keys[:, :LAT],
        preferred_element_type=jnp.float32,
    )
    own_upper = own_mixed.astype(jnp.bfloat16)
    own_lower = (own_mixed - own_upper.astype(jnp.float32)).astype(jnp.bfloat16)
    own_value = jnp.einsum(
        "hqc,hcv->hqv", own_upper, value_hm, preferred_element_type=jnp.float32
    ) + jnp.einsum("hqc,hcv->hqv", own_lower, value_hm, preferred_element_type=jnp.float32)
    old_part = (
        lax.dynamic_slice_in_dim(peak_hm, start_row, SPAN, 1),
        lax.dynamic_slice_in_dim(total_hm, start_row, SPAN, 1),
        lax.dynamic_slice_in_dim(value_out, start_row, SPAN, 1),
    )
    joint = merge_parts(old_part, (own_peak, own_total, own_value))
    peak_hm = lax.dynamic_update_slice_in_dim(peak_hm, joint[0], start_row, 1)
    total_hm = lax.dynamic_update_slice_in_dim(total_hm, joint[1], start_row, 1)
    value_out = lax.dynamic_update_slice_in_dim(value_out, joint[2], start_row, 1)

    stats = jnp.stack([peak_hm, total_hm], axis=0).astype(jnp.bfloat16)
    got_stats = lax.all_to_all(
        stats.reshape(2, heads_here, wide_count, tok_rows), "wide", 2, 2, tiled=True
    ).astype(jnp.float32)
    got_value = lax.all_to_all(
        value_out.astype(jnp.bfloat16).reshape(heads_here, wide_count, tok_rows, VDIM),
        "wide",
        1,
        1,
        tiled=True,
    ).astype(jnp.float32)
    got_peak = got_stats[0]
    got_total = got_stats[1]
    peak_value = jnp.max(got_peak, axis=1)
    factor = jnp.exp(got_peak - peak_value[:, None])
    denominator = jnp.sum(factor * got_total, axis=1)
    numerator = jnp.sum(factor[..., None] * got_value, axis=1)
    context = jnp.transpose(
        (numerator / denominator[..., None]).astype(jnp.bfloat16), (1, 0, 2)
    ).reshape(tok_rows, heads_here * VDIM)
    partial_out = jnp.einsum(
        "tk,wkc->twc", context, o_got, preferred_element_type=jnp.float32
    ).reshape(tok_rows, -1)
    out_cols = partial_out.shape[1]
    pieces = jnp.transpose(
        partial_out.astype(jnp.bfloat16).reshape(tok_rows, narrow_count, out_cols // narrow_count),
        (1, 0, 2),
    )
    got_pieces = lax.all_to_all(pieces, "narrow", 0, 0, tiled=True)
    mine = jnp.sum(got_pieces.astype(jnp.float32), axis=0).astype(jnp.bfloat16)
    all_pieces = gather_axis(mine, "narrow")
    return jnp.transpose(all_pieces, (1, 0, 2)).reshape(tok_rows, out_cols)


def solution(mesh):
    in_specs = (
        P("wide", None),
        P(),
        P("wide", "narrow"),
        P("wide", None),
        P(),
        P("wide", "narrow"),
        P("narrow", "wide"),
        P(None, "wide", None),
        P(),
    )
    out_specs = P("wide", None)
    return jax.shard_map(
        per_device, mesh=mesh, in_specs=in_specs, out_specs=out_specs, check_vma=False
    )
```

```python
import jax
import jax.numpy as jnp
from jax import lax
from jax.sharding import PartitionSpec as P
from jax.experimental import pallas as pl
from jax.experimental.pallas import tpu as pltpu

NOPE = 128
ROPE = 64
VDIM = 128
LAT = 512
SPAN = 512


eps = 1e-06
score_scale = 1.0 / 13.856406460551018


def rotate(values, positions):
    half_size = values.shape[-1] // 2
    frequency = 10000.0 ** (-jnp.arange(half_size, dtype=jnp.float32) / half_size)
    angles = positions.astype(jnp.float32)[..., None] * frequency
    lower_half = values[..., :half_size]
    upper_half = values[..., half_size:]
    cosine = jnp.cos(angles)
    sine_part = jnp.sin(angles)
    return jnp.concatenate(
        [
            lower_half * cosine - upper_half * sine_part,
            lower_half * sine_part + upper_half * cosine,
        ],
        axis=-1,
    )


def scaled_norm(values, gain):
    return (
        values
        * lax.rsqrt(jnp.mean(values * values, axis=-1, keepdims=True) + eps)
        * gain.astype(jnp.float32)
    )


def gather_axis(x, axis_name):
    count = lax.axis_size(axis_name)
    spread = jnp.broadcast_to(x[None], (count,) + x.shape)
    return lax.all_to_all(spread, axis_name, split_axis=0, concat_axis=0, tiled=True)


def absorb(nope_part, key_maps):
    return jnp.einsum(
        "thc,lhc->thl", nope_part, key_maps, preferred_element_type=jnp.float32
    ).astype(jnp.bfloat16)


def project_values(mixed, value_maps):
    upper_part = mixed.astype(jnp.bfloat16)
    lower_part = (mixed - upper_part.astype(jnp.float32)).astype(jnp.bfloat16)
    first_term = jnp.einsum(
        "qhc,chv->qhv", upper_part, value_maps, preferred_element_type=jnp.float32
    )
    second_term = jnp.einsum(
        "qhc,chv->qhv", lower_part, value_maps, preferred_element_type=jnp.float32
    )
    return first_term + second_term


def attend(block_queries, key_rows, live_mask, value_maps):
    scores = (
        jnp.einsum("qhc,kc->qhk", block_queries, key_rows, preferred_element_type=jnp.float32)
        * score_scale
    )
    live_rows = live_mask[:, None, :]
    row_peak = jnp.max(jnp.where(live_rows, scores, -1e30), axis=-1)
    weights = jnp.where(live_rows, jnp.exp(scores - row_peak[..., None]), 0.0)
    row_total = jnp.sum(weights, axis=-1)
    mixed = jnp.einsum(
        "qhk,kc->qhc",
        weights.astype(jnp.bfloat16),
        key_rows[:, :LAT],
        preferred_element_type=jnp.float32,
    )
    return (row_peak, row_total, project_values(mixed, value_maps))


def skipped(block_queries, key_rows, live_mask, value_maps):
    rows_here = block_queries.shape[0]
    heads_here = block_queries.shape[1]
    return (
        jnp.full((rows_here, heads_here), -1e30, jnp.float32),
        jnp.zeros((rows_here, heads_here), jnp.float32),
        jnp.zeros((rows_here, heads_here, value_maps.shape[2]), jnp.float32),
    )


def cache_kernel(lens_ref, base_ref, lat_ref, rope_ref, kv_ref, vm_ref, stats_ref, value_ref):
    length_now = lens_ref[pl.program_id(0)]
    base = base_ref[0]
    live_block = base < length_now

    @pl.when(live_block)
    def _():
        keys = kv_ref[0]
        key_lat = keys[:, :LAT]
        key_rope = keys[:, LAT:]
        nt = (((1,), (1,)), ((), ()))
        scores = (
            lax.dot_general(lat_ref[0], key_lat, nt, preferred_element_type=jnp.float32)
            + lax.dot_general(rope_ref[0], key_rope, nt, preferred_element_type=jnp.float32)
        ) * score_scale
        slots = base + lax.broadcasted_iota(jnp.int32, scores.shape, 1)
        live = slots < length_now
        peak = jnp.max(jnp.where(live, scores, -1e30), axis=-1, keepdims=True)
        weights = jnp.where(live, jnp.exp(scores - peak), 0.0)
        total = jnp.sum(weights, axis=-1, keepdims=True)
        lane = lax.broadcasted_iota(jnp.int32, (peak.shape[0], 128), 1)
        packed = jnp.where(lane == 0, peak, jnp.where(lane == 1, total, 0.0))
        stats_ref[0, 0] = jnp.transpose(packed)[: stats_ref.shape[2]]
        mixed = jnp.dot(weights.astype(jnp.bfloat16), key_lat, preferred_element_type=jnp.float32)
        value_map = vm_ref[0]
        upper_part = mixed.astype(jnp.bfloat16)
        lower_part = (mixed - upper_part.astype(jnp.float32)).astype(jnp.bfloat16)
        value_ref[0] = jnp.dot(upper_part, value_map, preferred_element_type=jnp.float32) + jnp.dot(
            lower_part, value_map, preferred_element_type=jnp.float32
        )

    @pl.when(jnp.logical_not(live_block))
    def _():
        row = lax.broadcasted_iota(jnp.int32, stats_ref.shape, 2)
        stats_ref[...] = jnp.where(row == 0, -1e30, 0.0).astype(jnp.float32)
        value_ref[...] = jnp.zeros(value_ref.shape, jnp.float32)


def cache_attention(lengths, base, lat_hm, rope_hm, cache, value_hm):
    heads_here, total_tokens, _ = lat_hm.shape
    requests, cache_rows, width = cache.shape
    span = total_tokens // requests
    vdim = value_hm.shape[2]
    grid_spec = pltpu.PrefetchScalarGridSpec(
        num_scalar_prefetch=2,
        grid=(requests, heads_here),
        in_specs=[
            pl.BlockSpec((1, span, LAT), lambda r, h, lens, b: (h, r, 0)),
            pl.BlockSpec((1, span, ROPE), lambda r, h, lens, b: (h, r, 0)),
            pl.BlockSpec((1, cache_rows, width), lambda r, h, lens, b: (r, 0, 0)),
            pl.BlockSpec((1, LAT, vdim), lambda r, h, lens, b: (h, 0, 0)),
        ],
        out_specs=[
            pl.BlockSpec((1, 1, 8, span), lambda r, h, lens, b: (h, r, 0, 0)),
            pl.BlockSpec((1, span, vdim), lambda r, h, lens, b: (h, r, 0)),
        ],
    )
    return pl.pallas_call(
        cache_kernel,
        grid_spec=grid_spec,
        out_shape=[
            jax.ShapeDtypeStruct((heads_here, requests, 8, span), jnp.float32),
            jax.ShapeDtypeStruct((heads_here, total_tokens, vdim), jnp.float32),
        ],
        compiler_params=pltpu.CompilerParams(dimension_semantics=("arbitrary", "arbitrary")),
    )(lengths, base, lat_hm, rope_hm, cache, value_hm)


def merge_parts(first, second):
    joint_peak = jnp.maximum(first[0], second[0])
    first_factor = jnp.exp(first[0] - joint_peak)
    second_factor = jnp.exp(second[0] - joint_peak)
    joint_total = first_factor * first[1] + second_factor * second[1]
    joint_value = first_factor[..., None] * first[2] + second_factor[..., None] * second[2]
    return (joint_peak, joint_total, joint_value)


def per_device(
    hidden, attn_gain, q_weight, kva_weight, kv_gain, kvb_weight, o_weight, cache, lengths
):
    wide_count = lax.axis_size("wide")
    wide_place = lax.axis_index("wide")
    tok_rows = hidden.shape[0]
    requests = lengths.shape[0]
    cache_rows = cache.shape[1]
    heads_here = q_weight.shape[1] // (NOPE + ROPE)
    narrow_count = lax.axis_size("narrow")
    narrow_place = lax.axis_index("narrow")
    q_cols = q_weight.shape[1]
    kva_cols = kva_weight.shape[1]
    kva_part = kva_cols // narrow_count
    kva_mine = lax.dynamic_slice_in_dim(kva_weight, narrow_place * kva_part, kva_part, 1)
    kvb_rows, kvb_cols = kvb_weight.shape
    w_rows = q_weight.shape[0]
    packed = jnp.concatenate(
        [q_weight, kva_mine, kvb_weight.reshape(w_rows, kvb_rows * kvb_cols // w_rows)], axis=1
    )
    got_weights = gather_axis(packed, "wide")
    proj_full = got_weights[:, :, : q_cols + kva_part].reshape(-1, q_cols + kva_part)
    kvb_full = got_weights[:, :, q_cols + kva_part :].reshape(-1, kvb_cols)
    o_got = lax.all_gather(o_weight, "wide", axis=0, tiled=False)

    normed = scaled_norm(hidden.astype(jnp.float32), attn_gain).astype(jnp.bfloat16)
    projected = jnp.dot(normed, proj_full, preferred_element_type=jnp.float32)
    query_rows = projected[:, :q_cols].astype(jnp.bfloat16)
    compressed_part = projected[:, q_cols:]
    first_token = wide_place * tok_rows
    token_ids = first_token + jnp.arange(tok_rows, dtype=jnp.int32)
    positions = lengths[token_ids // SPAN] + token_ids % SPAN

    query_heads = query_rows.reshape(tok_rows, heads_here, NOPE + ROPE)
    own_rope_q = rotate(query_heads[..., NOPE:].astype(jnp.float32), positions[:, None]).astype(
        jnp.bfloat16
    )
    outgoing = jnp.concatenate(
        [
            query_heads[..., :NOPE].reshape(tok_rows, heads_here * NOPE),
            own_rope_q.reshape(tok_rows, heads_here * ROPE),
        ],
        axis=1,
    )
    raw_all = gather_axis(outgoing, "wide")
    compressed_part, raw_all = lax.optimization_barrier((compressed_part, raw_all))
    compressed = jnp.transpose(gather_axis(compressed_part, "narrow"), (1, 0, 2)).reshape(
        tok_rows, kva_cols
    )
    own_keys = jnp.concatenate(
        [
            scaled_norm(compressed[:, :LAT], kv_gain).astype(jnp.bfloat16),
            rotate(compressed[:, LAT:], positions).astype(jnp.bfloat16),
        ],
        axis=1,
    )
    total_tokens = raw_all.shape[0] * tok_rows
    raw_all = raw_all.reshape(total_tokens, heads_here * (NOPE + ROPE))
    kvb_heads = kvb_full.reshape(LAT, heads_here, NOPE + VDIM)
    key_maps = kvb_heads[..., :NOPE]
    value_maps = kvb_heads[..., NOPE:]
    nope_all = raw_all[:, : heads_here * NOPE].reshape(total_tokens, heads_here, NOPE)
    rope_all = raw_all[:, heads_here * NOPE :].reshape(total_tokens, heads_here, ROPE)
    lat_hm = jnp.einsum(
        "thc,lhc->htl", nope_all, key_maps, preferred_element_type=jnp.float32
    ).astype(jnp.bfloat16)
    rope_hm = jnp.transpose(rope_all, (1, 0, 2))
    value_hm = jnp.transpose(value_maps, (1, 0, 2))

    base = (wide_place * cache_rows).reshape(1).astype(jnp.int32)
    stats_hm, value_out = cache_attention(lengths, base, lat_hm, rope_hm, cache, value_hm)
    peak_hm = stats_hm[:, :, 0].reshape(heads_here, total_tokens)
    total_hm = stats_hm[:, :, 1].reshape(heads_here, total_tokens)

    own_request = first_token // SPAN
    start_row = own_request * SPAN
    own_slots = first_token % SPAN + jnp.arange(tok_rows, dtype=jnp.int32)
    causal = own_slots[None, :] <= jnp.arange(SPAN, dtype=jnp.int32)[:, None]
    own_lat = lax.dynamic_slice_in_dim(lat_hm, start_row, SPAN, 1)
    own_rope = lax.dynamic_slice_in_dim(rope_hm, start_row, SPAN, 1)
    own_scores = (
        jnp.einsum("hqc,kc->hqk", own_lat, own_keys[:, :LAT], preferred_element_type=jnp.float32)
        + jnp.einsum("hqc,kc->hqk", own_rope, own_keys[:, LAT:], preferred_element_type=jnp.float32)
    ) * score_scale
    own_live = causal[None]
    own_peak = jnp.max(jnp.where(own_live, own_scores, -1e30), axis=-1)
    own_weights = jnp.where(own_live, jnp.exp(own_scores - own_peak[..., None]), 0.0)
    own_total = jnp.sum(own_weights, axis=-1)
    own_mixed = jnp.einsum(
        "hqk,kc->hqc", own_weights.astype(jnp.bfloat16), own_keys[:, :LAT],
        preferred_element_type=jnp.float32,
    )
    own_upper = own_mixed.astype(jnp.bfloat16)
    own_lower = (own_mixed - own_upper.astype(jnp.float32)).astype(jnp.bfloat16)
    own_value = jnp.einsum(
        "hqc,hcv->hqv", own_upper, value_hm, preferred_element_type=jnp.float32
    ) + jnp.einsum("hqc,hcv->hqv", own_lower, value_hm, preferred_element_type=jnp.float32)
    old_part = (
        lax.dynamic_slice_in_dim(peak_hm, start_row, SPAN, 1),
        lax.dynamic_slice_in_dim(total_hm, start_row, SPAN, 1),
        lax.dynamic_slice_in_dim(value_out, start_row, SPAN, 1),
    )
    joint = merge_parts(old_part, (own_peak, own_total, own_value))
    peak_hm = lax.dynamic_update_slice_in_dim(peak_hm, joint[0], start_row, 1)
    total_hm = lax.dynamic_update_slice_in_dim(total_hm, joint[1], start_row, 1)
    value_out = lax.dynamic_update_slice_in_dim(value_out, joint[2], start_row, 1)

    stats = jnp.stack([peak_hm, total_hm], axis=0).astype(jnp.bfloat16)
    got_stats = lax.all_to_all(
        stats.reshape(2, heads_here, wide_count, tok_rows), "wide", 2, 2, tiled=True
    ).astype(jnp.float32)
    got_value = lax.all_to_all(
        value_out.astype(jnp.bfloat16).reshape(heads_here, wide_count, tok_rows, VDIM),
        "wide",
        1,
        1,
        tiled=True,
    ).astype(jnp.float32)
    got_peak = got_stats[0]
    got_total = got_stats[1]
    peak_value = jnp.max(got_peak, axis=1)
    factor = jnp.exp(got_peak - peak_value[:, None])
    denominator = jnp.sum(factor * got_total, axis=1)
    numerator = jnp.sum(factor[..., None] * got_value, axis=1)
    context = jnp.transpose(
        (numerator / denominator[..., None]).astype(jnp.bfloat16), (1, 0, 2)
    ).reshape(tok_rows, heads_here * VDIM)
    partial_out = jnp.einsum(
        "tk,wkc->twc", context, o_got, preferred_element_type=jnp.float32
    ).reshape(tok_rows, -1)
    out_cols = partial_out.shape[1]
    pieces = jnp.transpose(
        partial_out.astype(jnp.bfloat16).reshape(tok_rows, narrow_count, out_cols // narrow_count),
        (1, 0, 2),
    )
    got_pieces = lax.all_to_all(pieces, "narrow", 0, 0, tiled=True)
    mine = jnp.sum(got_pieces.astype(jnp.float32), axis=0).astype(jnp.bfloat16)
    all_pieces = gather_axis(mine, "narrow")
    return jnp.transpose(all_pieces, (1, 0, 2)).reshape(tok_rows, out_cols)


def solution(mesh):
    in_specs = (
        P("wide", None),
        P(),
        P("wide", "narrow"),
        P("wide", None),
        P(),
        P("wide", "narrow"),
        P("narrow", "wide"),
        P(None, "wide", None),
        P(),
    )
    out_specs = P("wide", None)
    return jax.shard_map(
        per_device, mesh=mesh, in_specs=in_specs, out_specs=out_specs, check_vma=False
    )
```

```python
import jax
import jax.numpy as jnp
from jax import lax
from jax.sharding import PartitionSpec as P
from jax.experimental import pallas as pl
from jax.experimental.pallas import tpu as pltpu

NOPE = 128
ROPE = 64
VDIM = 128
LAT = 512
SPAN = 512
HEADS_PER_STEP = 2


eps = 1e-06
score_scale = 1.0 / 13.856406460551018


def rotate(values, positions):
    half_size = values.shape[-1] // 2
    frequency = 10000.0 ** (-jnp.arange(half_size, dtype=jnp.float32) / half_size)
    angles = positions.astype(jnp.float32)[..., None] * frequency
    lower_half = values[..., :half_size]
    upper_half = values[..., half_size:]
    cosine = jnp.cos(angles)
    sine_part = jnp.sin(angles)
    return jnp.concatenate(
        [
            lower_half * cosine - upper_half * sine_part,
            lower_half * sine_part + upper_half * cosine,
        ],
        axis=-1,
    )


def scaled_norm(values, gain):
    return (
        values
        * lax.rsqrt(jnp.mean(values * values, axis=-1, keepdims=True) + eps)
        * gain.astype(jnp.float32)
    )


def gather_axis(x, axis_name):
    count = lax.axis_size(axis_name)
    spread = jnp.broadcast_to(x[None], (count,) + x.shape)
    return lax.all_to_all(spread, axis_name, split_axis=0, concat_axis=0, tiled=True)


def absorb(nope_part, key_maps):
    return jnp.einsum(
        "thc,lhc->thl", nope_part, key_maps, preferred_element_type=jnp.float32
    ).astype(jnp.bfloat16)


def project_values(mixed, value_maps):
    upper_part = mixed.astype(jnp.bfloat16)
    lower_part = (mixed - upper_part.astype(jnp.float32)).astype(jnp.bfloat16)
    first_term = jnp.einsum(
        "qhc,chv->qhv", upper_part, value_maps, preferred_element_type=jnp.float32
    )
    second_term = jnp.einsum(
        "qhc,chv->qhv", lower_part, value_maps, preferred_element_type=jnp.float32
    )
    return first_term + second_term


def attend(block_queries, key_rows, live_mask, value_maps):
    scores = (
        jnp.einsum("qhc,kc->qhk", block_queries, key_rows, preferred_element_type=jnp.float32)
        * score_scale
    )
    live_rows = live_mask[:, None, :]
    row_peak = jnp.max(jnp.where(live_rows, scores, -1e30), axis=-1)
    weights = jnp.where(live_rows, jnp.exp(scores - row_peak[..., None]), 0.0)
    row_total = jnp.sum(weights, axis=-1)
    mixed = jnp.einsum(
        "qhk,kc->qhc",
        weights.astype(jnp.bfloat16),
        key_rows[:, :LAT],
        preferred_element_type=jnp.float32,
    )
    return (row_peak, row_total, project_values(mixed, value_maps))


def skipped(block_queries, key_rows, live_mask, value_maps):
    rows_here = block_queries.shape[0]
    heads_here = block_queries.shape[1]
    return (
        jnp.full((rows_here, heads_here), -1e30, jnp.float32),
        jnp.zeros((rows_here, heads_here), jnp.float32),
        jnp.zeros((rows_here, heads_here, value_maps.shape[2]), jnp.float32),
    )


def cache_kernel(lens_ref, base_ref, lat_ref, rope_ref, kv_ref, vm_ref, stats_ref, value_ref):
    length_now = lens_ref[pl.program_id(0)]
    base = base_ref[0]
    live_block = base < length_now

    def one_head(j):
        keys = kv_ref[0]
        key_lat = keys[:, :LAT]
        key_rope = keys[:, LAT:]
        nt = (((1,), (1,)), ((), ()))
        scores = (
            lax.dot_general(lat_ref[j], key_lat, nt, preferred_element_type=jnp.float32)
            + lax.dot_general(rope_ref[j], key_rope, nt, preferred_element_type=jnp.float32)
        ) * score_scale
        slots = base + lax.broadcasted_iota(jnp.int32, scores.shape, 1)
        live = slots < length_now
        peak = jnp.max(jnp.where(live, scores, -1e30), axis=-1, keepdims=True)
        weights = jnp.where(live, jnp.exp(scores - peak), 0.0)
        total = jnp.sum(weights, axis=-1, keepdims=True)
        lane = lax.broadcasted_iota(jnp.int32, (peak.shape[0], 128), 1)
        packed = jnp.where(lane == 0, peak, jnp.where(lane == 1, total, 0.0))
        stats_ref[j, 0] = jnp.transpose(packed)[: stats_ref.shape[2]]
        mixed = jnp.dot(weights.astype(jnp.bfloat16), key_lat, preferred_element_type=jnp.float32)
        value_map = vm_ref[j]
        upper_part = mixed.astype(jnp.bfloat16)
        lower_part = (mixed - upper_part.astype(jnp.float32)).astype(jnp.bfloat16)
        value_ref[j] = jnp.dot(upper_part, value_map, preferred_element_type=jnp.float32) + jnp.dot(
            lower_part, value_map, preferred_element_type=jnp.float32
        )

    @pl.when(live_block)
    def _():
        for j in range(lat_ref.shape[0]):
            one_head(j)

    @pl.when(jnp.logical_not(live_block))
    def _():
        row = lax.broadcasted_iota(jnp.int32, stats_ref.shape, 2)
        stats_ref[...] = jnp.where(row == 0, -1e30, 0.0).astype(jnp.float32)
        value_ref[...] = jnp.zeros(value_ref.shape, jnp.float32)


def cache_attention(lengths, base, lat_hm, rope_hm, cache, value_hm):
    heads_here, total_tokens, _ = lat_hm.shape
    requests, cache_rows, width = cache.shape
    span = total_tokens // requests
    vdim = value_hm.shape[2]
    grid_spec = pltpu.PrefetchScalarGridSpec(
        num_scalar_prefetch=2,
        grid=(requests, heads_here // HEADS_PER_STEP),
        in_specs=[
            pl.BlockSpec((HEADS_PER_STEP, span, LAT), lambda r, h, lens, b: (h, r, 0)),
            pl.BlockSpec((HEADS_PER_STEP, span, ROPE), lambda r, h, lens, b: (h, r, 0)),
            pl.BlockSpec((1, cache_rows, width), lambda r, h, lens, b: (r, 0, 0)),
            pl.BlockSpec((HEADS_PER_STEP, LAT, vdim), lambda r, h, lens, b: (h, 0, 0)),
        ],
        out_specs=[
            pl.BlockSpec((HEADS_PER_STEP, 1, 8, span), lambda r, h, lens, b: (h, r, 0, 0)),
            pl.BlockSpec((HEADS_PER_STEP, span, vdim), lambda r, h, lens, b: (h, r, 0)),
        ],
    )
    return pl.pallas_call(
        cache_kernel,
        grid_spec=grid_spec,
        out_shape=[
            jax.ShapeDtypeStruct((heads_here, requests, 8, span), jnp.float32),
            jax.ShapeDtypeStruct((heads_here, total_tokens, vdim), jnp.float32),
        ],
        compiler_params=pltpu.CompilerParams(dimension_semantics=("arbitrary", "arbitrary")),
    )(lengths, base, lat_hm, rope_hm, cache, value_hm)


def merge_parts(first, second):
    joint_peak = jnp.maximum(first[0], second[0])
    first_factor = jnp.exp(first[0] - joint_peak)
    second_factor = jnp.exp(second[0] - joint_peak)
    joint_total = first_factor * first[1] + second_factor * second[1]
    joint_value = first_factor[..., None] * first[2] + second_factor[..., None] * second[2]
    return (joint_peak, joint_total, joint_value)


def per_device(
    hidden, attn_gain, q_weight, kva_weight, kv_gain, kvb_weight, o_weight, cache, lengths
):
    wide_count = lax.axis_size("wide")
    wide_place = lax.axis_index("wide")
    tok_rows = hidden.shape[0]
    requests = lengths.shape[0]
    cache_rows = cache.shape[1]
    heads_here = q_weight.shape[1] // (NOPE + ROPE)
    narrow_count = lax.axis_size("narrow")
    narrow_place = lax.axis_index("narrow")
    q_cols = q_weight.shape[1]
    kva_cols = kva_weight.shape[1]
    kva_part = kva_cols // narrow_count
    kva_mine = lax.dynamic_slice_in_dim(kva_weight, narrow_place * kva_part, kva_part, 1)
    packed = jnp.concatenate([q_weight, kva_mine], axis=1)
    got_weights = gather_axis(packed, "wide")
    proj_full = got_weights.reshape(-1, q_cols + kva_part)
    kvb_full = gather_axis(kvb_weight, "wide").reshape(-1, kvb_weight.shape[1])
    o_got = lax.all_gather(o_weight, "wide", axis=0, tiled=False)

    normed = scaled_norm(hidden.astype(jnp.float32), attn_gain).astype(jnp.bfloat16)
    projected = jnp.dot(normed, proj_full, preferred_element_type=jnp.float32)
    query_rows = projected[:, :q_cols].astype(jnp.bfloat16)
    compressed_part = projected[:, q_cols:]
    first_token = wide_place * tok_rows
    token_ids = first_token + jnp.arange(tok_rows, dtype=jnp.int32)
    positions = lengths[token_ids // SPAN] + token_ids % SPAN

    query_heads = query_rows.reshape(tok_rows, heads_here, NOPE + ROPE)
    own_rope_q = rotate(query_heads[..., NOPE:].astype(jnp.float32), positions[:, None]).astype(
        jnp.bfloat16
    )
    outgoing = jnp.concatenate(
        [
            query_heads[..., :NOPE].reshape(tok_rows, heads_here * NOPE),
            own_rope_q.reshape(tok_rows, heads_here * ROPE),
        ],
        axis=1,
    )
    raw_all = gather_axis(outgoing, "wide")
    compressed_part, raw_all = lax.optimization_barrier((compressed_part, raw_all))
    compressed = jnp.transpose(gather_axis(compressed_part, "narrow"), (1, 0, 2)).reshape(
        tok_rows, kva_cols
    )
    own_keys = jnp.concatenate(
        [
            scaled_norm(compressed[:, :LAT], kv_gain).astype(jnp.bfloat16),
            rotate(compressed[:, LAT:], positions).astype(jnp.bfloat16),
        ],
        axis=1,
    )
    total_tokens = raw_all.shape[0] * tok_rows
    raw_all = raw_all.reshape(total_tokens, heads_here * (NOPE + ROPE))
    kvb_heads = kvb_full.reshape(LAT, heads_here, NOPE + VDIM)
    key_maps = kvb_heads[..., :NOPE]
    value_maps = kvb_heads[..., NOPE:]
    nope_all = raw_all[:, : heads_here * NOPE].reshape(total_tokens, heads_here, NOPE)
    rope_all = raw_all[:, heads_here * NOPE :].reshape(total_tokens, heads_here, ROPE)
    lat_hm = jnp.einsum(
        "thc,lhc->htl", nope_all, key_maps, preferred_element_type=jnp.float32
    ).astype(jnp.bfloat16)
    rope_hm = jnp.transpose(rope_all, (1, 0, 2))
    value_hm = jnp.transpose(value_maps, (1, 0, 2))

    base = (wide_place * cache_rows).reshape(1).astype(jnp.int32)
    stats_hm, value_out = cache_attention(lengths, base, lat_hm, rope_hm, cache, value_hm)
    peak_hm = stats_hm[:, :, 0].reshape(heads_here, total_tokens)
    total_hm = stats_hm[:, :, 1].reshape(heads_here, total_tokens)

    own_request = first_token // SPAN
    start_row = own_request * SPAN
    own_slots = first_token % SPAN + jnp.arange(tok_rows, dtype=jnp.int32)
    causal = own_slots[None, :] <= jnp.arange(SPAN, dtype=jnp.int32)[:, None]
    own_lat = lax.dynamic_slice_in_dim(lat_hm, start_row, SPAN, 1)
    own_rope = lax.dynamic_slice_in_dim(rope_hm, start_row, SPAN, 1)
    own_scores = (
        jnp.einsum("hqc,kc->hqk", own_lat, own_keys[:, :LAT], preferred_element_type=jnp.float32)
        + jnp.einsum("hqc,kc->hqk", own_rope, own_keys[:, LAT:], preferred_element_type=jnp.float32)
    ) * score_scale
    own_live = causal[None]
    own_peak = jnp.max(jnp.where(own_live, own_scores, -1e30), axis=-1)
    own_weights = jnp.where(own_live, jnp.exp(own_scores - own_peak[..., None]), 0.0)
    own_total = jnp.sum(own_weights, axis=-1)
    own_mixed = jnp.einsum(
        "hqk,kc->hqc", own_weights.astype(jnp.bfloat16), own_keys[:, :LAT],
        preferred_element_type=jnp.float32,
    )
    own_upper = own_mixed.astype(jnp.bfloat16)
    own_lower = (own_mixed - own_upper.astype(jnp.float32)).astype(jnp.bfloat16)
    own_value = jnp.einsum(
        "hqc,hcv->hqv", own_upper, value_hm, preferred_element_type=jnp.float32
    ) + jnp.einsum("hqc,hcv->hqv", own_lower, value_hm, preferred_element_type=jnp.float32)
    old_part = (
        lax.dynamic_slice_in_dim(peak_hm, start_row, SPAN, 1),
        lax.dynamic_slice_in_dim(total_hm, start_row, SPAN, 1),
        lax.dynamic_slice_in_dim(value_out, start_row, SPAN, 1),
    )
    joint = merge_parts(old_part, (own_peak, own_total, own_value))
    peak_hm = lax.dynamic_update_slice_in_dim(peak_hm, joint[0], start_row, 1)
    total_hm = lax.dynamic_update_slice_in_dim(total_hm, joint[1], start_row, 1)
    value_out = lax.dynamic_update_slice_in_dim(value_out, joint[2], start_row, 1)

    stats = jnp.stack([peak_hm, total_hm], axis=0).astype(jnp.bfloat16)
    got_stats = lax.all_to_all(
        stats.reshape(2, heads_here, wide_count, tok_rows), "wide", 2, 2, tiled=True
    ).astype(jnp.float32)
    got_value = lax.all_to_all(
        value_out.astype(jnp.bfloat16).reshape(heads_here, wide_count, tok_rows, VDIM),
        "wide",
        1,
        1,
        tiled=True,
    ).astype(jnp.float32)
    got_peak = got_stats[0]
    got_total = got_stats[1]
    peak_value = jnp.max(got_peak, axis=1)
    factor = jnp.exp(got_peak - peak_value[:, None])
    denominator = jnp.sum(factor * got_total, axis=1)
    numerator = jnp.sum(factor[..., None] * got_value, axis=1)
    context = jnp.transpose(
        (numerator / denominator[..., None]).astype(jnp.bfloat16), (1, 0, 2)
    ).reshape(tok_rows, heads_here * VDIM)
    partial_out = jnp.einsum(
        "tk,wkc->twc", context, o_got, preferred_element_type=jnp.float32
    ).reshape(tok_rows, -1)
    out_cols = partial_out.shape[1]
    pieces = jnp.transpose(
        partial_out.astype(jnp.bfloat16).reshape(tok_rows, narrow_count, out_cols // narrow_count),
        (1, 0, 2),
    )
    got_pieces = lax.all_to_all(pieces, "narrow", 0, 0, tiled=True)
    mine = jnp.sum(got_pieces.astype(jnp.float32), axis=0).astype(jnp.bfloat16)
    all_pieces = gather_axis(mine, "narrow")
    return jnp.transpose(all_pieces, (1, 0, 2)).reshape(tok_rows, out_cols)


def solution(mesh):
    in_specs = (
        P("wide", None),
        P(),
        P("wide", "narrow"),
        P("wide", None),
        P(),
        P("wide", "narrow"),
        P("narrow", "wide"),
        P(None, "wide", None),
        P(),
    )
    out_specs = P("wide", None)
    return jax.shard_map(
        per_device, mesh=mesh, in_specs=in_specs, out_specs=out_specs, check_vma=False
    )
```

```python
import jax
import jax.numpy as jnp
from jax import lax
from jax.sharding import PartitionSpec as P
from jax.experimental import pallas as pl
from jax.experimental.pallas import tpu as pltpu

NOPE = 128
ROPE = 64
VDIM = 128
LAT = 512
SPAN = 512
HEADS_PER_STEP = 4


eps = 1e-06
score_scale = 1.0 / 13.856406460551018


def rotate(values, positions):
    half_size = values.shape[-1] // 2
    frequency = 10000.0 ** (-jnp.arange(half_size, dtype=jnp.float32) / half_size)
    angles = positions.astype(jnp.float32)[..., None] * frequency
    lower_half = values[..., :half_size]
    upper_half = values[..., half_size:]
    cosine = jnp.cos(angles)
    sine_part = jnp.sin(angles)
    return jnp.concatenate(
        [
            lower_half * cosine - upper_half * sine_part,
            lower_half * sine_part + upper_half * cosine,
        ],
        axis=-1,
    )


def scaled_norm(values, gain):
    return (
        values
        * lax.rsqrt(jnp.mean(values * values, axis=-1, keepdims=True) + eps)
        * gain.astype(jnp.float32)
    )


def gather_axis(x, axis_name):
    count = lax.axis_size(axis_name)
    spread = jnp.broadcast_to(x[None], (count,) + x.shape)
    return lax.all_to_all(spread, axis_name, split_axis=0, concat_axis=0, tiled=True)


def absorb(nope_part, key_maps):
    return jnp.einsum(
        "thc,lhc->thl", nope_part, key_maps, preferred_element_type=jnp.float32
    ).astype(jnp.bfloat16)


def project_values(mixed, value_maps):
    upper_part = mixed.astype(jnp.bfloat16)
    lower_part = (mixed - upper_part.astype(jnp.float32)).astype(jnp.bfloat16)
    first_term = jnp.einsum(
        "qhc,chv->qhv", upper_part, value_maps, preferred_element_type=jnp.float32
    )
    second_term = jnp.einsum(
        "qhc,chv->qhv", lower_part, value_maps, preferred_element_type=jnp.float32
    )
    return first_term + second_term


def attend(block_queries, key_rows, live_mask, value_maps):
    scores = (
        jnp.einsum("qhc,kc->qhk", block_queries, key_rows, preferred_element_type=jnp.float32)
        * score_scale
    )
    live_rows = live_mask[:, None, :]
    row_peak = jnp.max(jnp.where(live_rows, scores, -1e30), axis=-1)
    weights = jnp.where(live_rows, jnp.exp(scores - row_peak[..., None]), 0.0)
    row_total = jnp.sum(weights, axis=-1)
    mixed = jnp.einsum(
        "qhk,kc->qhc",
        weights.astype(jnp.bfloat16),
        key_rows[:, :LAT],
        preferred_element_type=jnp.float32,
    )
    return (row_peak, row_total, project_values(mixed, value_maps))


def skipped(block_queries, key_rows, live_mask, value_maps):
    rows_here = block_queries.shape[0]
    heads_here = block_queries.shape[1]
    return (
        jnp.full((rows_here, heads_here), -1e30, jnp.float32),
        jnp.zeros((rows_here, heads_here), jnp.float32),
        jnp.zeros((rows_here, heads_here, value_maps.shape[2]), jnp.float32),
    )


def cache_kernel(lens_ref, base_ref, lat_ref, rope_ref, kv_ref, vm_ref, stats_ref, value_ref):
    length_now = lens_ref[pl.program_id(0)]
    base = base_ref[0]
    live_block = base < length_now

    def one_head(j):
        keys = kv_ref[0]
        key_lat = keys[:, :LAT]
        key_rope = keys[:, LAT:]
        nt = (((1,), (1,)), ((), ()))
        scores = (
            lax.dot_general(lat_ref[j], key_lat, nt, preferred_element_type=jnp.float32)
            + lax.dot_general(rope_ref[j], key_rope, nt, preferred_element_type=jnp.float32)
        ) * score_scale
        slots = base + lax.broadcasted_iota(jnp.int32, scores.shape, 1)
        live = slots < length_now
        peak = jnp.max(jnp.where(live, scores, -1e30), axis=-1, keepdims=True)
        weights = jnp.where(live, jnp.exp(scores - peak), 0.0)
        total = jnp.sum(weights, axis=-1, keepdims=True)
        lane = lax.broadcasted_iota(jnp.int32, (peak.shape[0], 128), 1)
        packed = jnp.where(lane == 0, peak, jnp.where(lane == 1, total, 0.0))
        stats_ref[j, 0] = jnp.transpose(packed)[: stats_ref.shape[2]]
        mixed = jnp.dot(weights.astype(jnp.bfloat16), key_lat, preferred_element_type=jnp.float32)
        value_map = vm_ref[j]
        upper_part = mixed.astype(jnp.bfloat16)
        lower_part = (mixed - upper_part.astype(jnp.float32)).astype(jnp.bfloat16)
        value_ref[j] = jnp.dot(upper_part, value_map, preferred_element_type=jnp.float32) + jnp.dot(
            lower_part, value_map, preferred_element_type=jnp.float32
        )

    @pl.when(live_block)
    def _():
        for j in range(lat_ref.shape[0]):
            one_head(j)

    @pl.when(jnp.logical_not(live_block))
    def _():
        row = lax.broadcasted_iota(jnp.int32, stats_ref.shape, 2)
        stats_ref[...] = jnp.where(row == 0, -1e30, 0.0).astype(jnp.float32)
        value_ref[...] = jnp.zeros(value_ref.shape, jnp.float32)


def cache_attention(lengths, base, lat_hm, rope_hm, cache, value_hm):
    heads_here, total_tokens, _ = lat_hm.shape
    requests, cache_rows, width = cache.shape
    span = total_tokens // requests
    vdim = value_hm.shape[2]
    grid_spec = pltpu.PrefetchScalarGridSpec(
        num_scalar_prefetch=2,
        grid=(requests, heads_here // HEADS_PER_STEP),
        in_specs=[
            pl.BlockSpec((HEADS_PER_STEP, span, LAT), lambda r, h, lens, b: (h, r, 0)),
            pl.BlockSpec((HEADS_PER_STEP, span, ROPE), lambda r, h, lens, b: (h, r, 0)),
            pl.BlockSpec((1, cache_rows, width), lambda r, h, lens, b: (r, 0, 0)),
            pl.BlockSpec((HEADS_PER_STEP, LAT, vdim), lambda r, h, lens, b: (h, 0, 0)),
        ],
        out_specs=[
            pl.BlockSpec((HEADS_PER_STEP, 1, 8, span), lambda r, h, lens, b: (h, r, 0, 0)),
            pl.BlockSpec((HEADS_PER_STEP, span, vdim), lambda r, h, lens, b: (h, r, 0)),
        ],
    )
    return pl.pallas_call(
        cache_kernel,
        grid_spec=grid_spec,
        out_shape=[
            jax.ShapeDtypeStruct((heads_here, requests, 8, span), jnp.float32),
            jax.ShapeDtypeStruct((heads_here, total_tokens, vdim), jnp.float32),
        ],
        compiler_params=pltpu.CompilerParams(dimension_semantics=("arbitrary", "arbitrary")),
    )(lengths, base, lat_hm, rope_hm, cache, value_hm)


def merge_parts(first, second):
    joint_peak = jnp.maximum(first[0], second[0])
    first_factor = jnp.exp(first[0] - joint_peak)
    second_factor = jnp.exp(second[0] - joint_peak)
    joint_total = first_factor * first[1] + second_factor * second[1]
    joint_value = first_factor[..., None] * first[2] + second_factor[..., None] * second[2]
    return (joint_peak, joint_total, joint_value)


def per_device(
    hidden, attn_gain, q_weight, kva_weight, kv_gain, kvb_weight, o_weight, cache, lengths
):
    wide_count = lax.axis_size("wide")
    wide_place = lax.axis_index("wide")
    tok_rows = hidden.shape[0]
    requests = lengths.shape[0]
    cache_rows = cache.shape[1]
    heads_here = q_weight.shape[1] // (NOPE + ROPE)
    narrow_count = lax.axis_size("narrow")
    narrow_place = lax.axis_index("narrow")
    q_cols = q_weight.shape[1]
    kva_cols = kva_weight.shape[1]
    kva_part = kva_cols // narrow_count
    kva_mine = lax.dynamic_slice_in_dim(kva_weight, narrow_place * kva_part, kva_part, 1)
    packed = jnp.concatenate([q_weight, kva_mine], axis=1)
    got_weights = gather_axis(packed, "wide")
    proj_full = got_weights.reshape(-1, q_cols + kva_part)
    kvb_full = gather_axis(kvb_weight, "wide").reshape(-1, kvb_weight.shape[1])
    o_got = lax.all_gather(o_weight, "wide", axis=0, tiled=False)

    normed = scaled_norm(hidden.astype(jnp.float32), attn_gain).astype(jnp.bfloat16)
    projected = jnp.dot(normed, proj_full, preferred_element_type=jnp.float32)
    query_rows = projected[:, :q_cols].astype(jnp.bfloat16)
    compressed_part = projected[:, q_cols:]
    first_token = wide_place * tok_rows
    token_ids = first_token + jnp.arange(tok_rows, dtype=jnp.int32)
    positions = lengths[token_ids // SPAN] + token_ids % SPAN

    query_heads = query_rows.reshape(tok_rows, heads_here, NOPE + ROPE)
    own_rope_q = rotate(query_heads[..., NOPE:].astype(jnp.float32), positions[:, None]).astype(
        jnp.bfloat16
    )
    outgoing = jnp.concatenate(
        [
            query_heads[..., :NOPE].reshape(tok_rows, heads_here * NOPE),
            own_rope_q.reshape(tok_rows, heads_here * ROPE),
        ],
        axis=1,
    )
    raw_all = gather_axis(outgoing, "wide")
    compressed_part, raw_all = lax.optimization_barrier((compressed_part, raw_all))
    compressed = jnp.transpose(gather_axis(compressed_part, "narrow"), (1, 0, 2)).reshape(
        tok_rows, kva_cols
    )
    own_keys = jnp.concatenate(
        [
            scaled_norm(compressed[:, :LAT], kv_gain).astype(jnp.bfloat16),
            rotate(compressed[:, LAT:], positions).astype(jnp.bfloat16),
        ],
        axis=1,
    )
    total_tokens = raw_all.shape[0] * tok_rows
    raw_all = raw_all.reshape(total_tokens, heads_here * (NOPE + ROPE))
    kvb_heads = kvb_full.reshape(LAT, heads_here, NOPE + VDIM)
    key_maps = kvb_heads[..., :NOPE]
    value_maps = kvb_heads[..., NOPE:]
    nope_all = raw_all[:, : heads_here * NOPE].reshape(total_tokens, heads_here, NOPE)
    rope_all = raw_all[:, heads_here * NOPE :].reshape(total_tokens, heads_here, ROPE)
    lat_hm = jnp.einsum(
        "thc,lhc->htl", nope_all, key_maps, preferred_element_type=jnp.float32
    ).astype(jnp.bfloat16)
    rope_hm = jnp.transpose(rope_all, (1, 0, 2))
    value_hm = jnp.transpose(value_maps, (1, 0, 2))

    base = (wide_place * cache_rows).reshape(1).astype(jnp.int32)
    stats_hm, value_out = cache_attention(lengths, base, lat_hm, rope_hm, cache, value_hm)
    peak_hm = stats_hm[:, :, 0].reshape(heads_here, total_tokens)
    total_hm = stats_hm[:, :, 1].reshape(heads_here, total_tokens)

    own_request = first_token // SPAN
    start_row = own_request * SPAN
    own_slots = first_token % SPAN + jnp.arange(tok_rows, dtype=jnp.int32)
    causal = own_slots[None, :] <= jnp.arange(SPAN, dtype=jnp.int32)[:, None]
    own_lat = lax.dynamic_slice_in_dim(lat_hm, start_row, SPAN, 1)
    own_rope = lax.dynamic_slice_in_dim(rope_hm, start_row, SPAN, 1)
    own_scores = (
        jnp.einsum("hqc,kc->hqk", own_lat, own_keys[:, :LAT], preferred_element_type=jnp.float32)
        + jnp.einsum("hqc,kc->hqk", own_rope, own_keys[:, LAT:], preferred_element_type=jnp.float32)
    ) * score_scale
    own_live = causal[None]
    own_peak = jnp.max(jnp.where(own_live, own_scores, -1e30), axis=-1)
    own_weights = jnp.where(own_live, jnp.exp(own_scores - own_peak[..., None]), 0.0)
    own_total = jnp.sum(own_weights, axis=-1)
    own_mixed = jnp.einsum(
        "hqk,kc->hqc", own_weights.astype(jnp.bfloat16), own_keys[:, :LAT],
        preferred_element_type=jnp.float32,
    )
    own_upper = own_mixed.astype(jnp.bfloat16)
    own_lower = (own_mixed - own_upper.astype(jnp.float32)).astype(jnp.bfloat16)
    own_value = jnp.einsum(
        "hqc,hcv->hqv", own_upper, value_hm, preferred_element_type=jnp.float32
    ) + jnp.einsum("hqc,hcv->hqv", own_lower, value_hm, preferred_element_type=jnp.float32)
    old_part = (
        lax.dynamic_slice_in_dim(peak_hm, start_row, SPAN, 1),
        lax.dynamic_slice_in_dim(total_hm, start_row, SPAN, 1),
        lax.dynamic_slice_in_dim(value_out, start_row, SPAN, 1),
    )
    joint = merge_parts(old_part, (own_peak, own_total, own_value))
    peak_hm = lax.dynamic_update_slice_in_dim(peak_hm, joint[0], start_row, 1)
    total_hm = lax.dynamic_update_slice_in_dim(total_hm, joint[1], start_row, 1)
    value_out = lax.dynamic_update_slice_in_dim(value_out, joint[2], start_row, 1)

    stats = jnp.stack([peak_hm, total_hm], axis=0).astype(jnp.bfloat16)
    got_stats = lax.all_to_all(
        stats.reshape(2, heads_here, wide_count, tok_rows), "wide", 2, 2, tiled=True
    ).astype(jnp.float32)
    got_value = lax.all_to_all(
        value_out.astype(jnp.bfloat16).reshape(heads_here, wide_count, tok_rows, VDIM),
        "wide",
        1,
        1,
        tiled=True,
    ).astype(jnp.float32)
    got_peak = got_stats[0]
    got_total = got_stats[1]
    peak_value = jnp.max(got_peak, axis=1)
    factor = jnp.exp(got_peak - peak_value[:, None])
    denominator = jnp.sum(factor * got_total, axis=1)
    numerator = jnp.sum(factor[..., None] * got_value, axis=1)
    context = jnp.transpose(
        (numerator / denominator[..., None]).astype(jnp.bfloat16), (1, 0, 2)
    ).reshape(tok_rows, heads_here * VDIM)
    partial_out = jnp.einsum(
        "tk,wkc->twc", context, o_got, preferred_element_type=jnp.float32
    ).reshape(tok_rows, -1)
    out_cols = partial_out.shape[1]
    pieces = jnp.transpose(
        partial_out.astype(jnp.bfloat16).reshape(tok_rows, narrow_count, out_cols // narrow_count),
        (1, 0, 2),
    )
    got_pieces = lax.all_to_all(pieces, "narrow", 0, 0, tiled=True)
    mine = jnp.sum(got_pieces.astype(jnp.float32), axis=0).astype(jnp.bfloat16)
    all_pieces = gather_axis(mine, "narrow")
    return jnp.transpose(all_pieces, (1, 0, 2)).reshape(tok_rows, out_cols)


def solution(mesh):
    in_specs = (
        P("wide", None),
        P(),
        P("wide", "narrow"),
        P("wide", None),
        P(),
        P("wide", "narrow"),
        P("narrow", "wide"),
        P(None, "wide", None),
        P(),
    )
    out_specs = P("wide", None)
    return jax.shard_map(
        per_device, mesh=mesh, in_specs=in_specs, out_specs=out_specs, check_vma=False
    )
```

```python
import jax
import jax.numpy as jnp
from jax import lax
from jax.sharding import PartitionSpec as P
from jax.experimental import pallas as pl
from jax.experimental.pallas import tpu as pltpu

NOPE = 128
ROPE = 64
VDIM = 128
LAT = 512
SPAN = 512
HEADS_PER_STEP = 4


eps = 1e-06
score_scale = 1.0 / 13.856406460551018


def rotate(values, positions):
    half_size = values.shape[-1] // 2
    frequency = 10000.0 ** (-jnp.arange(half_size, dtype=jnp.float32) / half_size)
    angles = positions.astype(jnp.float32)[..., None] * frequency
    lower_half = values[..., :half_size]
    upper_half = values[..., half_size:]
    cosine = jnp.cos(angles)
    sine_part = jnp.sin(angles)
    return jnp.concatenate(
        [
            lower_half * cosine - upper_half * sine_part,
            lower_half * sine_part + upper_half * cosine,
        ],
        axis=-1,
    )


def scaled_norm(values, gain):
    return (
        values
        * lax.rsqrt(jnp.mean(values * values, axis=-1, keepdims=True) + eps)
        * gain.astype(jnp.float32)
    )


def gather_axis(x, axis_name):
    count = lax.axis_size(axis_name)
    spread = jnp.broadcast_to(x[None], (count,) + x.shape)
    return lax.all_to_all(spread, axis_name, split_axis=0, concat_axis=0, tiled=True)


def absorb(nope_part, key_maps):
    return jnp.einsum(
        "thc,lhc->thl", nope_part, key_maps, preferred_element_type=jnp.float32
    ).astype(jnp.bfloat16)


def project_values(mixed, value_maps):
    upper_part = mixed.astype(jnp.bfloat16)
    lower_part = (mixed - upper_part.astype(jnp.float32)).astype(jnp.bfloat16)
    first_term = jnp.einsum(
        "qhc,chv->qhv", upper_part, value_maps, preferred_element_type=jnp.float32
    )
    second_term = jnp.einsum(
        "qhc,chv->qhv", lower_part, value_maps, preferred_element_type=jnp.float32
    )
    return first_term + second_term


def attend(block_queries, key_rows, live_mask, value_maps):
    scores = (
        jnp.einsum("qhc,kc->qhk", block_queries, key_rows, preferred_element_type=jnp.float32)
        * score_scale
    )
    live_rows = live_mask[:, None, :]
    row_peak = jnp.max(jnp.where(live_rows, scores, -1e30), axis=-1)
    weights = jnp.where(live_rows, jnp.exp(scores - row_peak[..., None]), 0.0)
    row_total = jnp.sum(weights, axis=-1)
    mixed = jnp.einsum(
        "qhk,kc->qhc",
        weights.astype(jnp.bfloat16),
        key_rows[:, :LAT],
        preferred_element_type=jnp.float32,
    )
    return (row_peak, row_total, project_values(mixed, value_maps))


def skipped(block_queries, key_rows, live_mask, value_maps):
    rows_here = block_queries.shape[0]
    heads_here = block_queries.shape[1]
    return (
        jnp.full((rows_here, heads_here), -1e30, jnp.float32),
        jnp.zeros((rows_here, heads_here), jnp.float32),
        jnp.zeros((rows_here, heads_here, value_maps.shape[2]), jnp.float32),
    )


def cache_kernel(lens_ref, base_ref, lat_ref, rope_ref, kv_ref, vm_ref, stats_ref, value_ref):
    length_now = lens_ref[pl.program_id(0)]
    base = base_ref[0]
    live_block = base < length_now

    def one_head(j, masked):
        keys = kv_ref[0]
        key_lat = keys[:, :LAT]
        key_rope = keys[:, LAT:]
        nt = (((1,), (1,)), ((), ()))
        scores = (
            lax.dot_general(lat_ref[j], key_lat, nt, preferred_element_type=jnp.float32)
            + lax.dot_general(rope_ref[j], key_rope, nt, preferred_element_type=jnp.float32)
        ) * score_scale
        if masked:
            slots = base + lax.broadcasted_iota(jnp.int32, scores.shape, 1)
            live = slots < length_now
            peak = jnp.max(jnp.where(live, scores, -1e30), axis=-1, keepdims=True)
            weights = jnp.where(live, jnp.exp(scores - peak), 0.0)
        else:
            peak = jnp.max(scores, axis=-1, keepdims=True)
            weights = jnp.exp(scores - peak)
        total = jnp.sum(weights, axis=-1, keepdims=True)
        lane = lax.broadcasted_iota(jnp.int32, (peak.shape[0], 128), 1)
        packed = jnp.where(lane == 0, peak, jnp.where(lane == 1, total, 0.0))
        stats_ref[j, 0] = jnp.transpose(packed)[: stats_ref.shape[2]]
        mixed = jnp.dot(weights.astype(jnp.bfloat16), key_lat, preferred_element_type=jnp.float32)
        value_map = vm_ref[j]
        upper_part = mixed.astype(jnp.bfloat16)
        lower_part = (mixed - upper_part.astype(jnp.float32)).astype(jnp.bfloat16)
        value_ref[j] = jnp.dot(upper_part, value_map, preferred_element_type=jnp.float32) + jnp.dot(
            lower_part, value_map, preferred_element_type=jnp.float32
        )

    whole_live = base + kv_ref.shape[1] <= length_now

    @pl.when(whole_live)
    def _():
        for j in range(lat_ref.shape[0]):
            one_head(j, False)

    @pl.when(jnp.logical_and(live_block, jnp.logical_not(whole_live)))
    def _():
        for j in range(lat_ref.shape[0]):
            one_head(j, True)

    @pl.when(jnp.logical_not(live_block))
    def _():
        row = lax.broadcasted_iota(jnp.int32, stats_ref.shape, 2)
        stats_ref[...] = jnp.where(row == 0, -1e30, 0.0).astype(jnp.float32)
        value_ref[...] = jnp.zeros(value_ref.shape, jnp.float32)


def cache_attention(lengths, base, lat_hm, rope_hm, cache, value_hm):
    heads_here, total_tokens, _ = lat_hm.shape
    requests, cache_rows, width = cache.shape
    span = total_tokens // requests
    vdim = value_hm.shape[2]
    grid_spec = pltpu.PrefetchScalarGridSpec(
        num_scalar_prefetch=2,
        grid=(requests, heads_here // HEADS_PER_STEP),
        in_specs=[
            pl.BlockSpec((HEADS_PER_STEP, span, LAT), lambda r, h, lens, b: (h, r, 0)),
            pl.BlockSpec((HEADS_PER_STEP, span, ROPE), lambda r, h, lens, b: (h, r, 0)),
            pl.BlockSpec((1, cache_rows, width), lambda r, h, lens, b: (r, 0, 0)),
            pl.BlockSpec((HEADS_PER_STEP, LAT, vdim), lambda r, h, lens, b: (h, 0, 0)),
        ],
        out_specs=[
            pl.BlockSpec((HEADS_PER_STEP, 1, 8, span), lambda r, h, lens, b: (h, r, 0, 0)),
            pl.BlockSpec((HEADS_PER_STEP, span, vdim), lambda r, h, lens, b: (h, r, 0)),
        ],
    )
    return pl.pallas_call(
        cache_kernel,
        grid_spec=grid_spec,
        out_shape=[
            jax.ShapeDtypeStruct((heads_here, requests, 8, span), jnp.float32),
            jax.ShapeDtypeStruct((heads_here, total_tokens, vdim), jnp.float32),
        ],
        compiler_params=pltpu.CompilerParams(dimension_semantics=("arbitrary", "arbitrary")),
    )(lengths, base, lat_hm, rope_hm, cache, value_hm)


def merge_parts(first, second):
    joint_peak = jnp.maximum(first[0], second[0])
    first_factor = jnp.exp(first[0] - joint_peak)
    second_factor = jnp.exp(second[0] - joint_peak)
    joint_total = first_factor * first[1] + second_factor * second[1]
    joint_value = first_factor[..., None] * first[2] + second_factor[..., None] * second[2]
    return (joint_peak, joint_total, joint_value)


def per_device(
    hidden, attn_gain, q_weight, kva_weight, kv_gain, kvb_weight, o_weight, cache, lengths
):
    wide_count = lax.axis_size("wide")
    wide_place = lax.axis_index("wide")
    tok_rows = hidden.shape[0]
    requests = lengths.shape[0]
    cache_rows = cache.shape[1]
    heads_here = q_weight.shape[1] // (NOPE + ROPE)
    narrow_count = lax.axis_size("narrow")
    narrow_place = lax.axis_index("narrow")
    q_cols = q_weight.shape[1]
    kva_cols = kva_weight.shape[1]
    kva_part = kva_cols // narrow_count
    kva_mine = lax.dynamic_slice_in_dim(kva_weight, narrow_place * kva_part, kva_part, 1)
    packed = jnp.concatenate([q_weight, kva_mine], axis=1)
    got_weights = gather_axis(packed, "wide")
    proj_full = got_weights.reshape(-1, q_cols + kva_part)
    kvb_full = gather_axis(kvb_weight, "wide").reshape(-1, kvb_weight.shape[1])
    o_got = lax.all_gather(o_weight, "wide", axis=0, tiled=False)

    normed = scaled_norm(hidden.astype(jnp.float32), attn_gain).astype(jnp.bfloat16)
    projected = jnp.dot(normed, proj_full, preferred_element_type=jnp.float32)
    query_rows = projected[:, :q_cols].astype(jnp.bfloat16)
    compressed_part = projected[:, q_cols:]
    first_token = wide_place * tok_rows
    token_ids = first_token + jnp.arange(tok_rows, dtype=jnp.int32)
    positions = lengths[token_ids // SPAN] + token_ids % SPAN

    query_heads = query_rows.reshape(tok_rows, heads_here, NOPE + ROPE)
    own_rope_q = rotate(query_heads[..., NOPE:].astype(jnp.float32), positions[:, None]).astype(
        jnp.bfloat16
    )
    outgoing = jnp.concatenate(
        [
            query_heads[..., :NOPE].reshape(tok_rows, heads_here * NOPE),
            own_rope_q.reshape(tok_rows, heads_here * ROPE),
        ],
        axis=1,
    )
    raw_all = gather_axis(outgoing, "wide")
    compressed_part, raw_all = lax.optimization_barrier((compressed_part, raw_all))
    compressed = jnp.transpose(gather_axis(compressed_part, "narrow"), (1, 0, 2)).reshape(
        tok_rows, kva_cols
    )
    own_keys = jnp.concatenate(
        [
            scaled_norm(compressed[:, :LAT], kv_gain).astype(jnp.bfloat16),
            rotate(compressed[:, LAT:], positions).astype(jnp.bfloat16),
        ],
        axis=1,
    )
    total_tokens = raw_all.shape[0] * tok_rows
    raw_all = raw_all.reshape(total_tokens, heads_here * (NOPE + ROPE))
    kvb_heads = kvb_full.reshape(LAT, heads_here, NOPE + VDIM)
    key_maps = kvb_heads[..., :NOPE]
    value_maps = kvb_heads[..., NOPE:]
    nope_all = raw_all[:, : heads_here * NOPE].reshape(total_tokens, heads_here, NOPE)
    rope_all = raw_all[:, heads_here * NOPE :].reshape(total_tokens, heads_here, ROPE)
    lat_hm = jnp.einsum(
        "thc,lhc->htl", nope_all, key_maps, preferred_element_type=jnp.float32
    ).astype(jnp.bfloat16)
    rope_hm = jnp.transpose(rope_all, (1, 0, 2))
    value_hm = jnp.transpose(value_maps, (1, 0, 2))

    base = (wide_place * cache_rows).reshape(1).astype(jnp.int32)
    stats_hm, value_out = cache_attention(lengths, base, lat_hm, rope_hm, cache, value_hm)
    peak_hm = stats_hm[:, :, 0].reshape(heads_here, total_tokens)
    total_hm = stats_hm[:, :, 1].reshape(heads_here, total_tokens)

    own_request = first_token // SPAN
    start_row = own_request * SPAN
    own_slots = first_token % SPAN + jnp.arange(tok_rows, dtype=jnp.int32)
    causal = own_slots[None, :] <= jnp.arange(SPAN, dtype=jnp.int32)[:, None]
    own_lat = lax.dynamic_slice_in_dim(lat_hm, start_row, SPAN, 1)
    own_rope = lax.dynamic_slice_in_dim(rope_hm, start_row, SPAN, 1)
    own_scores = (
        jnp.einsum("hqc,kc->hqk", own_lat, own_keys[:, :LAT], preferred_element_type=jnp.float32)
        + jnp.einsum("hqc,kc->hqk", own_rope, own_keys[:, LAT:], preferred_element_type=jnp.float32)
    ) * score_scale
    own_live = causal[None]
    own_peak = jnp.max(jnp.where(own_live, own_scores, -1e30), axis=-1)
    own_weights = jnp.where(own_live, jnp.exp(own_scores - own_peak[..., None]), 0.0)
    own_total = jnp.sum(own_weights, axis=-1)
    own_mixed = jnp.einsum(
        "hqk,kc->hqc", own_weights.astype(jnp.bfloat16), own_keys[:, :LAT],
        preferred_element_type=jnp.float32,
    )
    own_upper = own_mixed.astype(jnp.bfloat16)
    own_lower = (own_mixed - own_upper.astype(jnp.float32)).astype(jnp.bfloat16)
    own_value = jnp.einsum(
        "hqc,hcv->hqv", own_upper, value_hm, preferred_element_type=jnp.float32
    ) + jnp.einsum("hqc,hcv->hqv", own_lower, value_hm, preferred_element_type=jnp.float32)
    old_part = (
        lax.dynamic_slice_in_dim(peak_hm, start_row, SPAN, 1),
        lax.dynamic_slice_in_dim(total_hm, start_row, SPAN, 1),
        lax.dynamic_slice_in_dim(value_out, start_row, SPAN, 1),
    )
    joint = merge_parts(old_part, (own_peak, own_total, own_value))
    peak_hm = lax.dynamic_update_slice_in_dim(peak_hm, joint[0], start_row, 1)
    total_hm = lax.dynamic_update_slice_in_dim(total_hm, joint[1], start_row, 1)
    value_out = lax.dynamic_update_slice_in_dim(value_out, joint[2], start_row, 1)

    stats = jnp.stack([peak_hm, total_hm], axis=0).astype(jnp.bfloat16)
    got_stats = lax.all_to_all(
        stats.reshape(2, heads_here, wide_count, tok_rows), "wide", 2, 2, tiled=True
    ).astype(jnp.float32)
    got_value = lax.all_to_all(
        value_out.astype(jnp.bfloat16).reshape(heads_here, wide_count, tok_rows, VDIM),
        "wide",
        1,
        1,
        tiled=True,
    ).astype(jnp.float32)
    got_peak = got_stats[0]
    got_total = got_stats[1]
    peak_value = jnp.max(got_peak, axis=1)
    factor = jnp.exp(got_peak - peak_value[:, None])
    denominator = jnp.sum(factor * got_total, axis=1)
    numerator = jnp.sum(factor[..., None] * got_value, axis=1)
    context = jnp.transpose(
        (numerator / denominator[..., None]).astype(jnp.bfloat16), (1, 0, 2)
    ).reshape(tok_rows, heads_here * VDIM)
    partial_out = jnp.einsum(
        "tk,wkc->twc", context, o_got, preferred_element_type=jnp.float32
    ).reshape(tok_rows, -1)
    out_cols = partial_out.shape[1]
    pieces = jnp.transpose(
        partial_out.astype(jnp.bfloat16).reshape(tok_rows, narrow_count, out_cols // narrow_count),
        (1, 0, 2),
    )
    got_pieces = lax.all_to_all(pieces, "narrow", 0, 0, tiled=True)
    mine = jnp.sum(got_pieces.astype(jnp.float32), axis=0).astype(jnp.bfloat16)
    all_pieces = gather_axis(mine, "narrow")
    return jnp.transpose(all_pieces, (1, 0, 2)).reshape(tok_rows, out_cols)


def solution(mesh):
    in_specs = (
        P("wide", None),
        P(),
        P("wide", "narrow"),
        P("wide", None),
        P(),
        P("wide", "narrow"),
        P("narrow", "wide"),
        P(None, "wide", None),
        P(),
    )
    out_specs = P("wide", None)
    return jax.shard_map(
        per_device, mesh=mesh, in_specs=in_specs, out_specs=out_specs, check_vma=False
    )
```

```python
import jax
import jax.numpy as jnp
from jax import lax
from jax.sharding import PartitionSpec as P
from jax.experimental import pallas as pl
from jax.experimental.pallas import tpu as pltpu

NOPE = 128
ROPE = 64
VDIM = 128
LAT = 512
SPAN = 512
HEADS_PER_STEP = 4


eps = 1e-06
score_scale = 1.0 / 13.856406460551018


def rotate(values, positions):
    half_size = values.shape[-1] // 2
    frequency = 10000.0 ** (-jnp.arange(half_size, dtype=jnp.float32) / half_size)
    angles = positions.astype(jnp.float32)[..., None] * frequency
    lower_half = values[..., :half_size]
    upper_half = values[..., half_size:]
    cosine = jnp.cos(angles)
    sine_part = jnp.sin(angles)
    return jnp.concatenate(
        [
            lower_half * cosine - upper_half * sine_part,
            lower_half * sine_part + upper_half * cosine,
        ],
        axis=-1,
    )


def scaled_norm(values, gain):
    return (
        values
        * lax.rsqrt(jnp.mean(values * values, axis=-1, keepdims=True) + eps)
        * gain.astype(jnp.float32)
    )


def gather_axis(x, axis_name):
    count = lax.axis_size(axis_name)
    spread = jnp.broadcast_to(x[None], (count,) + x.shape)
    return lax.all_to_all(spread, axis_name, split_axis=0, concat_axis=0, tiled=True)


def absorb(nope_part, key_maps):
    return jnp.einsum(
        "thc,lhc->thl", nope_part, key_maps, preferred_element_type=jnp.float32
    ).astype(jnp.bfloat16)


def project_values(mixed, value_maps):
    upper_part = mixed.astype(jnp.bfloat16)
    lower_part = (mixed - upper_part.astype(jnp.float32)).astype(jnp.bfloat16)
    first_term = jnp.einsum(
        "qhc,chv->qhv", upper_part, value_maps, preferred_element_type=jnp.float32
    )
    second_term = jnp.einsum(
        "qhc,chv->qhv", lower_part, value_maps, preferred_element_type=jnp.float32
    )
    return first_term + second_term


def attend(block_queries, key_rows, live_mask, value_maps):
    scores = (
        jnp.einsum("qhc,kc->qhk", block_queries, key_rows, preferred_element_type=jnp.float32)
        * score_scale
    )
    live_rows = live_mask[:, None, :]
    row_peak = jnp.max(jnp.where(live_rows, scores, -1e30), axis=-1)
    weights = jnp.where(live_rows, jnp.exp(scores - row_peak[..., None]), 0.0)
    row_total = jnp.sum(weights, axis=-1)
    mixed = jnp.einsum(
        "qhk,kc->qhc",
        weights.astype(jnp.bfloat16),
        key_rows[:, :LAT],
        preferred_element_type=jnp.float32,
    )
    return (row_peak, row_total, project_values(mixed, value_maps))


def skipped(block_queries, key_rows, live_mask, value_maps):
    rows_here = block_queries.shape[0]
    heads_here = block_queries.shape[1]
    return (
        jnp.full((rows_here, heads_here), -1e30, jnp.float32),
        jnp.zeros((rows_here, heads_here), jnp.float32),
        jnp.zeros((rows_here, heads_here, value_maps.shape[2]), jnp.float32),
    )


def cache_kernel(lens_ref, base_ref, lat_ref, rope_ref, kv_ref, vm_ref, stats_ref, value_ref):
    length_now = lens_ref[pl.program_id(0)]
    base = base_ref[0]
    live_block = base < length_now

    def all_heads():
        keys = kv_ref[0]
        key_lat = keys[:, :LAT]
        key_rope = keys[:, LAT:]
        nt = (((1,), (1,)), ((), ()))
        heads_step, span = lat_ref.shape[0], lat_ref.shape[1]
        q_lat = lat_ref[...].reshape(heads_step * span, LAT)
        q_rope = rope_ref[...].reshape(heads_step * span, ROPE)
        scores = (
            lax.dot_general(q_lat, key_lat, nt, preferred_element_type=jnp.float32)
            + lax.dot_general(q_rope, key_rope, nt, preferred_element_type=jnp.float32)
        ) * score_scale
        slots = base + lax.broadcasted_iota(jnp.int32, scores.shape, 1)
        live = slots < length_now
        peak = jnp.max(jnp.where(live, scores, -1e30), axis=-1, keepdims=True)
        weights = jnp.where(live, jnp.exp(scores - peak), 0.0)
        total = jnp.sum(weights, axis=-1, keepdims=True)
        mixed = jnp.dot(weights.astype(jnp.bfloat16), key_lat, preferred_element_type=jnp.float32)
        for j in range(heads_step):
            rows = slice(j * span, (j + 1) * span)
            lane = lax.broadcasted_iota(jnp.int32, (span, 128), 1)
            packed = jnp.where(lane == 0, peak[rows], jnp.where(lane == 1, total[rows], 0.0))
            stats_ref[j, 0] = jnp.transpose(packed)[: stats_ref.shape[2]]
            value_map = vm_ref[j]
            head_mixed = mixed[rows]
            upper_part = head_mixed.astype(jnp.bfloat16)
            lower_part = (head_mixed - upper_part.astype(jnp.float32)).astype(jnp.bfloat16)
            value_ref[j] = jnp.dot(
                upper_part, value_map, preferred_element_type=jnp.float32
            ) + jnp.dot(lower_part, value_map, preferred_element_type=jnp.float32)

    @pl.when(live_block)
    def _():
        all_heads()

    @pl.when(jnp.logical_not(live_block))
    def _():
        row = lax.broadcasted_iota(jnp.int32, stats_ref.shape, 2)
        stats_ref[...] = jnp.where(row == 0, -1e30, 0.0).astype(jnp.float32)
        value_ref[...] = jnp.zeros(value_ref.shape, jnp.float32)


def cache_attention(lengths, base, lat_hm, rope_hm, cache, value_hm):
    heads_here, total_tokens, _ = lat_hm.shape
    requests, cache_rows, width = cache.shape
    span = total_tokens // requests
    vdim = value_hm.shape[2]
    grid_spec = pltpu.PrefetchScalarGridSpec(
        num_scalar_prefetch=2,
        grid=(requests, heads_here // HEADS_PER_STEP),
        in_specs=[
            pl.BlockSpec((HEADS_PER_STEP, span, LAT), lambda r, h, lens, b: (h, r, 0)),
            pl.BlockSpec((HEADS_PER_STEP, span, ROPE), lambda r, h, lens, b: (h, r, 0)),
            pl.BlockSpec((1, cache_rows, width), lambda r, h, lens, b: (r, 0, 0)),
            pl.BlockSpec((HEADS_PER_STEP, LAT, vdim), lambda r, h, lens, b: (h, 0, 0)),
        ],
        out_specs=[
            pl.BlockSpec((HEADS_PER_STEP, 1, 8, span), lambda r, h, lens, b: (h, r, 0, 0)),
            pl.BlockSpec((HEADS_PER_STEP, span, vdim), lambda r, h, lens, b: (h, r, 0)),
        ],
    )
    return pl.pallas_call(
        cache_kernel,
        grid_spec=grid_spec,
        out_shape=[
            jax.ShapeDtypeStruct((heads_here, requests, 8, span), jnp.float32),
            jax.ShapeDtypeStruct((heads_here, total_tokens, vdim), jnp.float32),
        ],
        compiler_params=pltpu.CompilerParams(dimension_semantics=("arbitrary", "arbitrary")),
    )(lengths, base, lat_hm, rope_hm, cache, value_hm)


def merge_parts(first, second):
    joint_peak = jnp.maximum(first[0], second[0])
    first_factor = jnp.exp(first[0] - joint_peak)
    second_factor = jnp.exp(second[0] - joint_peak)
    joint_total = first_factor * first[1] + second_factor * second[1]
    joint_value = first_factor[..., None] * first[2] + second_factor[..., None] * second[2]
    return (joint_peak, joint_total, joint_value)


def per_device(
    hidden, attn_gain, q_weight, kva_weight, kv_gain, kvb_weight, o_weight, cache, lengths
):
    wide_count = lax.axis_size("wide")
    wide_place = lax.axis_index("wide")
    tok_rows = hidden.shape[0]
    requests = lengths.shape[0]
    cache_rows = cache.shape[1]
    heads_here = q_weight.shape[1] // (NOPE + ROPE)
    narrow_count = lax.axis_size("narrow")
    narrow_place = lax.axis_index("narrow")
    q_cols = q_weight.shape[1]
    kva_cols = kva_weight.shape[1]
    kva_part = kva_cols // narrow_count
    kva_mine = lax.dynamic_slice_in_dim(kva_weight, narrow_place * kva_part, kva_part, 1)
    packed = jnp.concatenate([q_weight, kva_mine], axis=1)
    got_weights = gather_axis(packed, "wide")
    proj_full = got_weights.reshape(-1, q_cols + kva_part)
    kvb_full = gather_axis(kvb_weight, "wide").reshape(-1, kvb_weight.shape[1])
    o_got = lax.all_gather(o_weight, "wide", axis=0, tiled=False)

    normed = scaled_norm(hidden.astype(jnp.float32), attn_gain).astype(jnp.bfloat16)
    projected = jnp.dot(normed, proj_full, preferred_element_type=jnp.float32)
    query_rows = projected[:, :q_cols].astype(jnp.bfloat16)
    compressed_part = projected[:, q_cols:]
    first_token = wide_place * tok_rows
    token_ids = first_token + jnp.arange(tok_rows, dtype=jnp.int32)
    positions = lengths[token_ids // SPAN] + token_ids % SPAN

    query_heads = query_rows.reshape(tok_rows, heads_here, NOPE + ROPE)
    own_rope_q = rotate(query_heads[..., NOPE:].astype(jnp.float32), positions[:, None]).astype(
        jnp.bfloat16
    )
    outgoing = jnp.concatenate(
        [
            query_heads[..., :NOPE].reshape(tok_rows, heads_here * NOPE),
            own_rope_q.reshape(tok_rows, heads_here * ROPE),
        ],
        axis=1,
    )
    raw_all = gather_axis(outgoing, "wide")
    compressed_part, raw_all = lax.optimization_barrier((compressed_part, raw_all))
    compressed = jnp.transpose(gather_axis(compressed_part, "narrow"), (1, 0, 2)).reshape(
        tok_rows, kva_cols
    )
    own_keys = jnp.concatenate(
        [
            scaled_norm(compressed[:, :LAT], kv_gain).astype(jnp.bfloat16),
            rotate(compressed[:, LAT:], positions).astype(jnp.bfloat16),
        ],
        axis=1,
    )
    total_tokens = raw_all.shape[0] * tok_rows
    raw_all = raw_all.reshape(total_tokens, heads_here * (NOPE + ROPE))
    kvb_heads = kvb_full.reshape(LAT, heads_here, NOPE + VDIM)
    key_maps = kvb_heads[..., :NOPE]
    value_maps = kvb_heads[..., NOPE:]
    nope_all = raw_all[:, : heads_here * NOPE].reshape(total_tokens, heads_here, NOPE)
    rope_all = raw_all[:, heads_here * NOPE :].reshape(total_tokens, heads_here, ROPE)
    lat_hm = jnp.einsum(
        "thc,lhc->htl", nope_all, key_maps, preferred_element_type=jnp.float32
    ).astype(jnp.bfloat16)
    rope_hm = jnp.transpose(rope_all, (1, 0, 2))
    value_hm = jnp.transpose(value_maps, (1, 0, 2))

    base = (wide_place * cache_rows).reshape(1).astype(jnp.int32)
    stats_hm, value_out = cache_attention(lengths, base, lat_hm, rope_hm, cache, value_hm)
    peak_hm = stats_hm[:, :, 0].reshape(heads_here, total_tokens)
    total_hm = stats_hm[:, :, 1].reshape(heads_here, total_tokens)

    own_request = first_token // SPAN
    start_row = own_request * SPAN
    own_slots = first_token % SPAN + jnp.arange(tok_rows, dtype=jnp.int32)
    causal = own_slots[None, :] <= jnp.arange(SPAN, dtype=jnp.int32)[:, None]
    own_lat = lax.dynamic_slice_in_dim(lat_hm, start_row, SPAN, 1)
    own_rope = lax.dynamic_slice_in_dim(rope_hm, start_row, SPAN, 1)
    own_scores = (
        jnp.einsum("hqc,kc->hqk", own_lat, own_keys[:, :LAT], preferred_element_type=jnp.float32)
        + jnp.einsum("hqc,kc->hqk", own_rope, own_keys[:, LAT:], preferred_element_type=jnp.float32)
    ) * score_scale
    own_live = causal[None]
    own_peak = jnp.max(jnp.where(own_live, own_scores, -1e30), axis=-1)
    own_weights = jnp.where(own_live, jnp.exp(own_scores - own_peak[..., None]), 0.0)
    own_total = jnp.sum(own_weights, axis=-1)
    own_mixed = jnp.einsum(
        "hqk,kc->hqc", own_weights.astype(jnp.bfloat16), own_keys[:, :LAT],
        preferred_element_type=jnp.float32,
    )
    own_upper = own_mixed.astype(jnp.bfloat16)
    own_lower = (own_mixed - own_upper.astype(jnp.float32)).astype(jnp.bfloat16)
    own_value = jnp.einsum(
        "hqc,hcv->hqv", own_upper, value_hm, preferred_element_type=jnp.float32
    ) + jnp.einsum("hqc,hcv->hqv", own_lower, value_hm, preferred_element_type=jnp.float32)
    old_part = (
        lax.dynamic_slice_in_dim(peak_hm, start_row, SPAN, 1),
        lax.dynamic_slice_in_dim(total_hm, start_row, SPAN, 1),
        lax.dynamic_slice_in_dim(value_out, start_row, SPAN, 1),
    )
    joint = merge_parts(old_part, (own_peak, own_total, own_value))
    peak_hm = lax.dynamic_update_slice_in_dim(peak_hm, joint[0], start_row, 1)
    total_hm = lax.dynamic_update_slice_in_dim(total_hm, joint[1], start_row, 1)
    value_out = lax.dynamic_update_slice_in_dim(value_out, joint[2], start_row, 1)

    stats = jnp.stack([peak_hm, total_hm], axis=0).astype(jnp.bfloat16)
    got_stats = lax.all_to_all(
        stats.reshape(2, heads_here, wide_count, tok_rows), "wide", 2, 2, tiled=True
    ).astype(jnp.float32)
    got_value = lax.all_to_all(
        value_out.astype(jnp.bfloat16).reshape(heads_here, wide_count, tok_rows, VDIM),
        "wide",
        1,
        1,
        tiled=True,
    ).astype(jnp.float32)
    got_peak = got_stats[0]
    got_total = got_stats[1]
    peak_value = jnp.max(got_peak, axis=1)
    factor = jnp.exp(got_peak - peak_value[:, None])
    denominator = jnp.sum(factor * got_total, axis=1)
    numerator = jnp.sum(factor[..., None] * got_value, axis=1)
    context = jnp.transpose(
        (numerator / denominator[..., None]).astype(jnp.bfloat16), (1, 0, 2)
    ).reshape(tok_rows, heads_here * VDIM)
    partial_out = jnp.einsum(
        "tk,wkc->twc", context, o_got, preferred_element_type=jnp.float32
    ).reshape(tok_rows, -1)
    out_cols = partial_out.shape[1]
    pieces = jnp.transpose(
        partial_out.astype(jnp.bfloat16).reshape(tok_rows, narrow_count, out_cols // narrow_count),
        (1, 0, 2),
    )
    got_pieces = lax.all_to_all(pieces, "narrow", 0, 0, tiled=True)
    mine = jnp.sum(got_pieces.astype(jnp.float32), axis=0).astype(jnp.bfloat16)
    all_pieces = gather_axis(mine, "narrow")
    return jnp.transpose(all_pieces, (1, 0, 2)).reshape(tok_rows, out_cols)


def solution(mesh):
    in_specs = (
        P("wide", None),
        P(),
        P("wide", "narrow"),
        P("wide", None),
        P(),
        P("wide", "narrow"),
        P("narrow", "wide"),
        P(None, "wide", None),
        P(),
    )
    out_specs = P("wide", None)
    return jax.shard_map(
        per_device, mesh=mesh, in_specs=in_specs, out_specs=out_specs, check_vma=False
    )
```
